32 devices in a mesh: groups: 2 (over y), blk: 4 (over z), cls: 4 (over x, core).
Axes of the slice: x: 2, y: 2, z: 4, core: 2. Of those that a mesh axis runs over, the one named last changes fastest.
Arguments:
- particles: bfloat16 [64, 4096], P(('groups', 'blk')), parts along dimension 0
- references: bfloat16 [4, 400, 4096], P('blk', ('groups', 'cls')), parts along dimension 1
- ctf_table: float32 [32, 2048], P('groups'), parts along dimension 0, may hold values from 0.05 to 1
- spectral_reg: float32 [4096], P('groups'), parts along dimension 0, may hold values from 0.002 to 0.02
- defocus_bin: int32 [64], P(('groups', 'blk')), parts along dimension 0, may hold values from 0 to 15
- group_counts: int32 [32], P(('groups', 'blk')), parts along dimension 0, may hold values from 0 to 8, as said below
- group_scale: float32 [32], P(('groups', 'blk')), parts along dimension 0, may hold values from 0.5 to 2
Outputs:
- class_average: float32 [4, 400, 4096], P('blk', ('groups', 'cls')), parts along dimension 1
- log_evidence: float32 [64], P(('groups', 'blk')), parts along dimension 0
The draws below stay inside these ranges and needn't reach their ends.
There are 2 independent parts, one for each index of `groups`. The reference program is written for one: setup_inputs(seed, part) draws one part's arguments, and reference() takes and returns one part's arrays. A program takes and returns all parts, laid end to end along the dimension named above; each array names one. Nothing has to cross between parts.
Inputs may be any that keep to these rules, and one draw needn't show every extreme that they name: `group_counts`: the 4 groups of one block of 8 slots hold at most 8 particles together, filling the block's first slots; in every draw some single group holds exactly 8.
All inputs are finite; a program needn't handle non-finite values.
Results may differ from the reference program's by a relative error of at most 0.013.
Values may be sent and summed in bfloat16 or wider, within the bound.
No kernel may reach another device: no remote copies, remote signals or barrier semaphores. Data moves between devices by JAX's collectives and lax.ppermute only.
A program may use at most 64 MiB of HBM per device.

```python
import math
import jax
import jax.numpy as jnp
from jax import lax

KX = 32
KY = 64
FREQ = 2048
IMG = 128
CLASSES = 200
ROT = 4
SIDE = 4
BINS = 16
P_DEV = 8
PARTICLES = 32
MIC_DEV = 4
MICS = 16
N_BLK = 4


def reference_values(key):
    width = 2 * KX * KY
    base = jax.random.normal(jax.random.fold_in(key, 101), (ROT, CLASSES, width), jnp.float32)
    return base * (4.0 / math.sqrt(width))


def draw_references(key, part):
    return reference_values(key).astype(jnp.bfloat16)


def draw_particles(key, part):
    width = 2 * KX * KY
    noise_part = jax.random.normal(jax.random.fold_in(key, 206), (PARTICLES, width), jnp.float32)
    ref_rows = reference_values(key).reshape(ROT * CLASSES, width)
    picked = jax.random.randint(jax.random.fold_in(key, 203), (PARTICLES,), 0, ROT * CLASSES)
    chosen = jnp.take(ref_rows, picked, axis=0)
    strength = jax.random.uniform(jax.random.fold_in(key, 204), (PARTICLES, 1), jnp.float32, 20.0, 60.0)
    aligned = (jax.random.randint(jax.random.fold_in(key, 205), (PARTICLES, 1), 0, 4) == 0).astype(jnp.float32)
    values = noise_part + aligned * strength * chosen
    return values.astype(jnp.bfloat16)


def draw_group_counts(key, part):
    loads = jax.random.randint(jax.random.fold_in(key, 301), (N_BLK,), P_DEV // 4, P_DEV + 1)
    fullest = jax.random.randint(jax.random.fold_in(key, 302), (), 0, N_BLK)
    is_fullest = jnp.arange(N_BLK) == fullest
    loads = jnp.where(is_fullest, P_DEV, loads)
    cut_points = jnp.sort(jax.random.randint(jax.random.fold_in(key, 303), (N_BLK, MIC_DEV - 1), 0, P_DEV + 1), axis=1)
    cut_points = jnp.minimum(cut_points, loads[:, None])
    cut_points = jnp.where(is_fullest[:, None], 0, cut_points)
    edges = jnp.concatenate([jnp.zeros((N_BLK, 1), jnp.int32), cut_points, loads[:, None]], axis=1)
    return (edges[:, 1:] - edges[:, :-1]).reshape(MICS).astype(jnp.int32)


def with_ends(array, own_key, smallest, largest):
    longest = array.shape.index(max(array.shape))
    spots = []
    for shift in (0, 1):
        where = [jax.random.randint(jax.random.fold_in(own_key, axis), (), 0, length) for axis, length in enumerate(array.shape)]
        where[longest] = (where[longest] + shift) % array.shape[longest]
        spots.append(tuple(where))
    return array.at[spots[0]].set(smallest).at[spots[1]].set(largest)


def level_of(rng, dims, shards, smallest, largest):
    def one(position, parts):
        draws = jax.random.uniform(jax.random.fold_in(jax.random.fold_in(rng, 6), position), (parts,), jnp.float32, smallest / len(shards), largest / len(shards))
        return jnp.repeat(jnp.exp(draws), dims[position] // parts).reshape((-1,) + (1,) * (len(dims) - position - 1))

    factor_of = one(*shards[0])
    for cut in shards[1:]:
        factor_of = factor_of * one(*cut)
    return factor_of


def setup_inputs(seed: int = 0, part: int = 0) -> dict:
    streams_of = jax.random.split(jax.random.key(seed), 8)
    part_keys = jax.random.split(jax.random.fold_in(streams_of[7], part), 8)
    return {
        "particles": draw_particles(jax.random.fold_in(jax.random.fold_in(streams_of[7], part), 71), part),
        "references": draw_references(jax.random.fold_in(jax.random.fold_in(streams_of[7], part), 71), part),
        "ctf_table": jnp.clip(jax.random.uniform(part_keys[2], (BINS, FREQ), jnp.float32, 0.05, 1.0), 0.05, 1.0),
        "spectral_reg": jnp.clip(jnp.exp(jax.random.uniform(part_keys[3], (FREQ,), jnp.float32, math.log(0.002), math.log(0.02))), 0.002, 0.02),
        "defocus_bin": with_ends(jax.random.randint(part_keys[4], (PARTICLES,), 0, BINS), jax.random.fold_in(part_keys[4], 1), 0, BINS - 1).astype(jnp.int32),
        "group_counts": draw_group_counts(jax.random.fold_in(jax.random.fold_in(streams_of[7], part), 71), part),
        "group_scale": jnp.clip(jnp.exp(math.log(2.0) - 1.3862944 * jax.random.uniform(part_keys[6], (MICS,), jnp.float32) ** level_of(part_keys[6], (MICS,), ((0, 4),), -0.2, 0.2)), 0.5, 2.0),
    }


HIGHEST = lax.Precision.HIGHEST


def phase_tables():
    column = jnp.arange(KX * KY, dtype=jnp.int32)
    freq_x = (column % KX).astype(jnp.float32)
    freq_y = (column // KX - KY // 2).astype(jnp.float32)
    offsets = jnp.arange(SIDE, dtype=jnp.float32) - (SIDE - 1) / 2.0
    shift_x = jnp.tile(offsets, SIDE)
    shift_y = jnp.repeat(offsets, SIDE)
    phases = (2.0 * math.pi / IMG) * (shift_x[:, None] * freq_x[None, :] + shift_y[:, None] * freq_y[None, :])
    return jnp.cos(phases), jnp.sin(phases)


def bin_matrix(bin_values):
    return (bin_values[:, None] == jnp.arange(BINS, dtype=jnp.float32)[None, :]).astype(jnp.float32)


def slot_weights(group_sizes, scale_rows, slots):
    group_ends = jnp.cumsum(group_sizes, axis=1).astype(jnp.int32)
    group_starts = (group_ends - group_sizes).astype(jnp.int32)
    slot_index = jnp.arange(slots, dtype=jnp.int32)
    membership = ((slot_index[None, :, None] >= group_starts[:, None, :]) & (slot_index[None, :, None] < group_ends[:, None, :])).astype(jnp.float32)
    gain_rows = jnp.sum(membership * scale_rows[:, None, :], axis=2)
    live_mask = jnp.sum(membership, axis=2)
    return gain_rows.reshape(-1), live_mask.reshape(-1)


def shifted_rows(images, ctf_rows, cosine_table, sine_table):
    half_width = ctf_rows.shape[1]
    real_part = images[:, :half_width].astype(jnp.float32)[:, None, :]
    imag_part = images[:, half_width:].astype(jnp.float32)[:, None, :]
    ctf_wide = ctf_rows[:, None, :]
    new_real = (real_part * cosine_table + imag_part * sine_table) * ctf_wide
    new_imag = (imag_part * cosine_table - real_part * sine_table) * ctf_wide
    joined = jnp.concatenate([new_real, new_imag], axis=2).astype(jnp.bfloat16)
    return joined.reshape(images.shape[0] * cosine_table.shape[0], 2 * half_width)


def tile_norms(ref_rows, ctf_square):
    half_width = ctf_square.shape[1]
    values = ref_rows.astype(jnp.float32)
    power_sum = values[:, :half_width] * values[:, :half_width] + values[:, half_width:] * values[:, half_width:]
    return lax.dot_general(ctf_square, power_sum, (((1,), (1,)), ((), ())), precision=HIGHEST)


def tile_scores(shifted, ref_rows, norms, gain_rows, bin_rows):
    count_here = gain_rows.shape[0]
    products = lax.dot_general(shifted, ref_rows, (((1,), (1,)), ((), ())), preferred_element_type=jnp.float32)
    products = products.reshape(count_here, shifted.shape[0] // count_here, ref_rows.shape[0])
    norm_term = jnp.dot(bin_rows, norms, precision=HIGHEST)
    return gain_rows[:, None, None] * products - 0.5 * (gain_rows * gain_rows)[:, None, None] * norm_term[:, None, :]


def reference(particles, references, ctf_table, spectral_reg, defocus_bin, group_counts, group_scale):
    cosine_table, sine_table = phase_tables()
    ctf_square = ctf_table * ctf_table
    gain_rows, live_mask = slot_weights(group_counts.reshape(N_BLK, MIC_DEV), group_scale.reshape(N_BLK, MIC_DEV), P_DEV)
    bin_rows = bin_matrix(defocus_bin.astype(jnp.float32))
    ctf_rows = jnp.dot(bin_rows, ctf_table, precision=HIGHEST)
    shifted = shifted_rows(particles, ctf_rows, cosine_table, sine_table)
    all_refs = references.reshape(ROT * CLASSES, 2 * KX * KY)
    norms = tile_norms(all_refs, ctf_square)
    scores = tile_scores(shifted, all_refs, norms, gain_rows, bin_rows)
    peak_score = jnp.max(scores, axis=(1, 2))
    totals = jnp.sum(jnp.exp(scores - peak_score[:, None, None]), axis=(1, 2))
    log_evidence = jnp.where(live_mask > 0.5, peak_score + jnp.log(totals), 0.0)
    weights = jnp.exp(scores - peak_score[:, None, None]) / totals[:, None, None] * live_mask[:, None, None]
    scaled = (weights * gain_rows[:, None, None]).astype(jnp.bfloat16).reshape(shifted.shape[0], -1)
    numerator = lax.dot_general(scaled, shifted, (((0,), (0,)), ((), ())), preferred_element_type=jnp.float32)
    summed = jnp.sum(weights, axis=1) * (gain_rows * gain_rows)[:, None]
    bin_weight = lax.dot_general(summed, bin_rows, (((0,), (0,)), ((), ())), precision=HIGHEST)
    denominator = jnp.dot(bin_weight, ctf_square, precision=HIGHEST)
    denominator = jnp.concatenate([denominator, denominator], axis=1) + jnp.concatenate([spectral_reg, spectral_reg])[None, :]
    class_average = (numerator / denominator).reshape(ROT, CLASSES, 2 * KX * KY)
    return class_average, log_evidence
```

```python
import math

import jax
import jax.numpy as jnp
from jax import lax
from jax.sharding import PartitionSpec as P

KX = 32
KY = 64
IMG = 128
SIDE = 4
BINS = 16
META = 128


HIGHEST = lax.Precision.HIGHEST


def phase_tables():
    column = jnp.arange(KX * KY, dtype=jnp.int32)
    freq_x = (column % KX).astype(jnp.float32)
    freq_y = (column // KX - KY // 2).astype(jnp.float32)
    offsets = jnp.arange(SIDE, dtype=jnp.float32) - (SIDE - 1) / 2.0
    shift_x = jnp.tile(offsets, SIDE)
    shift_y = jnp.repeat(offsets, SIDE)
    phases = (
        2.0
        * math.pi
        / IMG
        * (shift_x[:, None] * freq_x[None, :] + shift_y[:, None] * freq_y[None, :])
    )
    return (jnp.cos(phases), jnp.sin(phases))


def bin_matrix(bin_values):
    return (bin_values[:, None] == jnp.arange(BINS, dtype=jnp.float32)[None, :]).astype(jnp.float32)


def slot_weights(group_sizes, scale_rows, slots):
    group_ends = jnp.cumsum(group_sizes, axis=1)
    group_starts = group_ends - group_sizes
    slot_index = jnp.arange(slots, dtype=jnp.int32)
    membership = (
        (slot_index[None, :, None] >= group_starts[:, None, :])
        & (slot_index[None, :, None] < group_ends[:, None, :])
    ).astype(jnp.float32)
    gain_rows = jnp.sum(membership * scale_rows[:, None, :], axis=2)
    live_mask = jnp.sum(membership, axis=2)
    return (gain_rows.reshape(-1), live_mask.reshape(-1))


def shifted_rows(images, ctf_rows, cosine_table, sine_table):
    half_width = ctf_rows.shape[1]
    real_part = images[:, :half_width].astype(jnp.float32)[:, None, :]
    imag_part = images[:, half_width:].astype(jnp.float32)[:, None, :]
    ctf_wide = ctf_rows[:, None, :]
    new_real = (real_part * cosine_table + imag_part * sine_table) * ctf_wide
    new_imag = (imag_part * cosine_table - real_part * sine_table) * ctf_wide
    joined = jnp.concatenate([new_real, new_imag], axis=2).astype(jnp.bfloat16)
    return joined.reshape(images.shape[0] * cosine_table.shape[0], 2 * half_width)


def tile_norms(ref_rows, ctf_square):
    half_width = ctf_square.shape[1]
    values = ref_rows.astype(jnp.float32)
    power_sum = (
        values[:, :half_width] * values[:, :half_width]
        + values[:, half_width:] * values[:, half_width:]
    )
    return lax.dot_general(ctf_square, power_sum, (((1,), (1,)), ((), ())), precision=HIGHEST)


def tile_scores(shifted, ref_rows, norms, gain_rows, bin_rows):
    count_here = gain_rows.shape[0]
    products = lax.dot_general(
        shifted, ref_rows, (((1,), (1,)), ((), ())), preferred_element_type=jnp.float32
    )
    products = products.reshape(count_here, shifted.shape[0] // count_here, ref_rows.shape[0])
    norm_term = jnp.dot(bin_rows, norms, precision=HIGHEST)
    return (
        gain_rows[:, None, None] * products
        - 0.5 * (gain_rows * gain_rows)[:, None, None] * norm_term[:, None, :]
    )


def combine_stats(former, latter):
    new_peak = jnp.maximum(former[0], latter[0])
    return (
        new_peak,
        former[1] * jnp.exp(former[0] - new_peak) + latter[1] * jnp.exp(latter[0] - new_peak),
    )


def combine_many(peaks, totals):
    new_peak = jnp.max(peaks, axis=0)
    return (new_peak, jnp.sum(totals * jnp.exp(peaks - new_peak[None]), axis=0))


def split_exact(value):
    high = lax.reduce_precision(value, exponent_bits=8, mantissa_bits=7)
    rest = value - high
    middle = lax.reduce_precision(rest, exponent_bits=8, mantissa_bits=7)
    return (high, middle, rest - middle)


def shift_gather(value, axis, size):
    pieces = [value] + [
        lax.ppermute(value, axis, [(i, (i + k) % size) for i in range(size)])
        for k in range(1, size)
    ]
    return jnp.concatenate(pieces, axis=0)


def xor_butterfly(stats, axis, size):
    step = 1
    while step < size:
        other = jax.tree.map(
            lambda part: lax.ppermute(part, axis, [(i, i ^ step) for i in range(size)]), stats
        )
        stats = combine_stats(stats, other)
        step *= 2
    return stats


def accumulate(shifted, scores, gain_rows, bin_rows, live_mask, peak_score, totals):
    weights = (
        jnp.exp(scores - peak_score[:, None, None])
        / totals[:, None, None]
        * live_mask[:, None, None]
    )
    scaled = (weights * gain_rows[:, None, None]).astype(jnp.bfloat16).reshape(shifted.shape[0], -1)
    numerator = lax.dot_general(
        scaled, shifted, (((0,), (0,)), ((), ())), preferred_element_type=jnp.float32
    )
    summed = jnp.sum(weights, axis=1) * (gain_rows * gain_rows)[:, None]
    bin_weight = lax.dot_general(summed, bin_rows, (((0,), (0,)), ((), ())), precision=HIGHEST)
    return (numerator, bin_weight)


def per_device(
    particles, references, ctf_table, spectral_reg, defocus_bin, group_counts, group_scale,
    *, n_blk, n_cls,
):
    cosine_table, sine_table = phase_tables()
    ctf_square = ctf_table * ctf_table
    batch_size, width = particles.shape
    gain_rows, live_mask = slot_weights(
        group_counts.reshape(1, -1), group_scale.reshape(1, -1), batch_size
    )
    ref_tile = references[0]
    own_norms = tile_norms(ref_tile, ctf_square)
    classes_here = ref_tile.shape[0]
    shifts_count = cosine_table.shape[0]

    small = n_blk <= 4
    if small:
        meta = jnp.stack(
            [*split_exact(gain_rows), live_mask, defocus_bin.astype(jnp.float32)], axis=1
        )
        meta = jnp.pad(meta, ((0, 0), (0, META - meta.shape[1]))).astype(jnp.bfloat16)
        packed = jnp.concatenate([particles, meta], axis=1)
        everyone = shift_gather(packed, "blk", n_blk)
        images = everyone[:, :width]
        meta_all = everyone[:, width : width + 5].astype(jnp.float32)
        gain_all = (meta_all[:, 0] + meta_all[:, 1]) + meta_all[:, 2]
        live_all = meta_all[:, 3]
        bins_all = meta_all[:, 4]
    else:
        images = lax.all_gather(particles, "blk", axis=0, tiled=True)
        gain_all, bins_all, live_all = (
            lax.all_gather(gain_rows, "blk", axis=0, tiled=True),
            lax.all_gather(defocus_bin.astype(jnp.float32), "blk", axis=0, tiled=True),
            lax.all_gather(live_mask, "blk", axis=0, tiled=True),
        )
    whole_count = images.shape[0]

    bin_rows = bin_matrix(bins_all)
    ctf_rows = jnp.dot(bin_rows, ctf_table, precision=HIGHEST)
    shifted = shifted_rows(images, ctf_rows, cosine_table, sine_table)
    all_scores = tile_scores(shifted, ref_tile, own_norms, gain_all, bin_rows)
    flattened = all_scores.reshape(whole_count, -1)
    peak_all = jnp.max(flattened, axis=1)
    totals_all = jnp.sum(jnp.exp(flattened - peak_all[:, None]), axis=1)

    if small and n_cls & (n_cls - 1) == 0:
        peak_all, totals_all = xor_butterfly((peak_all, totals_all), "cls", n_cls)
        stats = jnp.stack([peak_all, totals_all]).reshape(2, n_blk, batch_size)
        parts = [stats] + [
            jnp.roll(lax.ppermute(stats, "blk", [(i, (i + k) % n_blk) for i in range(n_blk)]), k, axis=1)
            for k in range(1, n_blk)
        ]
        parts = jnp.stack(parts)
        peak_all, totals_all = combine_many(parts[:, 0], parts[:, 1])
        peak_all = peak_all.reshape(-1)
        totals_all = totals_all.reshape(-1)
        peak_score = peak_all[:batch_size]
        totals = totals_all[:batch_size]
    else:
        gathered = lax.all_gather(jnp.stack([peak_all, totals_all]), ("blk", "cls"))
        peak_all, totals_all = combine_many(gathered[:, 0], gathered[:, 1])
        if small:
            own_offset = 0
        else:
            own_offset = lax.axis_index("blk") * batch_size
        peak_score = lax.dynamic_slice_in_dim(peak_all, own_offset, batch_size)
        totals = lax.dynamic_slice_in_dim(totals_all, own_offset, batch_size)

    numerator, bin_weight = accumulate(
        shifted, all_scores, gain_all, bin_rows, live_all, peak_all, totals_all
    )
    log_evidence = jnp.where(live_mask > 0.5, peak_score + jnp.log(totals), 0.0)
    denominator = jnp.dot(bin_weight, ctf_square, precision=HIGHEST)
    denominator = (
        jnp.concatenate([denominator, denominator], axis=1)
        + jnp.concatenate([spectral_reg, spectral_reg])[None, :]
    )
    class_average = (numerator / denominator)[None]
    return (class_average, log_evidence)


def solution(mesh):
    placed = (
        P(("groups", "blk"), None),
        P("blk", ("groups", "cls"), None),
        P("groups", None),
        P("groups"),
        P(("groups", "blk")),
        P(("groups", "blk")),
        P(("groups", "blk")),
    )
    body = lambda *args: per_device(*args, n_blk=mesh.shape["blk"], n_cls=mesh.shape["cls"])
    return jax.shard_map(
        body,
        mesh=mesh,
        in_specs=placed,
        out_specs=(P("blk", ("groups", "cls"), None), P(("groups", "blk"))),
        check_vma=False,
    )
```

```python
import math

import jax
import jax.numpy as jnp
from jax import lax
from jax.sharding import PartitionSpec as P

KX = 32
KY = 64
IMG = 128
SIDE = 4
BINS = 16
META = 128


HIGHEST = lax.Precision.HIGHEST


def phase_tables():
    column = jnp.arange(KX * KY, dtype=jnp.int32)
    freq_x = (column % KX).astype(jnp.float32)
    freq_y = (column // KX - KY // 2).astype(jnp.float32)
    offsets = jnp.arange(SIDE, dtype=jnp.float32) - (SIDE - 1) / 2.0
    shift_x = jnp.tile(offsets, SIDE)
    shift_y = jnp.repeat(offsets, SIDE)
    phases = (
        2.0
        * math.pi
        / IMG
        * (shift_x[:, None] * freq_x[None, :] + shift_y[:, None] * freq_y[None, :])
    )
    return (jnp.cos(phases), jnp.sin(phases))


def bin_matrix(bin_values):
    return (bin_values[:, None] == jnp.arange(BINS, dtype=jnp.float32)[None, :]).astype(jnp.float32)


def slot_weights(group_sizes, scale_rows, slots):
    groups = group_sizes.shape[1]
    before = jnp.arange(groups)[:, None] < jnp.arange(groups)[None, :]
    group_starts = jnp.sum(jnp.where(before[None], group_sizes[:, :, None], 0), axis=1)
    group_ends = group_starts + group_sizes
    slot_index = jnp.arange(slots, dtype=jnp.int32)
    membership = (slot_index[None, :, None] >= group_starts[:, None, :]) & (
        slot_index[None, :, None] < group_ends[:, None, :]
    )
    gain_rows = jnp.sum(jnp.where(membership, scale_rows[:, None, :], 0.0), axis=2)
    live_mask = jnp.sum(membership.astype(jnp.float32), axis=2)
    return (gain_rows.reshape(-1), live_mask.reshape(-1))


def shifted_rows(images, ctf_rows, cosine_table, sine_table):
    half_width = ctf_rows.shape[1]
    real_part = images[:, :half_width].astype(jnp.float32)[:, None, :]
    imag_part = images[:, half_width:].astype(jnp.float32)[:, None, :]
    ctf_wide = ctf_rows[:, None, :]
    new_real = (real_part * cosine_table + imag_part * sine_table) * ctf_wide
    new_imag = (imag_part * cosine_table - real_part * sine_table) * ctf_wide
    joined = jnp.concatenate([new_real, new_imag], axis=2).astype(jnp.bfloat16)
    return joined.reshape(images.shape[0] * cosine_table.shape[0], 2 * half_width)


def tile_norms(ref_rows, ctf_square):
    half_width = ctf_square.shape[1]
    values = ref_rows.astype(jnp.float32)
    power_sum = (
        values[:, :half_width] * values[:, :half_width]
        + values[:, half_width:] * values[:, half_width:]
    )
    return lax.dot_general(ctf_square, power_sum, (((1,), (1,)), ((), ())), precision=HIGHEST)


def tile_scores(shifted, ref_rows, norms, gain_rows, bin_rows):
    count_here = gain_rows.shape[0]
    products = lax.dot_general(
        shifted, ref_rows, (((1,), (1,)), ((), ())), preferred_element_type=jnp.float32
    )
    products = products.reshape(count_here, shifted.shape[0] // count_here, ref_rows.shape[0])
    norm_term = jnp.dot(bin_rows, norms, precision=HIGHEST)
    return (
        gain_rows[:, None, None] * products
        - 0.5 * (gain_rows * gain_rows)[:, None, None] * norm_term[:, None, :]
    )


def combine_stats(former, latter):
    new_peak = jnp.maximum(former[0], latter[0])
    return (
        new_peak,
        former[1] * jnp.exp(former[0] - new_peak) + latter[1] * jnp.exp(latter[0] - new_peak),
    )


def combine_many(peaks, totals):
    new_peak = jnp.max(peaks, axis=0)
    return (new_peak, jnp.sum(totals * jnp.exp(peaks - new_peak[None]), axis=0))


def split_exact(value):
    high = lax.reduce_precision(value, exponent_bits=8, mantissa_bits=7)
    rest = value - high
    middle = lax.reduce_precision(rest, exponent_bits=8, mantissa_bits=7)
    return (high, middle, rest - middle)


def pack_rows(particles, group_counts, group_scale, defocus_bin):
    slots = particles.shape[0]
    slot_index = jnp.arange(slots, dtype=jnp.int32)
    start = jnp.int32(0)
    gain = jnp.zeros((slots,), jnp.float32)
    live = jnp.zeros((slots,), jnp.float32)
    for group in range(group_counts.shape[0]):
        size = group_counts[group]
        inside = (slot_index >= start) & (slot_index < start + size)
        gain = jnp.where(inside, group_scale[group], gain)
        live = jnp.where(inside, 1.0, live)
        start = start + size
    fields = (*split_exact(gain), live, defocus_bin.astype(jnp.float32))
    column = jnp.arange(META, dtype=jnp.int32)[None, :]
    meta = jnp.zeros((slots, META), jnp.float32)
    for index, field in enumerate(fields):
        meta = jnp.where(column == index, field[:, None], meta)
    return jnp.concatenate([particles, meta.astype(jnp.bfloat16)], axis=1)


def shift_gather(value, axis, size):
    pieces = [value] + [
        lax.ppermute(value, axis, [(i, (i + k) % size) for i in range(size)])
        for k in range(1, size)
    ]
    return jnp.concatenate(pieces, axis=0)


def xor_butterfly(stats, axis, size):
    step = 1
    while step < size:
        other = jax.tree.map(
            lambda part: lax.ppermute(part, axis, [(i, i ^ step) for i in range(size)]), stats
        )
        stats = combine_stats(stats, other)
        step *= 2
    return stats


def accumulate(shifted, scores, gain_rows, bin_rows, live_mask, peak_score, totals):
    weights = (
        jnp.exp(scores - peak_score[:, None, None])
        / totals[:, None, None]
        * live_mask[:, None, None]
    )
    scaled = (weights * gain_rows[:, None, None]).astype(jnp.bfloat16).reshape(shifted.shape[0], -1)
    numerator = lax.dot_general(
        scaled, shifted, (((0,), (0,)), ((), ())), preferred_element_type=jnp.float32
    )
    summed = jnp.sum(weights, axis=1) * (gain_rows * gain_rows)[:, None]
    bin_weight = lax.dot_general(summed, bin_rows, (((0,), (0,)), ((), ())), precision=HIGHEST)
    return (numerator, bin_weight)


def per_device(
    particles, references, ctf_table, spectral_reg, defocus_bin, group_counts, group_scale,
    *, n_blk, n_cls,
):
    cosine_table, sine_table = phase_tables()
    ctf_square = ctf_table * ctf_table
    batch_size, width = particles.shape
    gain_rows, live_mask = slot_weights(
        group_counts.reshape(1, -1), group_scale.reshape(1, -1), batch_size
    )
    ref_tile = references[0]
    own_norms = tile_norms(ref_tile, ctf_square)
    classes_here = ref_tile.shape[0]
    shifts_count = cosine_table.shape[0]

    small = n_blk <= 4
    if small:
        packed = pack_rows(particles, group_counts, group_scale, defocus_bin)
        everyone = shift_gather(packed, "blk", n_blk)
        images = everyone[:, :width]
        meta_all = everyone[:, width : width + 5].astype(jnp.float32)
        gain_all = (meta_all[:, 0] + meta_all[:, 1]) + meta_all[:, 2]
        live_all = meta_all[:, 3]
        bins_all = meta_all[:, 4]
    else:
        images = lax.all_gather(particles, "blk", axis=0, tiled=True)
        gain_all, bins_all, live_all = (
            lax.all_gather(gain_rows, "blk", axis=0, tiled=True),
            lax.all_gather(defocus_bin.astype(jnp.float32), "blk", axis=0, tiled=True),
            lax.all_gather(live_mask, "blk", axis=0, tiled=True),
        )
    whole_count = images.shape[0]

    bin_rows = bin_matrix(bins_all)
    ctf_rows = jnp.dot(bin_rows, ctf_table, precision=HIGHEST)
    shifted = shifted_rows(images, ctf_rows, cosine_table, sine_table)
    all_scores = tile_scores(shifted, ref_tile, own_norms, gain_all, bin_rows)
    flattened = all_scores.reshape(whole_count, -1)
    peak_all = jnp.max(flattened, axis=1)
    totals_all = jnp.sum(jnp.exp(flattened - peak_all[:, None]), axis=1)

    if small and n_cls & (n_cls - 1) == 0:
        peak_all, totals_all = xor_butterfly((peak_all, totals_all), "cls", n_cls)
        stats = jnp.stack([peak_all, totals_all]).reshape(2, n_blk, batch_size)
        parts = [stats] + [
            jnp.roll(lax.ppermute(stats, "blk", [(i, (i + k) % n_blk) for i in range(n_blk)]), k, axis=1)
            for k in range(1, n_blk)
        ]
        parts = jnp.stack(parts)
        peak_all, totals_all = combine_many(parts[:, 0], parts[:, 1])
        peak_all = peak_all.reshape(-1)
        totals_all = totals_all.reshape(-1)
        peak_score = peak_all[:batch_size]
        totals = totals_all[:batch_size]
    else:
        gathered = lax.all_gather(jnp.stack([peak_all, totals_all]), ("blk", "cls"))
        peak_all, totals_all = combine_many(gathered[:, 0], gathered[:, 1])
        if small:
            own_offset = 0
        else:
            own_offset = lax.axis_index("blk") * batch_size
        peak_score = lax.dynamic_slice_in_dim(peak_all, own_offset, batch_size)
        totals = lax.dynamic_slice_in_dim(totals_all, own_offset, batch_size)

    numerator, bin_weight = accumulate(
        shifted, all_scores, gain_all, bin_rows, live_all, peak_all, totals_all
    )
    log_evidence = jnp.where(live_mask > 0.5, peak_score + jnp.log(totals), 0.0)
    denominator = jnp.dot(bin_weight, ctf_square, precision=HIGHEST)
    denominator = (
        jnp.concatenate([denominator, denominator], axis=1)
        + jnp.concatenate([spectral_reg, spectral_reg])[None, :]
    )
    class_average = (numerator / denominator)[None]
    return (class_average, log_evidence)


def solution(mesh):
    placed = (
        P(("groups", "blk"), None),
        P("blk", ("groups", "cls"), None),
        P("groups", None),
        P("groups"),
        P(("groups", "blk")),
        P(("groups", "blk")),
        P(("groups", "blk")),
    )
    body = lambda *args: per_device(*args, n_blk=mesh.shape["blk"], n_cls=mesh.shape["cls"])
    return jax.shard_map(
        body,
        mesh=mesh,
        in_specs=placed,
        out_specs=(P("blk", ("groups", "cls"), None), P(("groups", "blk"))),
        check_vma=False,
    )
```

```python
import math

import jax
import jax.numpy as jnp
from jax import lax
from jax.experimental import pallas as pl
from jax.experimental.pallas import tpu as pltpu
from jax.sharding import PartitionSpec as P

KX = 32
KY = 64
IMG = 128
SIDE = 4
BINS = 16
META = 128


HIGHEST = lax.Precision.HIGHEST


def phase_tables():
    column = jnp.arange(KX * KY, dtype=jnp.int32)
    freq_x = (column % KX).astype(jnp.float32)
    freq_y = (column // KX - KY // 2).astype(jnp.float32)
    offsets = jnp.arange(SIDE, dtype=jnp.float32) - (SIDE - 1) / 2.0
    shift_x = jnp.tile(offsets, SIDE)
    shift_y = jnp.repeat(offsets, SIDE)
    phases = (
        2.0
        * math.pi
        / IMG
        * (shift_x[:, None] * freq_x[None, :] + shift_y[:, None] * freq_y[None, :])
    )
    return (jnp.cos(phases), jnp.sin(phases))


def bin_matrix(bin_values):
    return (bin_values[:, None] == jnp.arange(BINS, dtype=jnp.float32)[None, :]).astype(jnp.float32)


def slot_weights(group_sizes, scale_rows, slots):
    group_ends = jnp.cumsum(group_sizes, axis=1)
    group_starts = group_ends - group_sizes
    slot_index = jnp.arange(slots, dtype=jnp.int32)
    membership = (
        (slot_index[None, :, None] >= group_starts[:, None, :])
        & (slot_index[None, :, None] < group_ends[:, None, :])
    ).astype(jnp.float32)
    gain_rows = jnp.sum(membership * scale_rows[:, None, :], axis=2)
    live_mask = jnp.sum(membership, axis=2)
    return (gain_rows.reshape(-1), live_mask.reshape(-1))


def shifted_rows(images, ctf_rows, cosine_table, sine_table):
    half_width = ctf_rows.shape[1]
    real_part = images[:, :half_width].astype(jnp.float32)[:, None, :]
    imag_part = images[:, half_width:].astype(jnp.float32)[:, None, :]
    ctf_wide = ctf_rows[:, None, :]
    new_real = (real_part * cosine_table + imag_part * sine_table) * ctf_wide
    new_imag = (imag_part * cosine_table - real_part * sine_table) * ctf_wide
    joined = jnp.concatenate([new_real, new_imag], axis=2).astype(jnp.bfloat16)
    return joined.reshape(images.shape[0] * cosine_table.shape[0], 2 * half_width)


def tile_norms(ref_rows, ctf_square):
    half_width = ctf_square.shape[1]
    values = ref_rows.astype(jnp.float32)
    power_sum = (
        values[:, :half_width] * values[:, :half_width]
        + values[:, half_width:] * values[:, half_width:]
    )
    return lax.dot_general(ctf_square, power_sum, (((1,), (1,)), ((), ())), precision=HIGHEST)


def tile_scores(shifted, ref_rows, norms, gain_rows, bin_rows):
    count_here = gain_rows.shape[0]
    products = lax.dot_general(
        shifted, ref_rows, (((1,), (1,)), ((), ())), preferred_element_type=jnp.float32
    )
    products = products.reshape(count_here, shifted.shape[0] // count_here, ref_rows.shape[0])
    norm_term = jnp.dot(bin_rows, norms, precision=HIGHEST)
    return (
        gain_rows[:, None, None] * products
        - 0.5 * (gain_rows * gain_rows)[:, None, None] * norm_term[:, None, :]
    )


def combine_stats(former, latter):
    new_peak = jnp.maximum(former[0], latter[0])
    return (
        new_peak,
        former[1] * jnp.exp(former[0] - new_peak) + latter[1] * jnp.exp(latter[0] - new_peak),
    )


def combine_many(peaks, totals):
    new_peak = jnp.max(peaks, axis=0)
    return (new_peak, jnp.sum(totals * jnp.exp(peaks - new_peak[None]), axis=0))


def split_exact(value):
    high = lax.reduce_precision(value, exponent_bits=8, mantissa_bits=7)
    rest = value - high
    middle = lax.reduce_precision(rest, exponent_bits=8, mantissa_bits=7)
    return (high, middle, rest - middle)


def pack_kernel(sizes_ref, scales_ref, bins_ref, images_ref, out_ref):
    slots, width = images_ref.shape
    row = lax.broadcasted_iota(jnp.int32, (slots, META), 0)
    column = lax.broadcasted_iota(jnp.int32, (slots, META), 1)
    start = jnp.int32(0)
    gain = jnp.zeros((slots, META), jnp.float32)
    live = jnp.zeros((slots, META), jnp.float32)
    for group in range(sizes_ref.shape[0]):
        size = sizes_ref[group]
        inside = (row >= start) & (row < start + size)
        gain = jnp.where(inside, scales_ref[group], gain)
        live = jnp.where(inside, 1.0, live)
        start = start + size
    bins = jnp.zeros((slots, META), jnp.float32)
    for slot in range(slots):
        bins = jnp.where(row == slot, bins_ref[slot].astype(jnp.float32), bins)
    high = gain.astype(jnp.bfloat16).astype(jnp.float32)
    rest = gain - high
    middle = rest.astype(jnp.bfloat16).astype(jnp.float32)
    fields = (high, middle, rest - middle, live, bins)
    meta = jnp.zeros((slots, META), jnp.float32)
    for index, field in enumerate(fields):
        meta = jnp.where(column == index, field, meta)
    out_ref[:, :width] = images_ref[...]
    out_ref[:, width:] = meta.astype(out_ref.dtype)


def pack_rows(particles, group_counts, group_scale, defocus_bin):
    slots, width = particles.shape
    scalar = pl.BlockSpec(memory_space=pltpu.SMEM)
    whole = pl.BlockSpec(memory_space=pltpu.VMEM)
    return pl.pallas_call(
        pack_kernel,
        out_shape=jax.ShapeDtypeStruct((slots, width + META), particles.dtype),
        in_specs=[scalar, scalar, scalar, whole],
        out_specs=whole,
    )(group_counts, group_scale, defocus_bin, particles)


def shift_gather(value, axis, size):
    pieces = [value] + [
        lax.ppermute(value, axis, [(i, (i + k) % size) for i in range(size)])
        for k in range(1, size)
    ]
    return jnp.concatenate(pieces, axis=0)


def xor_butterfly(stats, axis, size):
    step = 1
    while step < size:
        other = jax.tree.map(
            lambda part: lax.ppermute(part, axis, [(i, i ^ step) for i in range(size)]), stats
        )
        stats = combine_stats(stats, other)
        step *= 2
    return stats


def accumulate(shifted, scores, gain_rows, bin_rows, live_mask, peak_score, totals):
    weights = (
        jnp.exp(scores - peak_score[:, None, None])
        / totals[:, None, None]
        * live_mask[:, None, None]
    )
    scaled = (weights * gain_rows[:, None, None]).astype(jnp.bfloat16).reshape(shifted.shape[0], -1)
    numerator = lax.dot_general(
        scaled, shifted, (((0,), (0,)), ((), ())), preferred_element_type=jnp.float32
    )
    summed = jnp.sum(weights, axis=1) * (gain_rows * gain_rows)[:, None]
    bin_weight = lax.dot_general(summed, bin_rows, (((0,), (0,)), ((), ())), precision=HIGHEST)
    return (numerator, bin_weight)


def per_device(
    particles, references, ctf_table, spectral_reg, defocus_bin, group_counts, group_scale,
    *, n_blk, n_cls,
):
    cosine_table, sine_table = phase_tables()
    ctf_square = ctf_table * ctf_table
    batch_size, width = particles.shape
    ref_tile = references[0]
    own_norms = tile_norms(ref_tile, ctf_square)
    classes_here = ref_tile.shape[0]
    shifts_count = cosine_table.shape[0]

    small = n_blk <= 4
    if small:
        packed = pack_rows(particles, group_counts, group_scale, defocus_bin)
        everyone = shift_gather(packed, "blk", n_blk)
        images = everyone[:, :width]
        meta_all = everyone[:, width : width + 5].astype(jnp.float32)
        gain_all = (meta_all[:, 0] + meta_all[:, 1]) + meta_all[:, 2]
        live_all = meta_all[:, 3]
        bins_all = meta_all[:, 4]
        live_mask = live_all[:batch_size]
    else:
        gain_rows, live_mask = slot_weights(
            group_counts.reshape(1, -1), group_scale.reshape(1, -1), batch_size
        )
        images = lax.all_gather(particles, "blk", axis=0, tiled=True)
        gain_all, bins_all, live_all = (
            lax.all_gather(gain_rows, "blk", axis=0, tiled=True),
            lax.all_gather(defocus_bin.astype(jnp.float32), "blk", axis=0, tiled=True),
            lax.all_gather(live_mask, "blk", axis=0, tiled=True),
        )
    whole_count = images.shape[0]

    bin_rows = bin_matrix(bins_all)
    ctf_rows = jnp.dot(bin_rows, ctf_table, precision=HIGHEST)
    shifted = shifted_rows(images, ctf_rows, cosine_table, sine_table)
    all_scores = tile_scores(shifted, ref_tile, own_norms, gain_all, bin_rows)
    flattened = all_scores.reshape(whole_count, -1)
    peak_all = jnp.max(flattened, axis=1)
    totals_all = jnp.sum(jnp.exp(flattened - peak_all[:, None]), axis=1)

    if small and n_cls & (n_cls - 1) == 0:
        peak_all, totals_all = xor_butterfly((peak_all, totals_all), "cls", n_cls)
        stats = jnp.stack([peak_all, totals_all]).reshape(2, n_blk, batch_size)
        parts = [stats] + [
            jnp.roll(lax.ppermute(stats, "blk", [(i, (i + k) % n_blk) for i in range(n_blk)]), k, axis=1)
            for k in range(1, n_blk)
        ]
        parts = jnp.stack(parts)
        peak_all, totals_all = combine_many(parts[:, 0], parts[:, 1])
        peak_all = peak_all.reshape(-1)
        totals_all = totals_all.reshape(-1)
        peak_score = peak_all[:batch_size]
        totals = totals_all[:batch_size]
    else:
        gathered = lax.all_gather(jnp.stack([peak_all, totals_all]), ("blk", "cls"))
        peak_all, totals_all = combine_many(gathered[:, 0], gathered[:, 1])
        if small:
            own_offset = 0
        else:
            own_offset = lax.axis_index("blk") * batch_size
        peak_score = lax.dynamic_slice_in_dim(peak_all, own_offset, batch_size)
        totals = lax.dynamic_slice_in_dim(totals_all, own_offset, batch_size)

    numerator, bin_weight = accumulate(
        shifted, all_scores, gain_all, bin_rows, live_all, peak_all, totals_all
    )
    log_evidence = jnp.where(live_mask > 0.5, peak_score + jnp.log(totals), 0.0)
    denominator = jnp.dot(bin_weight, ctf_square, precision=HIGHEST)
    denominator = (
        jnp.concatenate([denominator, denominator], axis=1)
        + jnp.concatenate([spectral_reg, spectral_reg])[None, :]
    )
    class_average = (numerator / denominator)[None]
    return (class_average, log_evidence)


def solution(mesh):
    placed = (
        P(("groups", "blk"), None),
        P("blk", ("groups", "cls"), None),
        P("groups", None),
        P("groups"),
        P(("groups", "blk")),
        P(("groups", "blk")),
        P(("groups", "blk")),
    )
    body = lambda *args: per_device(*args, n_blk=mesh.shape["blk"], n_cls=mesh.shape["cls"])
    return jax.shard_map(
        body,
        mesh=mesh,
        in_specs=placed,
        out_specs=(P("blk", ("groups", "cls"), None), P(("groups", "blk"))),
        check_vma=False,
    )
```

```python
import math

import jax
import jax.numpy as jnp
from jax import lax
from jax.experimental import pallas as pl
from jax.experimental.pallas import tpu as pltpu
from jax.sharding import PartitionSpec as P

KX = 32
KY = 64
IMG = 128
SIDE = 4
BINS = 16
META = 128


HIGHEST = lax.Precision.HIGHEST


def phase_tables():
    column = jnp.arange(KX * KY, dtype=jnp.int32)
    freq_x = (column % KX).astype(jnp.float32)
    freq_y = (column // KX - KY // 2).astype(jnp.float32)
    offsets = jnp.arange(SIDE, dtype=jnp.float32) - (SIDE - 1) / 2.0
    shift_x = jnp.tile(offsets, SIDE)
    shift_y = jnp.repeat(offsets, SIDE)
    phases = (
        2.0
        * math.pi
        / IMG
        * (shift_x[:, None] * freq_x[None, :] + shift_y[:, None] * freq_y[None, :])
    )
    return (jnp.cos(phases), jnp.sin(phases))


def bin_matrix(bin_values):
    return (bin_values[:, None] == jnp.arange(BINS, dtype=jnp.float32)[None, :]).astype(jnp.float32)


def slot_weights(group_sizes, scale_rows, slots):
    group_ends = jnp.cumsum(group_sizes, axis=1)
    group_starts = group_ends - group_sizes
    slot_index = jnp.arange(slots, dtype=jnp.int32)
    membership = (
        (slot_index[None, :, None] >= group_starts[:, None, :])
        & (slot_index[None, :, None] < group_ends[:, None, :])
    ).astype(jnp.float32)
    gain_rows = jnp.sum(membership * scale_rows[:, None, :], axis=2)
    live_mask = jnp.sum(membership, axis=2)
    return (gain_rows.reshape(-1), live_mask.reshape(-1))


def shifted_rows(images, ctf_rows, cosine_table, sine_table):
    half_width = ctf_rows.shape[1]
    real_part = images[:, :half_width].astype(jnp.float32)[:, None, :]
    imag_part = images[:, half_width:].astype(jnp.float32)[:, None, :]
    ctf_wide = ctf_rows[:, None, :]
    new_real = (real_part * cosine_table + imag_part * sine_table) * ctf_wide
    new_imag = (imag_part * cosine_table - real_part * sine_table) * ctf_wide
    joined = jnp.concatenate([new_real, new_imag], axis=2).astype(jnp.bfloat16)
    return joined.reshape(images.shape[0] * cosine_table.shape[0], 2 * half_width)


def tile_norms(ref_rows, ctf_square):
    half_width = ctf_square.shape[1]
    values = ref_rows.astype(jnp.float32)
    power_sum = (
        values[:, :half_width] * values[:, :half_width]
        + values[:, half_width:] * values[:, half_width:]
    )
    return lax.dot_general(ctf_square, power_sum, (((1,), (1,)), ((), ())), precision=HIGHEST)


def tile_scores(shifted, ref_rows, norms, gain_rows, bin_rows):
    count_here = gain_rows.shape[0]
    products = lax.dot_general(
        shifted, ref_rows, (((1,), (1,)), ((), ())), preferred_element_type=jnp.float32
    )
    products = products.reshape(count_here, shifted.shape[0] // count_here, ref_rows.shape[0])
    norm_term = jnp.dot(bin_rows, norms, precision=HIGHEST)
    return (
        gain_rows[:, None, None] * products
        - 0.5 * (gain_rows * gain_rows)[:, None, None] * norm_term[:, None, :]
    )


def combine_stats(former, latter):
    new_peak = jnp.maximum(former[0], latter[0])
    return (
        new_peak,
        former[1] * jnp.exp(former[0] - new_peak) + latter[1] * jnp.exp(latter[0] - new_peak),
    )


def combine_many(peaks, totals):
    new_peak = jnp.max(peaks, axis=0)
    return (new_peak, jnp.sum(totals * jnp.exp(peaks - new_peak[None]), axis=0))


def split_exact(value):
    high = lax.reduce_precision(value, exponent_bits=8, mantissa_bits=7)
    rest = value - high
    middle = lax.reduce_precision(rest, exponent_bits=8, mantissa_bits=7)
    return (high, middle, rest - middle)


def pack_kernel(sizes_ref, scales_ref, bins_ref, images_ref, out_ref):
    slots, width = images_ref.shape
    row = lax.broadcasted_iota(jnp.int32, (slots, META), 0)
    column = lax.broadcasted_iota(jnp.int32, (slots, META), 1)
    start = jnp.int32(0)
    gain = jnp.zeros((slots, META), jnp.float32)
    live = jnp.zeros((slots, META), jnp.float32)
    for group in range(sizes_ref.shape[0]):
        size = sizes_ref[group]
        inside = (row >= start) & (row < start + size)
        gain = jnp.where(inside, scales_ref[group], gain)
        live = jnp.where(inside, 1.0, live)
        start = start + size
    bins = jnp.zeros((slots, META), jnp.float32)
    for slot in range(slots):
        bins = jnp.where(row == slot, bins_ref[slot].astype(jnp.float32), bins)
    high = gain.astype(jnp.bfloat16).astype(jnp.float32)
    rest = gain - high
    middle = rest.astype(jnp.bfloat16).astype(jnp.float32)
    fields = (high, middle, rest - middle, live, bins)
    meta = jnp.zeros((slots, META), jnp.float32)
    for index, field in enumerate(fields):
        meta = jnp.where(column == index, field, meta)
    out_ref[:, :width] = images_ref[...]
    out_ref[:, width:] = meta.astype(out_ref.dtype)


def pack_rows(particles, group_counts, group_scale, defocus_bin):
    slots, width = particles.shape
    scalar = pl.BlockSpec(memory_space=pltpu.SMEM)
    whole = pl.BlockSpec(memory_space=pltpu.VMEM)
    return pl.pallas_call(
        pack_kernel,
        out_shape=jax.ShapeDtypeStruct((slots, width + META), particles.dtype),
        in_specs=[scalar, scalar, scalar, whole],
        out_specs=whole,
    )(group_counts, group_scale, defocus_bin, particles)


def shift_gather(value, axis, size):
    pieces = [value] + [
        lax.ppermute(value, axis, [(i, (i + k) % size) for i in range(size)])
        for k in range(1, size)
    ]
    return jnp.concatenate(pieces, axis=0)


def xor_butterfly(stats, axis, size):
    step = 1
    while step < size:
        other = lax.ppermute(stats, axis, [(i, i ^ step) for i in range(size)])
        stats = jnp.stack(combine_stats(stats, other))
        step *= 2
    return stats


def accumulate(shifted, scores, gain_rows, ctf_rows, live_mask, peak_score, totals):
    weights = (
        jnp.exp(scores - peak_score[:, None, None])
        / totals[:, None, None]
        * live_mask[:, None, None]
    )
    scaled = (weights * gain_rows[:, None, None]).astype(jnp.bfloat16).reshape(shifted.shape[0], -1)
    numerator = lax.dot_general(
        scaled, shifted, (((0,), (0,)), ((), ())), preferred_element_type=jnp.float32
    )
    summed = jnp.sum(weights, axis=1) * (gain_rows * gain_rows)[:, None]
    denominator = lax.dot_general(
        summed, ctf_rows * ctf_rows, (((0,), (0,)), ((), ())), precision=HIGHEST
    )
    return (numerator, denominator)


def per_device(
    particles, references, ctf_table, spectral_reg, defocus_bin, group_counts, group_scale,
    *, n_blk, n_cls,
):
    cosine_table, sine_table = phase_tables()
    ctf_square = ctf_table * ctf_table
    batch_size, width = particles.shape
    ref_tile = references[0]
    own_norms = tile_norms(ref_tile, ctf_square)
    classes_here = ref_tile.shape[0]
    shifts_count = cosine_table.shape[0]

    small = n_blk <= 4
    if small:
        packed = pack_rows(particles, group_counts, group_scale, defocus_bin)
        everyone = shift_gather(packed, "blk", n_blk)
        images = everyone[:, :width]
        meta_all = everyone[:, width : width + 5].astype(jnp.float32)
        gain_all = (meta_all[:, 0] + meta_all[:, 1]) + meta_all[:, 2]
        live_all = meta_all[:, 3]
        bins_all = meta_all[:, 4]
        live_mask = live_all[:batch_size]
    else:
        gain_rows, live_mask = slot_weights(
            group_counts.reshape(1, -1), group_scale.reshape(1, -1), batch_size
        )
        images = lax.all_gather(particles, "blk", axis=0, tiled=True)
        gain_all, bins_all, live_all = (
            lax.all_gather(gain_rows, "blk", axis=0, tiled=True),
            lax.all_gather(defocus_bin.astype(jnp.float32), "blk", axis=0, tiled=True),
            lax.all_gather(live_mask, "blk", axis=0, tiled=True),
        )
    whole_count = images.shape[0]

    bin_rows = bin_matrix(bins_all)
    ctf_rows = jnp.dot(bin_rows, ctf_table, precision=HIGHEST)
    shifted = shifted_rows(images, ctf_rows, cosine_table, sine_table)
    all_scores = tile_scores(shifted, ref_tile, own_norms, gain_all, bin_rows)
    flattened = all_scores.reshape(whole_count, -1)
    peak_all = jnp.max(flattened, axis=1)
    totals_all = jnp.sum(jnp.exp(flattened - peak_all[:, None]), axis=1)

    if small and n_cls & (n_cls - 1) == 0:
        stats = xor_butterfly(jnp.stack([peak_all, totals_all]), "cls", n_cls)
        stats = stats.reshape(2, n_blk, batch_size)
        parts = [stats] + [
            jnp.roll(lax.ppermute(stats, "blk", [(i, (i + k) % n_blk) for i in range(n_blk)]), k, axis=1)
            for k in range(1, n_blk)
        ]
        parts = jnp.stack(parts)
        peak_all, totals_all = combine_many(parts[:, 0], parts[:, 1])
        peak_all = peak_all.reshape(-1)
        totals_all = totals_all.reshape(-1)
        peak_score = peak_all[:batch_size]
        totals = totals_all[:batch_size]
    else:
        gathered = lax.all_gather(jnp.stack([peak_all, totals_all]), ("blk", "cls"))
        peak_all, totals_all = combine_many(gathered[:, 0], gathered[:, 1])
        if small:
            own_offset = 0
        else:
            own_offset = lax.axis_index("blk") * batch_size
        peak_score = lax.dynamic_slice_in_dim(peak_all, own_offset, batch_size)
        totals = lax.dynamic_slice_in_dim(totals_all, own_offset, batch_size)

    numerator, denominator = accumulate(
        shifted, all_scores, gain_all, ctf_rows, live_all, peak_all, totals_all
    )
    log_evidence = jnp.where(live_mask > 0.5, peak_score + jnp.log(totals), 0.0)
    denominator = (
        jnp.concatenate([denominator, denominator], axis=1)
        + jnp.concatenate([spectral_reg, spectral_reg])[None, :]
    )
    class_average = (numerator / denominator)[None]
    return (class_average, log_evidence)


def solution(mesh):
    placed = (
        P(("groups", "blk"), None),
        P("blk", ("groups", "cls"), None),
        P("groups", None),
        P("groups"),
        P(("groups", "blk")),
        P(("groups", "blk")),
        P(("groups", "blk")),
    )
    body = lambda *args: per_device(*args, n_blk=mesh.shape["blk"], n_cls=mesh.shape["cls"])
    return jax.shard_map(
        body,
        mesh=mesh,
        in_specs=placed,
        out_specs=(P("blk", ("groups", "cls"), None), P(("groups", "blk"))),
        check_vma=False,
    )
```

```python
import math

import jax
import numpy as np
import jax.numpy as jnp
from jax import lax
from jax.experimental import pallas as pl
from jax.experimental.pallas import tpu as pltpu
from jax.sharding import PartitionSpec as P

KX = 32
KY = 64
IMG = 128
SIDE = 4
BINS = 16
META = 128


HIGHEST = lax.Precision.HIGHEST


def phase_tables():
    column = np.arange(KX * KY, dtype=np.int32)
    freq_x = (column % KX).astype(np.float32)
    freq_y = (column // KX - KY // 2).astype(np.float32)
    offsets = np.arange(SIDE, dtype=np.float32) - np.float32((SIDE - 1) / 2.0)
    shift_x = np.tile(offsets, SIDE)
    shift_y = np.repeat(offsets, SIDE)
    phases = np.float32(2.0 * math.pi / IMG) * (
        shift_x[:, None] * freq_x[None, :] + shift_y[:, None] * freq_y[None, :]
    )
    return (jnp.asarray(np.cos(phases)), jnp.asarray(np.sin(phases)))


def bin_matrix(bin_values):
    return (bin_values[:, None] == jnp.arange(BINS, dtype=jnp.float32)[None, :]).astype(jnp.float32)


def slot_weights(group_sizes, scale_rows, slots):
    group_ends = jnp.cumsum(group_sizes, axis=1)
    group_starts = group_ends - group_sizes
    slot_index = jnp.arange(slots, dtype=jnp.int32)
    membership = (
        (slot_index[None, :, None] >= group_starts[:, None, :])
        & (slot_index[None, :, None] < group_ends[:, None, :])
    ).astype(jnp.float32)
    gain_rows = jnp.sum(membership * scale_rows[:, None, :], axis=2)
    live_mask = jnp.sum(membership, axis=2)
    return (gain_rows.reshape(-1), live_mask.reshape(-1))


def shifted_rows(images, ctf_rows, cosine_table, sine_table):
    half_width = ctf_rows.shape[1]
    real_part = images[:, :half_width].astype(jnp.float32)[:, None, :]
    imag_part = images[:, half_width:].astype(jnp.float32)[:, None, :]
    ctf_wide = ctf_rows[:, None, :]
    new_real = (real_part * cosine_table + imag_part * sine_table) * ctf_wide
    new_imag = (imag_part * cosine_table - real_part * sine_table) * ctf_wide
    joined = jnp.concatenate([new_real, new_imag], axis=2).astype(jnp.bfloat16)
    return joined.reshape(images.shape[0] * cosine_table.shape[0], 2 * half_width)


def tile_norms(ref_rows, ctf_square):
    half_width = ctf_square.shape[1]
    values = ref_rows.astype(jnp.float32)
    power_sum = (
        values[:, :half_width] * values[:, :half_width]
        + values[:, half_width:] * values[:, half_width:]
    )
    return lax.dot_general(ctf_square, power_sum, (((1,), (1,)), ((), ())), precision=HIGHEST)


def tile_scores(shifted, ref_rows, norms, gain_rows, bin_rows):
    count_here = gain_rows.shape[0]
    products = lax.dot_general(
        shifted, ref_rows, (((1,), (1,)), ((), ())), preferred_element_type=jnp.float32
    )
    products = products.reshape(count_here, shifted.shape[0] // count_here, ref_rows.shape[0])
    norm_term = jnp.dot(bin_rows, norms, precision=HIGHEST)
    return (
        gain_rows[:, None, None] * products
        - 0.5 * (gain_rows * gain_rows)[:, None, None] * norm_term[:, None, :]
    )


def combine_stats(former, latter):
    new_peak = jnp.maximum(former[0], latter[0])
    return (
        new_peak,
        former[1] * jnp.exp(former[0] - new_peak) + latter[1] * jnp.exp(latter[0] - new_peak),
    )


def combine_many(peaks, totals):
    new_peak = jnp.max(peaks, axis=0)
    return (new_peak, jnp.sum(totals * jnp.exp(peaks - new_peak[None]), axis=0))


def split_exact(value):
    high = lax.reduce_precision(value, exponent_bits=8, mantissa_bits=7)
    rest = value - high
    middle = lax.reduce_precision(rest, exponent_bits=8, mantissa_bits=7)
    return (high, middle, rest - middle)


def pack_kernel(sizes_ref, scales_ref, bins_ref, images_ref, out_ref):
    slots, width = images_ref.shape
    row = lax.broadcasted_iota(jnp.int32, (slots, META), 0)
    column = lax.broadcasted_iota(jnp.int32, (slots, META), 1)
    start = jnp.int32(0)
    gain = jnp.zeros((slots, META), jnp.float32)
    live = jnp.zeros((slots, META), jnp.float32)
    for group in range(sizes_ref.shape[0]):
        size = sizes_ref[group]
        inside = (row >= start) & (row < start + size)
        gain = jnp.where(inside, scales_ref[group], gain)
        live = jnp.where(inside, 1.0, live)
        start = start + size
    bins = jnp.zeros((slots, META), jnp.float32)
    for slot in range(slots):
        bins = jnp.where(row == slot, bins_ref[slot].astype(jnp.float32), bins)
    high = gain.astype(jnp.bfloat16).astype(jnp.float32)
    rest = gain - high
    middle = rest.astype(jnp.bfloat16).astype(jnp.float32)
    fields = (high, middle, rest - middle, live, bins)
    meta = jnp.zeros((slots, META), jnp.float32)
    for index, field in enumerate(fields):
        meta = jnp.where(column == index, field, meta)
    out_ref[:, :width] = images_ref[...]
    out_ref[:, width:] = meta.astype(out_ref.dtype)


def pack_rows(particles, group_counts, group_scale, defocus_bin):
    slots, width = particles.shape
    scalar = pl.BlockSpec(memory_space=pltpu.SMEM)
    whole = pl.BlockSpec(memory_space=pltpu.VMEM)
    return pl.pallas_call(
        pack_kernel,
        out_shape=jax.ShapeDtypeStruct((slots, width + META), particles.dtype),
        in_specs=[scalar, scalar, scalar, whole],
        out_specs=whole,
    )(group_counts, group_scale, defocus_bin, particles)


def shift_gather(value, axis, size):
    pieces = [value] + [
        lax.ppermute(value, axis, [(i, (i + k) % size) for i in range(size)])
        for k in range(1, size)
    ]
    return jnp.concatenate(pieces, axis=0)


def xor_butterfly(stats, axis, size):
    step = 1
    while step < size:
        other = lax.ppermute(stats, axis, [(i, i ^ step) for i in range(size)])
        stats = jnp.stack(combine_stats(stats, other))
        step *= 2
    return stats


def accumulate(pieces, scores, gain_rows, ctf_rows, live_mask, peak_score, totals):
    weights = (
        jnp.exp(scores - peak_score[:, None, None])
        / totals[:, None, None]
        * live_mask[:, None, None]
    )
    scaled = (weights * gain_rows[:, None, None]).astype(jnp.bfloat16)
    numerator = None
    start = 0
    for shifted in pieces:
        count = shifted.shape[0] // scaled.shape[1]
        part = lax.dot_general(
            scaled[start : start + count].reshape(shifted.shape[0], -1),
            shifted,
            (((0,), (0,)), ((), ())),
            preferred_element_type=jnp.float32,
        )
        numerator = part if numerator is None else numerator + part
        start += count
    summed = jnp.sum(weights, axis=1) * (gain_rows * gain_rows)[:, None]
    denominator = lax.dot_general(
        summed, ctf_rows * ctf_rows, (((0,), (0,)), ((), ())), precision=HIGHEST
    )
    return (numerator, denominator)


def block_rows(images, gains, bins, norms, ref_tile, ctf_table, cosine_table, sine_table):
    bin_rows = bin_matrix(bins)
    ctf_rows = jnp.dot(bin_rows, ctf_table, precision=HIGHEST)
    shifted = shifted_rows(images, ctf_rows, cosine_table, sine_table)
    scores = tile_scores(shifted, ref_tile, norms, gains, bin_rows)
    return (shifted, scores, ctf_rows)


def per_device(
    particles, references, ctf_table, spectral_reg, defocus_bin, group_counts, group_scale,
    *, n_blk, n_cls,
):
    cosine_table, sine_table = phase_tables()
    ctf_square = ctf_table * ctf_table
    batch_size, width = particles.shape
    ref_tile = references[0]
    own_norms = tile_norms(ref_tile, ctf_square)
    classes_here = ref_tile.shape[0]
    shifts_count = cosine_table.shape[0]

    small = n_blk <= 4
    tables = (ref_tile, ctf_table, cosine_table, sine_table)
    if small:
        packed = pack_rows(particles, group_counts, group_scale, defocus_bin)
        others = shift_gather(packed, "blk", n_blk)[batch_size:]
        groups = []
        for rows in (packed, others):
            meta = rows[:, width : width + 5].astype(jnp.float32)
            gains = (meta[:, 0] + meta[:, 1]) + meta[:, 2]
            groups.append((rows[:, :width], gains, meta[:, 3], meta[:, 4]))
        live_mask = groups[0][2]
    else:
        gain_rows, live_mask = slot_weights(
            group_counts.reshape(1, -1), group_scale.reshape(1, -1), batch_size
        )
        groups = [(
            lax.all_gather(particles, "blk", axis=0, tiled=True),
            lax.all_gather(gain_rows, "blk", axis=0, tiled=True),
            lax.all_gather(live_mask, "blk", axis=0, tiled=True),
            lax.all_gather(defocus_bin.astype(jnp.float32), "blk", axis=0, tiled=True),
        )]
    results = [block_rows(images, gains, bins, own_norms, *tables) for images, gains, _, bins in groups]
    pieces = [shifted for shifted, _, _ in results]
    all_scores = jnp.concatenate([scores for _, scores, _ in results], axis=0)
    ctf_rows = jnp.concatenate([rows for _, _, rows in results], axis=0)
    gain_all = jnp.concatenate([group[1] for group in groups])
    live_all = jnp.concatenate([group[2] for group in groups])
    whole_count = all_scores.shape[0]
    flattened = all_scores.reshape(whole_count, -1)
    peak_all = jnp.max(flattened, axis=1)
    totals_all = jnp.sum(jnp.exp(flattened - peak_all[:, None]), axis=1)

    if small and n_cls & (n_cls - 1) == 0:
        stats = xor_butterfly(jnp.stack([peak_all, totals_all]), "cls", n_cls)
        stats = stats.reshape(2, n_blk, batch_size)
        parts = [stats] + [
            jnp.roll(lax.ppermute(stats, "blk", [(i, (i + k) % n_blk) for i in range(n_blk)]), k, axis=1)
            for k in range(1, n_blk)
        ]
        parts = jnp.stack(parts)
        peak_all, totals_all = combine_many(parts[:, 0], parts[:, 1])
        peak_all = peak_all.reshape(-1)
        totals_all = totals_all.reshape(-1)
        peak_score = peak_all[:batch_size]
        totals = totals_all[:batch_size]
    else:
        gathered = lax.all_gather(jnp.stack([peak_all, totals_all]), ("blk", "cls"))
        peak_all, totals_all = combine_many(gathered[:, 0], gathered[:, 1])
        if small:
            own_offset = 0
        else:
            own_offset = lax.axis_index("blk") * batch_size
        peak_score = lax.dynamic_slice_in_dim(peak_all, own_offset, batch_size)
        totals = lax.dynamic_slice_in_dim(totals_all, own_offset, batch_size)

    numerator, denominator = accumulate(
        pieces, all_scores, gain_all, ctf_rows, live_all, peak_all, totals_all
    )
    log_evidence = jnp.where(live_mask > 0.5, peak_score + jnp.log(totals), 0.0)
    denominator = (
        jnp.concatenate([denominator, denominator], axis=1)
        + jnp.concatenate([spectral_reg, spectral_reg])[None, :]
    )
    class_average = (numerator / denominator)[None]
    return (class_average, log_evidence)


def solution(mesh):
    placed = (
        P(("groups", "blk"), None),
        P("blk", ("groups", "cls"), None),
        P("groups", None),
        P("groups"),
        P(("groups", "blk")),
        P(("groups", "blk")),
        P(("groups", "blk")),
    )
    body = lambda *args: per_device(*args, n_blk=mesh.shape["blk"], n_cls=mesh.shape["cls"])
    return jax.shard_map(
        body,
        mesh=mesh,
        in_specs=placed,
        out_specs=(P("blk", ("groups", "cls"), None), P(("groups", "blk"))),
        check_vma=False,
    )
```

```python
import math

import jax
import numpy as np
import jax.numpy as jnp
from jax import lax
from jax.experimental import pallas as pl
from jax.experimental.pallas import tpu as pltpu
from jax.sharding import PartitionSpec as P

KX = 32
KY = 64
IMG = 128
SIDE = 4
BINS = 16
META = 128


HIGHEST = lax.Precision.HIGHEST


def phase_tables():
    column = np.arange(KX * KY, dtype=np.int32)
    freq_x = (column % KX).astype(np.float32)
    freq_y = (column // KX - KY // 2).astype(np.float32)
    offsets = np.arange(SIDE, dtype=np.float32) - np.float32((SIDE - 1) / 2.0)
    shift_x = np.tile(offsets, SIDE)
    shift_y = np.repeat(offsets, SIDE)
    phases = np.float32(2.0 * math.pi / IMG) * (
        shift_x[:, None] * freq_x[None, :] + shift_y[:, None] * freq_y[None, :]
    )
    return (jnp.asarray(np.cos(phases)), jnp.asarray(np.sin(phases)))


def bin_matrix(bin_values):
    return (bin_values[:, None] == jnp.arange(BINS, dtype=jnp.float32)[None, :]).astype(jnp.float32)


def slot_weights(group_sizes, scale_rows, slots):
    group_ends = jnp.cumsum(group_sizes, axis=1)
    group_starts = group_ends - group_sizes
    slot_index = jnp.arange(slots, dtype=jnp.int32)
    membership = (
        (slot_index[None, :, None] >= group_starts[:, None, :])
        & (slot_index[None, :, None] < group_ends[:, None, :])
    ).astype(jnp.float32)
    gain_rows = jnp.sum(membership * scale_rows[:, None, :], axis=2)
    live_mask = jnp.sum(membership, axis=2)
    return (gain_rows.reshape(-1), live_mask.reshape(-1))


def shifted_rows(images, ctf_rows, cosine_table, sine_table):
    half_width = ctf_rows.shape[1]
    real_part = images[:, :half_width].astype(jnp.float32)[:, None, :]
    imag_part = images[:, half_width:].astype(jnp.float32)[:, None, :]
    ctf_wide = ctf_rows[:, None, :]
    new_real = (real_part * cosine_table + imag_part * sine_table) * ctf_wide
    new_imag = (imag_part * cosine_table - real_part * sine_table) * ctf_wide
    joined = jnp.concatenate([new_real, new_imag], axis=2).astype(jnp.bfloat16)
    return joined.reshape(images.shape[0] * cosine_table.shape[0], 2 * half_width)


def tile_norms(ref_rows, ctf_square):
    half_width = ctf_square.shape[1]
    real_part = ref_rows[:, :half_width].astype(jnp.float32)
    imag_part = ref_rows[:, half_width:].astype(jnp.float32)
    power_sum = real_part * real_part + imag_part * imag_part
    return lax.dot_general(ctf_square, power_sum, (((1,), (1,)), ((), ())), precision=HIGHEST)


def tile_scores(shifted, ref_rows, norms, gain_rows, bin_rows):
    count_here = gain_rows.shape[0]
    products = lax.dot_general(
        shifted, ref_rows, (((1,), (1,)), ((), ())), preferred_element_type=jnp.float32
    )
    products = products.reshape(count_here, shifted.shape[0] // count_here, ref_rows.shape[0])
    norm_term = jnp.dot(bin_rows, norms, precision=HIGHEST)
    return (
        gain_rows[:, None, None] * products
        - 0.5 * (gain_rows * gain_rows)[:, None, None] * norm_term[:, None, :]
    )


def combine_stats(former, latter):
    new_peak = jnp.maximum(former[0], latter[0])
    return (
        new_peak,
        former[1] * jnp.exp(former[0] - new_peak) + latter[1] * jnp.exp(latter[0] - new_peak),
    )


def combine_many(peaks, totals):
    new_peak = jnp.max(peaks, axis=0)
    return (new_peak, jnp.sum(totals * jnp.exp(peaks - new_peak[None]), axis=0))


def split_exact(value):
    high = lax.reduce_precision(value, exponent_bits=8, mantissa_bits=7)
    rest = value - high
    middle = lax.reduce_precision(rest, exponent_bits=8, mantissa_bits=7)
    return (high, middle, rest - middle)


def pack_kernel(sizes_ref, scales_ref, bins_ref, images_ref, out_ref):
    slots, width = images_ref.shape
    row = lax.broadcasted_iota(jnp.int32, (slots, META), 0)
    column = lax.broadcasted_iota(jnp.int32, (slots, META), 1)
    start = jnp.int32(0)
    gain = jnp.zeros((slots, META), jnp.float32)
    live = jnp.zeros((slots, META), jnp.float32)
    for group in range(sizes_ref.shape[0]):
        size = sizes_ref[group]
        inside = (row >= start) & (row < start + size)
        gain = jnp.where(inside, scales_ref[group], gain)
        live = jnp.where(inside, 1.0, live)
        start = start + size
    bins = jnp.zeros((slots, META), jnp.float32)
    for slot in range(slots):
        bins = jnp.where(row == slot, bins_ref[slot].astype(jnp.float32), bins)
    high = gain.astype(jnp.bfloat16).astype(jnp.float32)
    rest = gain - high
    middle = rest.astype(jnp.bfloat16).astype(jnp.float32)
    fields = (high, middle, rest - middle, live, bins)
    meta = jnp.zeros((slots, META), jnp.float32)
    for index, field in enumerate(fields):
        meta = jnp.where(column == index, field, meta)
    out_ref[:, :width] = images_ref[...]
    out_ref[:, width:] = meta.astype(out_ref.dtype)


def pack_rows(particles, group_counts, group_scale, defocus_bin):
    slots, width = particles.shape
    scalar = pl.BlockSpec(memory_space=pltpu.SMEM)
    whole = pl.BlockSpec(memory_space=pltpu.VMEM)
    return pl.pallas_call(
        pack_kernel,
        out_shape=jax.ShapeDtypeStruct((slots, width + META), particles.dtype),
        in_specs=[scalar, scalar, scalar, whole],
        out_specs=whole,
    )(group_counts, group_scale, defocus_bin, particles)


def shift_gather(value, axis, size):
    pieces = [value] + [
        lax.ppermute(value, axis, [(i, (i + k) % size) for i in range(size)])
        for k in range(1, size)
    ]
    return jnp.concatenate(pieces, axis=0)


def xor_butterfly(stats, axis, size):
    step = 1
    while step < size:
        other = lax.ppermute(stats, axis, [(i, i ^ step) for i in range(size)])
        stats = jnp.stack(combine_stats(stats, other))
        step *= 2
    return stats


def accumulate(pieces, scores, gain_rows, ctf_rows, live_mask, peak_score, totals):
    weights = (
        jnp.exp(scores - peak_score[:, None, None])
        / totals[:, None, None]
        * live_mask[:, None, None]
    )
    scaled = (weights * gain_rows[:, None, None]).astype(jnp.bfloat16)
    numerator = None
    start = 0
    for shifted in pieces:
        count = shifted.shape[0] // scaled.shape[1]
        part = lax.dot_general(
            scaled[start : start + count].reshape(shifted.shape[0], -1),
            shifted,
            (((0,), (0,)), ((), ())),
            preferred_element_type=jnp.float32,
        )
        numerator = part if numerator is None else numerator + part
        start += count
    summed = jnp.sum(weights, axis=1) * (gain_rows * gain_rows)[:, None]
    denominator = lax.dot_general(
        summed, ctf_rows * ctf_rows, (((0,), (0,)), ((), ())), precision=HIGHEST
    )
    return (numerator, denominator)


def block_rows(images, gains, bins, norms, ref_tile, ctf_table, cosine_table, sine_table):
    bin_rows = bin_matrix(bins)
    ctf_rows = jnp.dot(bin_rows, ctf_table, precision=HIGHEST)
    shifted = shifted_rows(images, ctf_rows, cosine_table, sine_table)
    scores = tile_scores(shifted, ref_tile, norms, gains, bin_rows)
    return (shifted, scores, ctf_rows)


def per_device(
    particles, references, ctf_table, spectral_reg, defocus_bin, group_counts, group_scale,
    *, n_blk, n_cls,
):
    cosine_table, sine_table = phase_tables()
    ctf_square = ctf_table * ctf_table
    batch_size, width = particles.shape
    ref_tile = references[0]
    own_norms = tile_norms(ref_tile, ctf_square)
    classes_here = ref_tile.shape[0]
    shifts_count = cosine_table.shape[0]

    small = n_blk <= 4
    tables = (ref_tile, ctf_table, cosine_table, sine_table)
    if small:
        packed = pack_rows(particles, group_counts, group_scale, defocus_bin)
        others = shift_gather(packed, "blk", n_blk)[batch_size:]
        groups = []
        for rows in (packed, others):
            meta = rows[:, width : width + 5].astype(jnp.float32)
            gains = (meta[:, 0] + meta[:, 1]) + meta[:, 2]
            groups.append((rows[:, :width], gains, meta[:, 3], meta[:, 4]))
        live_mask = groups[0][2]
    else:
        gain_rows, live_mask = slot_weights(
            group_counts.reshape(1, -1), group_scale.reshape(1, -1), batch_size
        )
        groups = [(
            lax.all_gather(particles, "blk", axis=0, tiled=True),
            lax.all_gather(gain_rows, "blk", axis=0, tiled=True),
            lax.all_gather(live_mask, "blk", axis=0, tiled=True),
            lax.all_gather(defocus_bin.astype(jnp.float32), "blk", axis=0, tiled=True),
        )]
    results = [block_rows(images, gains, bins, own_norms, *tables) for images, gains, _, bins in groups]
    pieces = [shifted for shifted, _, _ in results]
    all_scores = jnp.concatenate([scores for _, scores, _ in results], axis=0)
    ctf_rows = jnp.concatenate([rows for _, _, rows in results], axis=0)
    gain_all = jnp.concatenate([group[1] for group in groups])
    live_all = jnp.concatenate([group[2] for group in groups])
    whole_count = all_scores.shape[0]
    flattened = all_scores.reshape(whole_count, -1)
    peak_all = jnp.max(flattened, axis=1)
    totals_all = jnp.sum(jnp.exp(flattened - peak_all[:, None]), axis=1)

    if small and n_cls & (n_cls - 1) == 0:
        stats = jnp.stack([peak_all, totals_all]).reshape(2, n_blk, batch_size)
        stats = xor_butterfly(stats, "cls", n_cls)
        parts = [stats] + [
            jnp.roll(lax.ppermute(stats, "blk", [(i, (i + k) % n_blk) for i in range(n_blk)]), k, axis=1)
            for k in range(1, n_blk)
        ]
        parts = jnp.stack(parts)
        peak_all, totals_all = combine_many(parts[:, 0], parts[:, 1])
        peak_all = peak_all.reshape(-1)
        totals_all = totals_all.reshape(-1)
        peak_score = peak_all[:batch_size]
        totals = totals_all[:batch_size]
    else:
        gathered = lax.all_gather(jnp.stack([peak_all, totals_all]), ("blk", "cls"))
        peak_all, totals_all = combine_many(gathered[:, 0], gathered[:, 1])
        if small:
            own_offset = 0
        else:
            own_offset = lax.axis_index("blk") * batch_size
        peak_score = lax.dynamic_slice_in_dim(peak_all, own_offset, batch_size)
        totals = lax.dynamic_slice_in_dim(totals_all, own_offset, batch_size)

    numerator, denominator = accumulate(
        pieces, all_scores, gain_all, ctf_rows, live_all, peak_all, totals_all
    )
    log_evidence = jnp.where(live_mask > 0.5, peak_score + jnp.log(totals), 0.0)
    denominator = (
        jnp.concatenate([denominator, denominator], axis=1)
        + jnp.concatenate([spectral_reg, spectral_reg])[None, :]
    )
    class_average = (numerator / denominator)[None]
    return (class_average, log_evidence)


def solution(mesh):
    placed = (
        P(("groups", "blk"), None),
        P("blk", ("groups", "cls"), None),
        P("groups", None),
        P("groups"),
        P(("groups", "blk")),
        P(("groups", "blk")),
        P(("groups", "blk")),
    )
    body = lambda *args: per_device(*args, n_blk=mesh.shape["blk"], n_cls=mesh.shape["cls"])
    return jax.shard_map(
        body,
        mesh=mesh,
        in_specs=placed,
        out_specs=(P("blk", ("groups", "cls"), None), P(("groups", "blk"))),
        check_vma=False,
    )
```

```python
import math

import jax
import numpy as np
import jax.numpy as jnp
from jax import lax
from jax.experimental import pallas as pl
from jax.experimental.pallas import tpu as pltpu
from jax.sharding import PartitionSpec as P

KX = 32
KY = 64
IMG = 128
SIDE = 4
BINS = 16
META = 128


HIGHEST = lax.Precision.HIGHEST


def phase_tables():
    column = np.arange(KX * KY, dtype=np.int32)
    freq_x = (column % KX).astype(np.float32)
    freq_y = (column // KX - KY // 2).astype(np.float32)
    offsets = np.arange(SIDE, dtype=np.float32) - np.float32((SIDE - 1) / 2.0)
    shift_x = np.tile(offsets, SIDE)
    shift_y = np.repeat(offsets, SIDE)
    phases = np.float32(2.0 * math.pi / IMG) * (
        shift_x[:, None] * freq_x[None, :] + shift_y[:, None] * freq_y[None, :]
    )
    return (jnp.asarray(np.cos(phases)), jnp.asarray(np.sin(phases)))


def bin_matrix(bin_values):
    return (bin_values[:, None] == jnp.arange(BINS, dtype=jnp.float32)[None, :]).astype(jnp.float32)


def slot_weights(group_sizes, scale_rows, slots):
    group_ends = jnp.cumsum(group_sizes, axis=1)
    group_starts = group_ends - group_sizes
    slot_index = jnp.arange(slots, dtype=jnp.int32)
    membership = (
        (slot_index[None, :, None] >= group_starts[:, None, :])
        & (slot_index[None, :, None] < group_ends[:, None, :])
    ).astype(jnp.float32)
    gain_rows = jnp.sum(membership * scale_rows[:, None, :], axis=2)
    live_mask = jnp.sum(membership, axis=2)
    return (gain_rows.reshape(-1), live_mask.reshape(-1))


def shifted_rows(images, ctf_rows, cosine_table, sine_table):
    half_width = ctf_rows.shape[1]
    real_part = images[:, :half_width].astype(jnp.float32)[:, None, :]
    imag_part = images[:, half_width:].astype(jnp.float32)[:, None, :]
    ctf_wide = ctf_rows[:, None, :]
    new_real = (real_part * cosine_table + imag_part * sine_table) * ctf_wide
    new_imag = (imag_part * cosine_table - real_part * sine_table) * ctf_wide
    joined = jnp.concatenate([new_real, new_imag], axis=2).astype(jnp.bfloat16)
    return joined.reshape(images.shape[0] * cosine_table.shape[0], 2 * half_width)


def tile_norms(ref_rows, ctf_square):
    half_width = ctf_square.shape[1]
    values = ref_rows.astype(jnp.float32)
    power_sum = (
        values[:, :half_width] * values[:, :half_width]
        + values[:, half_width:] * values[:, half_width:]
    )
    return lax.dot_general(ctf_square, power_sum, (((1,), (1,)), ((), ())), precision=HIGHEST)


def tile_scores(shifted, ref_rows, norms, gain_rows, bin_rows):
    count_here = gain_rows.shape[0]
    products = lax.dot_general(
        shifted, ref_rows, (((1,), (1,)), ((), ())), preferred_element_type=jnp.float32
    )
    products = products.reshape(count_here, shifted.shape[0] // count_here, ref_rows.shape[0])
    norm_term = jnp.dot(bin_rows, norms, precision=HIGHEST)
    return (
        gain_rows[:, None, None] * products
        - 0.5 * (gain_rows * gain_rows)[:, None, None] * norm_term[:, None, :]
    )


def combine_stats(former, latter):
    new_peak = jnp.maximum(former[0], latter[0])
    return (
        new_peak,
        former[1] * jnp.exp(former[0] - new_peak) + latter[1] * jnp.exp(latter[0] - new_peak),
    )


def combine_many(peaks, totals):
    new_peak = jnp.max(peaks, axis=0)
    return (new_peak, jnp.sum(totals * jnp.exp(peaks - new_peak[None]), axis=0))


def split_exact(value):
    high = lax.reduce_precision(value, exponent_bits=8, mantissa_bits=7)
    rest = value - high
    middle = lax.reduce_precision(rest, exponent_bits=8, mantissa_bits=7)
    return (high, middle, rest - middle)


def pack_kernel(sizes_ref, scales_ref, bins_ref, images_ref, out_ref):
    slots, width = images_ref.shape
    row = lax.broadcasted_iota(jnp.int32, (slots, META), 0)
    column = lax.broadcasted_iota(jnp.int32, (slots, META), 1)
    start = jnp.int32(0)
    gain = jnp.zeros((slots, META), jnp.float32)
    live = jnp.zeros((slots, META), jnp.float32)
    for group in range(sizes_ref.shape[0]):
        size = sizes_ref[group]
        inside = (row >= start) & (row < start + size)
        gain = jnp.where(inside, scales_ref[group], gain)
        live = jnp.where(inside, 1.0, live)
        start = start + size
    bins = jnp.zeros((slots, META), jnp.float32)
    for slot in range(slots):
        bins = jnp.where(row == slot, bins_ref[slot].astype(jnp.float32), bins)
    high = gain.astype(jnp.bfloat16).astype(jnp.float32)
    rest = gain - high
    middle = rest.astype(jnp.bfloat16).astype(jnp.float32)
    fields = (high, middle, rest - middle, live, bins)
    meta = jnp.zeros((slots, META), jnp.float32)
    for index, field in enumerate(fields):
        meta = jnp.where(column == index, field, meta)
    out_ref[:, :width] = images_ref[...]
    out_ref[:, width:] = meta.astype(out_ref.dtype)


def pack_rows(particles, group_counts, group_scale, defocus_bin):
    slots, width = particles.shape
    scalar = pl.BlockSpec(memory_space=pltpu.SMEM)
    whole = pl.BlockSpec(memory_space=pltpu.VMEM)
    return pl.pallas_call(
        pack_kernel,
        out_shape=jax.ShapeDtypeStruct((slots, width + META), particles.dtype),
        in_specs=[scalar, scalar, scalar, whole],
        out_specs=whole,
    )(group_counts, group_scale, defocus_bin, particles)


def shift_gather(value, axis, size):
    pieces = [value] + [
        lax.ppermute(value, axis, [(i, (i + k) % size) for i in range(size)])
        for k in range(1, size)
    ]
    return jnp.concatenate(pieces, axis=0)


def xor_butterfly(stats, axis, size):
    step = 1
    while step < size:
        other = lax.ppermute(stats, axis, [(i, i ^ step) for i in range(size)])
        stats = jnp.stack(combine_stats(stats, other))
        step *= 2
    return stats


def accumulate(pieces, scores, gain_rows, ctf_rows, live_mask, peak_score, totals):
    weights = (
        jnp.exp(scores - peak_score[:, None, None])
        / totals[:, None, None]
        * live_mask[:, None, None]
    )
    scaled = (weights * gain_rows[:, None, None]).astype(jnp.bfloat16)
    numerator = None
    start = 0
    for shifted in pieces:
        count = shifted.shape[0] // scaled.shape[1]
        part = lax.dot_general(
            scaled[start : start + count].reshape(shifted.shape[0], -1),
            shifted,
            (((0,), (0,)), ((), ())),
            preferred_element_type=jnp.float32,
        )
        numerator = part if numerator is None else numerator + part
        start += count
    summed = jnp.sum(weights, axis=1) * (gain_rows * gain_rows)[:, None]
    denominator = lax.dot_general(
        summed, ctf_rows * ctf_rows, (((0,), (0,)), ((), ())), precision=HIGHEST
    )
    return (numerator, denominator)


def block_rows(images, gains, bins, norms, ref_tile, ctf_table, cosine_table, sine_table):
    bin_rows = bin_matrix(bins)
    ctf_rows = jnp.dot(bin_rows, ctf_table, precision=HIGHEST)
    shifted = shifted_rows(images, ctf_rows, cosine_table, sine_table)
    scores = tile_scores(shifted, ref_tile, norms, gains, bin_rows)
    return (shifted, scores, ctf_rows)


def per_device(
    particles, references, ctf_table, spectral_reg, defocus_bin, group_counts, group_scale,
    *, n_blk, n_cls,
):
    cosine_table, sine_table = phase_tables()
    ctf_square = ctf_table * ctf_table
    batch_size, width = particles.shape
    ref_tile = references[0]
    own_norms = tile_norms(ref_tile, ctf_square)
    classes_here = ref_tile.shape[0]
    shifts_count = cosine_table.shape[0]

    small = n_blk <= 4
    tables = (ref_tile, ctf_table, cosine_table, sine_table)
    if small:
        packed = pack_rows(particles, group_counts, group_scale, defocus_bin)
        others = shift_gather(packed, "blk", n_blk)[batch_size:]
        groups = []
        for rows in (packed, others):
            meta = rows[:, width : width + 5].astype(jnp.float32)
            gains = (meta[:, 0] + meta[:, 1]) + meta[:, 2]
            groups.append((rows[:, :width], gains, meta[:, 3], meta[:, 4]))
        live_mask = groups[0][2]
    else:
        gain_rows, live_mask = slot_weights(
            group_counts.reshape(1, -1), group_scale.reshape(1, -1), batch_size
        )
        groups = [(
            lax.all_gather(particles, "blk", axis=0, tiled=True),
            lax.all_gather(gain_rows, "blk", axis=0, tiled=True),
            lax.all_gather(live_mask, "blk", axis=0, tiled=True),
            lax.all_gather(defocus_bin.astype(jnp.float32), "blk", axis=0, tiled=True),
        )]
    results = [block_rows(images, gains, bins, own_norms, *tables) for images, gains, _, bins in groups]
    pieces = [shifted for shifted, _, _ in results]
    all_scores = jnp.concatenate([scores for _, scores, _ in results], axis=0)
    ctf_rows = jnp.concatenate([rows for _, _, rows in results], axis=0)
    gain_all = jnp.concatenate([group[1] for group in groups])
    live_all = jnp.concatenate([group[2] for group in groups])
    whole_count = all_scores.shape[0]
    flattened = all_scores.reshape(whole_count, -1)
    peak_all = jnp.max(flattened, axis=1)
    totals_all = jnp.sum(jnp.exp(flattened - peak_all[:, None]), axis=1)

    if small and n_cls & (n_cls - 1) == 0:
        stats = jnp.stack([peak_all, totals_all]).reshape(2, n_blk, batch_size)
        stats = xor_butterfly(stats, "cls", n_cls)
        parts = [stats] + [
            jnp.roll(lax.ppermute(stats, "blk", [(i, (i + k) % n_blk) for i in range(n_blk)]), k, axis=1)
            for k in range(1, n_blk)
        ]
        parts = jnp.stack(parts)
        peak_all, totals_all = combine_many(parts[:, 0], parts[:, 1])
        peak_all = peak_all.reshape(-1)
        totals_all = totals_all.reshape(-1)
        peak_score = peak_all[:batch_size]
        totals = totals_all[:batch_size]
    else:
        gathered = lax.all_gather(jnp.stack([peak_all, totals_all]), ("blk", "cls"))
        peak_all, totals_all = combine_many(gathered[:, 0], gathered[:, 1])
        if small:
            own_offset = 0
        else:
            own_offset = lax.axis_index("blk") * batch_size
        peak_score = lax.dynamic_slice_in_dim(peak_all, own_offset, batch_size)
        totals = lax.dynamic_slice_in_dim(totals_all, own_offset, batch_size)

    numerator, denominator = accumulate(
        pieces, all_scores, gain_all, ctf_rows, live_all, peak_all, totals_all
    )
    log_evidence = jnp.where(live_mask > 0.5, peak_score + jnp.log(totals), 0.0)
    denominator = (
        jnp.concatenate([denominator, denominator], axis=1)
        + jnp.concatenate([spectral_reg, spectral_reg])[None, :]
    )
    class_average = (numerator / denominator)[None]
    return (class_average, log_evidence)


def solution(mesh):
    placed = (
        P(("groups", "blk"), None),
        P("blk", ("groups", "cls"), None),
        P("groups", None),
        P("groups"),
        P(("groups", "blk")),
        P(("groups", "blk")),
        P(("groups", "blk")),
    )
    body = lambda *args: per_device(*args, n_blk=mesh.shape["blk"], n_cls=mesh.shape["cls"])
    return jax.shard_map(
        body,
        mesh=mesh,
        in_specs=placed,
        out_specs=(P("blk", ("groups", "cls"), None), P(("groups", "blk"))),
        check_vma=False,
    )
```

```python
import math

import jax
import numpy as np
import jax.numpy as jnp
from jax import lax
from jax.experimental import pallas as pl
from jax.experimental.pallas import tpu as pltpu
from jax.sharding import PartitionSpec as P

KX = 32
KY = 64
IMG = 128
SIDE = 4
BINS = 16
META = 128


HIGHEST = lax.Precision.HIGHEST


def phase_tables():
    column = np.arange(KX * KY, dtype=np.int32)
    freq_x = (column % KX).astype(np.float32)
    freq_y = (column // KX - KY // 2).astype(np.float32)
    offsets = np.arange(SIDE, dtype=np.float32) - np.float32((SIDE - 1) / 2.0)
    shift_x = np.tile(offsets, SIDE)
    shift_y = np.repeat(offsets, SIDE)
    phases = np.float32(2.0 * math.pi / IMG) * (
        shift_x[:, None] * freq_x[None, :] + shift_y[:, None] * freq_y[None, :]
    )
    return (jnp.asarray(np.cos(phases)), jnp.asarray(np.sin(phases)))


def bin_matrix(bin_values):
    return (bin_values[:, None] == jnp.arange(BINS, dtype=jnp.float32)[None, :]).astype(jnp.float32)


def slot_weights(group_sizes, scale_rows, slots):
    group_ends = jnp.cumsum(group_sizes, axis=1)
    group_starts = group_ends - group_sizes
    slot_index = jnp.arange(slots, dtype=jnp.int32)
    membership = (
        (slot_index[None, :, None] >= group_starts[:, None, :])
        & (slot_index[None, :, None] < group_ends[:, None, :])
    ).astype(jnp.float32)
    gain_rows = jnp.sum(membership * scale_rows[:, None, :], axis=2)
    live_mask = jnp.sum(membership, axis=2)
    return (gain_rows.reshape(-1), live_mask.reshape(-1))


def shifted_rows(images, ctf_rows, cosine_table, sine_table):
    half_width = ctf_rows.shape[1]
    real_part = images[:, :half_width].astype(jnp.float32)[:, None, :]
    imag_part = images[:, half_width:].astype(jnp.float32)[:, None, :]
    ctf_wide = ctf_rows[:, None, :]
    new_real = (real_part * cosine_table + imag_part * sine_table) * ctf_wide
    new_imag = (imag_part * cosine_table - real_part * sine_table) * ctf_wide
    joined = jnp.concatenate([new_real, new_imag], axis=2).astype(jnp.bfloat16)
    return joined.reshape(images.shape[0] * cosine_table.shape[0], 2 * half_width)


def tile_norms(ref_rows, ctf_square):
    half_width = ctf_square.shape[1]
    values = ref_rows.astype(jnp.float32)
    power_sum = (
        values[:, :half_width] * values[:, :half_width]
        + values[:, half_width:] * values[:, half_width:]
    )
    return lax.dot_general(ctf_square, power_sum, (((1,), (1,)), ((), ())), precision=HIGHEST)


def tile_scores(shifted, ref_rows, norms, gain_rows, bin_rows):
    count_here = gain_rows.shape[0]
    products = lax.dot_general(
        shifted, ref_rows, (((1,), (1,)), ((), ())), preferred_element_type=jnp.float32
    )
    products = products.reshape(count_here, shifted.shape[0] // count_here, ref_rows.shape[0])
    norm_term = jnp.dot(bin_rows, norms, precision=HIGHEST)
    return (
        gain_rows[:, None, None] * products
        - 0.5 * (gain_rows * gain_rows)[:, None, None] * norm_term[:, None, :]
    )


def combine_stats(former, latter):
    new_peak = jnp.maximum(former[0], latter[0])
    return (
        new_peak,
        former[1] * jnp.exp(former[0] - new_peak) + latter[1] * jnp.exp(latter[0] - new_peak),
    )


def combine_many(peaks, totals):
    new_peak = jnp.max(peaks, axis=0)
    return (new_peak, jnp.sum(totals * jnp.exp(peaks - new_peak[None]), axis=0))


def split_exact(value):
    high = lax.reduce_precision(value, exponent_bits=8, mantissa_bits=7)
    rest = value - high
    middle = lax.reduce_precision(rest, exponent_bits=8, mantissa_bits=7)
    return (high, middle, rest - middle)


def pack_kernel(sizes_ref, scales_ref, bins_ref, images_ref, out_ref):
    slots, width = images_ref.shape
    row = lax.broadcasted_iota(jnp.int32, (slots, META), 0)
    column = lax.broadcasted_iota(jnp.int32, (slots, META), 1)
    start = jnp.int32(0)
    gain = jnp.zeros((slots, META), jnp.float32)
    live = jnp.zeros((slots, META), jnp.float32)
    for group in range(sizes_ref.shape[0]):
        size = sizes_ref[group]
        inside = (row >= start) & (row < start + size)
        gain = jnp.where(inside, scales_ref[group], gain)
        live = jnp.where(inside, 1.0, live)
        start = start + size
    bins = jnp.zeros((slots, META), jnp.float32)
    for slot in range(slots):
        bins = jnp.where(row == slot, bins_ref[slot].astype(jnp.float32), bins)
    high = gain.astype(jnp.bfloat16).astype(jnp.float32)
    rest = gain - high
    middle = rest.astype(jnp.bfloat16).astype(jnp.float32)
    fields = (high, middle, rest - middle, live, bins)
    meta = jnp.zeros((slots, META), jnp.float32)
    for index, field in enumerate(fields):
        meta = jnp.where(column == index, field, meta)
    out_ref[:, :width] = images_ref[...]
    out_ref[:, width:] = meta.astype(out_ref.dtype)


def pack_rows(particles, group_counts, group_scale, defocus_bin):
    slots, width = particles.shape
    scalar = pl.BlockSpec(memory_space=pltpu.SMEM)
    whole = pl.BlockSpec(memory_space=pltpu.VMEM)
    return pl.pallas_call(
        pack_kernel,
        out_shape=jax.ShapeDtypeStruct((slots, width + META), particles.dtype),
        in_specs=[scalar, scalar, scalar, whole],
        out_specs=whole,
    )(group_counts, group_scale, defocus_bin, particles)


def xor_gather(value, axis, size):
    pieces = [value] + [
        lax.ppermute(value, axis, [(i, i ^ k) for i in range(size)]) for k in range(1, size)
    ]
    return jnp.concatenate(pieces, axis=0)


def xor_reorder(value, step, axis):
    return jnp.concatenate(
        [lax.slice_in_dim(value, j ^ step, (j ^ step) + 1, axis=axis) for j in range(value.shape[axis])],
        axis=axis,
    )


def xor_butterfly(stats, axis, size):
    step = 1
    while step < size:
        other = lax.ppermute(stats, axis, [(i, i ^ step) for i in range(size)])
        stats = jnp.stack(combine_stats(stats, other))
        step *= 2
    return stats


def accumulate(pieces, scores, gain_rows, ctf_rows, live_mask, peak_score, totals):
    weights = (
        jnp.exp(scores - peak_score[:, None, None])
        / totals[:, None, None]
        * live_mask[:, None, None]
    )
    scaled = (weights * gain_rows[:, None, None]).astype(jnp.bfloat16)
    numerator = None
    start = 0
    for shifted in pieces:
        count = shifted.shape[0] // scaled.shape[1]
        part = lax.dot_general(
            scaled[start : start + count].reshape(shifted.shape[0], -1),
            shifted,
            (((0,), (0,)), ((), ())),
            preferred_element_type=jnp.float32,
        )
        numerator = part if numerator is None else numerator + part
        start += count
    summed = jnp.sum(weights, axis=1) * (gain_rows * gain_rows)[:, None]
    denominator = lax.dot_general(
        summed, ctf_rows * ctf_rows, (((0,), (0,)), ((), ())), precision=HIGHEST
    )
    return (numerator, denominator)


def block_rows(images, gains, bins, norms, ref_tile, ctf_table, cosine_table, sine_table):
    bin_rows = bin_matrix(bins)
    ctf_rows = jnp.dot(bin_rows, ctf_table, precision=HIGHEST)
    shifted = shifted_rows(images, ctf_rows, cosine_table, sine_table)
    scores = tile_scores(shifted, ref_tile, norms, gains, bin_rows)
    return (shifted, scores, ctf_rows)


def per_device(
    particles, references, ctf_table, spectral_reg, defocus_bin, group_counts, group_scale,
    *, n_blk, n_cls,
):
    cosine_table, sine_table = phase_tables()
    ctf_square = ctf_table * ctf_table
    batch_size, width = particles.shape
    ref_tile = references[0]
    own_norms = tile_norms(ref_tile, ctf_square)
    classes_here = ref_tile.shape[0]
    shifts_count = cosine_table.shape[0]

    small = n_blk <= 4 and n_blk & (n_blk - 1) == 0 and n_cls & (n_cls - 1) == 0
    tables = (ref_tile, ctf_table, cosine_table, sine_table)
    if small:
        packed = pack_rows(particles, group_counts, group_scale, defocus_bin)
        others = xor_gather(packed, "blk", n_blk)[batch_size:]
        groups = []
        for rows in (packed, others):
            meta = rows[:, width : width + 5].astype(jnp.float32)
            gains = (meta[:, 0] + meta[:, 1]) + meta[:, 2]
            groups.append((rows[:, :width], gains, meta[:, 3], meta[:, 4]))
        live_mask = groups[0][2]
    else:
        gain_rows, live_mask = slot_weights(
            group_counts.reshape(1, -1), group_scale.reshape(1, -1), batch_size
        )
        groups = [(
            lax.all_gather(particles, "blk", axis=0, tiled=True),
            lax.all_gather(gain_rows, "blk", axis=0, tiled=True),
            lax.all_gather(live_mask, "blk", axis=0, tiled=True),
            lax.all_gather(defocus_bin.astype(jnp.float32), "blk", axis=0, tiled=True),
        )]
    results = [block_rows(images, gains, bins, own_norms, *tables) for images, gains, _, bins in groups]
    pieces = [shifted for shifted, _, _ in results]
    all_scores = jnp.concatenate([scores for _, scores, _ in results], axis=0)
    ctf_rows = jnp.concatenate([rows for _, _, rows in results], axis=0)
    gain_all = jnp.concatenate([group[1] for group in groups])
    live_all = jnp.concatenate([group[2] for group in groups])
    whole_count = all_scores.shape[0]
    flattened = all_scores.reshape(whole_count, -1)
    peak_all = jnp.max(flattened, axis=1)
    totals_all = jnp.sum(jnp.exp(flattened - peak_all[:, None]), axis=1)

    if small:
        stats = jnp.stack([peak_all, totals_all]).reshape(2, n_blk, batch_size)
        stats = xor_butterfly(stats, "cls", n_cls)
        parts = [stats] + [
            xor_reorder(lax.ppermute(stats, "blk", [(i, i ^ k) for i in range(n_blk)]), k, 1)
            for k in range(1, n_blk)
        ]
        parts = jnp.stack(parts)
        peak_all, totals_all = combine_many(parts[:, 0], parts[:, 1])
        peak_all = peak_all.reshape(-1)
        totals_all = totals_all.reshape(-1)
        peak_score = peak_all[:batch_size]
        totals = totals_all[:batch_size]
    else:
        gathered = lax.all_gather(jnp.stack([peak_all, totals_all]), ("blk", "cls"))
        peak_all, totals_all = combine_many(gathered[:, 0], gathered[:, 1])
        own_offset = lax.axis_index("blk") * batch_size
        peak_score = lax.dynamic_slice_in_dim(peak_all, own_offset, batch_size)
        totals = lax.dynamic_slice_in_dim(totals_all, own_offset, batch_size)

    numerator, denominator = accumulate(
        pieces, all_scores, gain_all, ctf_rows, live_all, peak_all, totals_all
    )
    log_evidence = jnp.where(live_mask > 0.5, peak_score + jnp.log(totals), 0.0)
    denominator = (
        jnp.concatenate([denominator, denominator], axis=1)
        + jnp.concatenate([spectral_reg, spectral_reg])[None, :]
    )
    class_average = (numerator / denominator)[None]
    return (class_average, log_evidence)


def solution(mesh):
    placed = (
        P(("groups", "blk"), None),
        P("blk", ("groups", "cls"), None),
        P("groups", None),
        P("groups"),
        P(("groups", "blk")),
        P(("groups", "blk")),
        P(("groups", "blk")),
    )
    body = lambda *args: per_device(*args, n_blk=mesh.shape["blk"], n_cls=mesh.shape["cls"])
    return jax.shard_map(
        body,
        mesh=mesh,
        in_specs=placed,
        out_specs=(P("blk", ("groups", "cls"), None), P(("groups", "blk"))),
        check_vma=False,
    )
```

```python
import math

import jax
import numpy as np
import jax.numpy as jnp
from jax import lax
from jax.experimental import pallas as pl
from jax.experimental.pallas import tpu as pltpu
from jax.sharding import PartitionSpec as P

KX = 32
KY = 64
IMG = 128
SIDE = 4
BINS = 16
META = 128


HIGHEST = lax.Precision.HIGHEST


def phase_tables():
    column = np.arange(KX * KY, dtype=np.int32)
    freq_x = (column % KX).astype(np.float32)
    freq_y = (column // KX - KY // 2).astype(np.float32)
    offsets = np.arange(SIDE, dtype=np.float32) - np.float32((SIDE - 1) / 2.0)
    shift_x = np.tile(offsets, SIDE)
    shift_y = np.repeat(offsets, SIDE)
    phases = np.float32(2.0 * math.pi / IMG) * (
        shift_x[:, None] * freq_x[None, :] + shift_y[:, None] * freq_y[None, :]
    )
    return (jnp.asarray(np.cos(phases)), jnp.asarray(np.sin(phases)))


def bin_matrix(bin_values):
    return (bin_values[:, None] == jnp.arange(BINS, dtype=jnp.float32)[None, :]).astype(jnp.float32)


def slot_weights(group_sizes, scale_rows, slots):
    group_ends = jnp.cumsum(group_sizes, axis=1)
    group_starts = group_ends - group_sizes
    slot_index = jnp.arange(slots, dtype=jnp.int32)
    membership = (
        (slot_index[None, :, None] >= group_starts[:, None, :])
        & (slot_index[None, :, None] < group_ends[:, None, :])
    ).astype(jnp.float32)
    gain_rows = jnp.sum(membership * scale_rows[:, None, :], axis=2)
    live_mask = jnp.sum(membership, axis=2)
    return (gain_rows.reshape(-1), live_mask.reshape(-1))


def shifted_rows(images, ctf_rows, cosine_table, sine_table):
    half_width = ctf_rows.shape[1]
    real_part = images[:, :half_width].astype(jnp.float32)[:, None, :]
    imag_part = images[:, half_width:].astype(jnp.float32)[:, None, :]
    ctf_wide = ctf_rows[:, None, :]
    new_real = (real_part * cosine_table + imag_part * sine_table) * ctf_wide
    new_imag = (imag_part * cosine_table - real_part * sine_table) * ctf_wide
    joined = jnp.concatenate([new_real, new_imag], axis=2).astype(jnp.bfloat16)
    return joined.reshape(images.shape[0] * cosine_table.shape[0], 2 * half_width)


def tile_norms(ref_rows, ctf_square):
    half_width = ctf_square.shape[1]
    values = ref_rows.astype(jnp.float32)
    power_sum = (
        values[:, :half_width] * values[:, :half_width]
        + values[:, half_width:] * values[:, half_width:]
    )
    return lax.dot_general(ctf_square, power_sum, (((1,), (1,)), ((), ())), precision=HIGHEST)


def tile_scores(shifted, ref_rows, norms, gain_rows, bin_rows):
    count_here = gain_rows.shape[0]
    products = lax.dot_general(
        shifted, ref_rows, (((1,), (1,)), ((), ())), preferred_element_type=jnp.float32
    )
    products = products.reshape(count_here, shifted.shape[0] // count_here, ref_rows.shape[0])
    norm_term = jnp.dot(bin_rows, norms, precision=HIGHEST)
    return (
        gain_rows[:, None, None] * products
        - 0.5 * (gain_rows * gain_rows)[:, None, None] * norm_term[:, None, :]
    )


def combine_stats(former, latter):
    new_peak = jnp.maximum(former[0], latter[0])
    return (
        new_peak,
        former[1] * jnp.exp(former[0] - new_peak) + latter[1] * jnp.exp(latter[0] - new_peak),
    )


def combine_many(peaks, totals):
    new_peak = jnp.max(peaks, axis=0)
    return (new_peak, jnp.sum(totals * jnp.exp(peaks - new_peak[None]), axis=0))


def split_exact(value):
    high = lax.reduce_precision(value, exponent_bits=8, mantissa_bits=7)
    rest = value - high
    middle = lax.reduce_precision(rest, exponent_bits=8, mantissa_bits=7)
    return (high, middle, rest - middle)


def pack_kernel(sizes_ref, scales_ref, bins_ref, images_hbm, out_hbm, meta_vmem, copy_sems):
    slots, width = images_hbm.shape
    image_copy = pltpu.make_async_copy(images_hbm, out_hbm.at[:, pl.ds(0, width)], copy_sems.at[0])
    image_copy.start()
    row = lax.broadcasted_iota(jnp.int32, (slots, META), 0)
    column = lax.broadcasted_iota(jnp.int32, (slots, META), 1)
    start = jnp.int32(0)
    gain = jnp.zeros((slots, META), jnp.float32)
    live = jnp.zeros((slots, META), jnp.float32)
    for group in range(sizes_ref.shape[0]):
        size = sizes_ref[group]
        inside = (row >= start) & (row < start + size)
        gain = jnp.where(inside, scales_ref[group], gain)
        live = jnp.where(inside, 1.0, live)
        start = start + size
    bins = jnp.zeros((slots, META), jnp.float32)
    for slot in range(slots):
        bins = jnp.where(row == slot, bins_ref[slot].astype(jnp.float32), bins)
    high = gain.astype(jnp.bfloat16).astype(jnp.float32)
    rest = gain - high
    middle = rest.astype(jnp.bfloat16).astype(jnp.float32)
    fields = (high, middle, rest - middle, live, bins)
    meta = jnp.zeros((slots, META), jnp.float32)
    for index, field in enumerate(fields):
        meta = jnp.where(column == index, field, meta)
    meta_vmem[...] = meta.astype(meta_vmem.dtype)
    meta_copy = pltpu.make_async_copy(meta_vmem, out_hbm.at[:, pl.ds(width, META)], copy_sems.at[1])
    meta_copy.start()
    image_copy.wait()
    meta_copy.wait()


def pack_rows(particles, group_counts, group_scale, defocus_bin):
    slots, width = particles.shape
    scalar = pl.BlockSpec(memory_space=pltpu.SMEM)
    anywhere = pl.BlockSpec(memory_space=pl.ANY)
    return pl.pallas_call(
        pack_kernel,
        out_shape=jax.ShapeDtypeStruct((slots, width + META), particles.dtype),
        in_specs=[scalar, scalar, scalar, anywhere],
        out_specs=anywhere,
        scratch_shapes=[pltpu.VMEM((slots, META), particles.dtype), pltpu.SemaphoreType.DMA((2,))],
    )(group_counts, group_scale, defocus_bin, particles)


def xor_gather(value, axis, size):
    pieces = [value] + [
        lax.ppermute(value, axis, [(i, i ^ k) for i in range(size)]) for k in range(1, size)
    ]
    return jnp.concatenate(pieces, axis=0)


def xor_reorder(value, step, axis):
    return jnp.concatenate(
        [lax.slice_in_dim(value, j ^ step, (j ^ step) + 1, axis=axis) for j in range(value.shape[axis])],
        axis=axis,
    )


def xor_butterfly(stats, axis, size):
    step = 1
    while step < size:
        other = lax.ppermute(stats, axis, [(i, i ^ step) for i in range(size)])
        stats = jnp.stack(combine_stats(stats, other))
        step *= 2
    return stats


def accumulate(pieces, scores, gain_rows, ctf_rows, live_mask, peak_score, totals):
    weights = (
        jnp.exp(scores - peak_score[:, None, None])
        / totals[:, None, None]
        * live_mask[:, None, None]
    )
    scaled = (weights * gain_rows[:, None, None]).astype(jnp.bfloat16)
    numerator = None
    start = 0
    for shifted in pieces:
        count = shifted.shape[0] // scaled.shape[1]
        part = lax.dot_general(
            scaled[start : start + count].reshape(shifted.shape[0], -1),
            shifted,
            (((0,), (0,)), ((), ())),
            preferred_element_type=jnp.float32,
        )
        numerator = part if numerator is None else numerator + part
        start += count
    summed = jnp.sum(weights, axis=1) * (gain_rows * gain_rows)[:, None]
    denominator = lax.dot_general(
        summed, ctf_rows * ctf_rows, (((0,), (0,)), ((), ())), precision=HIGHEST
    )
    return (numerator, denominator)


def block_rows(images, gains, bins, norms, ref_tile, ctf_table, cosine_table, sine_table):
    bin_rows = bin_matrix(bins)
    ctf_rows = jnp.dot(bin_rows, ctf_table, precision=HIGHEST)
    shifted = shifted_rows(images, ctf_rows, cosine_table, sine_table)
    scores = tile_scores(shifted, ref_tile, norms, gains, bin_rows)
    return (shifted, scores, ctf_rows)


def per_device(
    particles, references, ctf_table, spectral_reg, defocus_bin, group_counts, group_scale,
    *, n_blk, n_cls,
):
    cosine_table, sine_table = phase_tables()
    ctf_square = ctf_table * ctf_table
    batch_size, width = particles.shape
    ref_tile = references[0]
    own_norms = tile_norms(ref_tile, ctf_square)
    classes_here = ref_tile.shape[0]
    shifts_count = cosine_table.shape[0]

    small = n_blk <= 4 and n_blk & (n_blk - 1) == 0 and n_cls & (n_cls - 1) == 0
    tables = (ref_tile, ctf_table, cosine_table, sine_table)
    if small:
        packed = pack_rows(particles, group_counts, group_scale, defocus_bin)
        others = xor_gather(packed, "blk", n_blk)[batch_size:]
        groups = []
        for rows in (packed, others):
            meta = rows[:, width : width + 5].astype(jnp.float32)
            gains = (meta[:, 0] + meta[:, 1]) + meta[:, 2]
            groups.append((rows[:, :width], gains, meta[:, 3], meta[:, 4]))
        live_mask = groups[0][2]
    else:
        gain_rows, live_mask = slot_weights(
            group_counts.reshape(1, -1), group_scale.reshape(1, -1), batch_size
        )
        groups = [(
            lax.all_gather(particles, "blk", axis=0, tiled=True),
            lax.all_gather(gain_rows, "blk", axis=0, tiled=True),
            lax.all_gather(live_mask, "blk", axis=0, tiled=True),
            lax.all_gather(defocus_bin.astype(jnp.float32), "blk", axis=0, tiled=True),
        )]
    results = [block_rows(images, gains, bins, own_norms, *tables) for images, gains, _, bins in groups]
    pieces = [shifted for shifted, _, _ in results]
    all_scores = jnp.concatenate([scores for _, scores, _ in results], axis=0)
    ctf_rows = jnp.concatenate([rows for _, _, rows in results], axis=0)
    gain_all = jnp.concatenate([group[1] for group in groups])
    live_all = jnp.concatenate([group[2] for group in groups])
    whole_count = all_scores.shape[0]
    flattened = all_scores.reshape(whole_count, -1)
    peak_all = jnp.max(flattened, axis=1)
    totals_all = jnp.sum(jnp.exp(flattened - peak_all[:, None]), axis=1)

    if small:
        stats = jnp.stack([peak_all, totals_all]).reshape(2, n_blk, batch_size)
        stats = xor_butterfly(stats, "cls", n_cls)
        parts = [stats] + [
            xor_reorder(lax.ppermute(stats, "blk", [(i, i ^ k) for i in range(n_blk)]), k, 1)
            for k in range(1, n_blk)
        ]
        parts = jnp.stack(parts)
        peak_all, totals_all = combine_many(parts[:, 0], parts[:, 1])
        peak_all = peak_all.reshape(-1)
        totals_all = totals_all.reshape(-1)
        peak_score = peak_all[:batch_size]
        totals = totals_all[:batch_size]
    else:
        gathered = lax.all_gather(jnp.stack([peak_all, totals_all]), ("blk", "cls"))
        peak_all, totals_all = combine_many(gathered[:, 0], gathered[:, 1])
        own_offset = lax.axis_index("blk") * batch_size
        peak_score = lax.dynamic_slice_in_dim(peak_all, own_offset, batch_size)
        totals = lax.dynamic_slice_in_dim(totals_all, own_offset, batch_size)

    numerator, denominator = accumulate(
        pieces, all_scores, gain_all, ctf_rows, live_all, peak_all, totals_all
    )
    log_evidence = jnp.where(live_mask > 0.5, peak_score + jnp.log(totals), 0.0)
    denominator = (
        jnp.concatenate([denominator, denominator], axis=1)
        + jnp.concatenate([spectral_reg, spectral_reg])[None, :]
    )
    class_average = (numerator / denominator)[None]
    return (class_average, log_evidence)


def solution(mesh):
    placed = (
        P(("groups", "blk"), None),
        P("blk", ("groups", "cls"), None),
        P("groups", None),
        P("groups"),
        P(("groups", "blk")),
        P(("groups", "blk")),
        P(("groups", "blk")),
    )
    body = lambda *args: per_device(*args, n_blk=mesh.shape["blk"], n_cls=mesh.shape["cls"])
    return jax.shard_map(
        body,
        mesh=mesh,
        in_specs=placed,
        out_specs=(P("blk", ("groups", "cls"), None), P(("groups", "blk"))),
        check_vma=False,
    )
```

```python
import math

import jax
import numpy as np
import jax.numpy as jnp
from jax import lax
from jax.experimental import pallas as pl
from jax.experimental.pallas import tpu as pltpu
from jax.sharding import PartitionSpec as P

KX = 32
KY = 64
IMG = 128
SIDE = 4
BINS = 16
META = 128


HIGHEST = lax.Precision.HIGHEST


def phase_tables():
    column = np.arange(KX * KY, dtype=np.int32)
    freq_x = (column % KX).astype(np.float32)
    freq_y = (column // KX - KY // 2).astype(np.float32)
    offsets = np.arange(SIDE, dtype=np.float32) - np.float32((SIDE - 1) / 2.0)
    shift_x = np.tile(offsets, SIDE)
    shift_y = np.repeat(offsets, SIDE)
    phases = np.float32(2.0 * math.pi / IMG) * (
        shift_x[:, None] * freq_x[None, :] + shift_y[:, None] * freq_y[None, :]
    )
    return (jnp.asarray(np.cos(phases)), jnp.asarray(np.sin(phases)))


def bin_matrix(bin_values):
    return (bin_values[:, None] == jnp.arange(BINS, dtype=jnp.float32)[None, :]).astype(jnp.float32)


def slot_weights(group_sizes, scale_rows, slots):
    group_ends = jnp.cumsum(group_sizes, axis=1)
    group_starts = group_ends - group_sizes
    slot_index = jnp.arange(slots, dtype=jnp.int32)
    membership = (
        (slot_index[None, :, None] >= group_starts[:, None, :])
        & (slot_index[None, :, None] < group_ends[:, None, :])
    ).astype(jnp.float32)
    gain_rows = jnp.sum(membership * scale_rows[:, None, :], axis=2)
    live_mask = jnp.sum(membership, axis=2)
    return (gain_rows.reshape(-1), live_mask.reshape(-1))


def shifted_rows(images, ctf_rows, cosine_table, sine_table):
    half_width = ctf_rows.shape[1]
    real_part = images[:, :half_width].astype(jnp.float32)[:, None, :]
    imag_part = images[:, half_width:].astype(jnp.float32)[:, None, :]
    ctf_wide = ctf_rows[:, None, :]
    new_real = (real_part * cosine_table + imag_part * sine_table) * ctf_wide
    new_imag = (imag_part * cosine_table - real_part * sine_table) * ctf_wide
    joined = jnp.concatenate([new_real, new_imag], axis=2).astype(jnp.bfloat16)
    return joined.reshape(images.shape[0] * cosine_table.shape[0], 2 * half_width)


def tile_norms(ref_rows, ctf_square):
    half_width = ctf_square.shape[1]
    values = ref_rows.astype(jnp.float32)
    power_sum = (
        values[:, :half_width] * values[:, :half_width]
        + values[:, half_width:] * values[:, half_width:]
    )
    return lax.dot_general(ctf_square, power_sum, (((1,), (1,)), ((), ())), precision=HIGHEST)


def tile_scores(shifted, ref_rows, norms, gain_rows, bin_rows):
    count_here = gain_rows.shape[0]
    products = lax.dot_general(
        shifted, ref_rows, (((1,), (1,)), ((), ())), preferred_element_type=jnp.float32
    )
    products = products.reshape(count_here, shifted.shape[0] // count_here, ref_rows.shape[0])
    norm_term = jnp.dot(bin_rows, norms, precision=HIGHEST)
    return (
        gain_rows[:, None, None] * products
        - 0.5 * (gain_rows * gain_rows)[:, None, None] * norm_term[:, None, :]
    )


def combine_stats(former, latter):
    new_peak = jnp.maximum(former[0], latter[0])
    return (
        new_peak,
        former[1] * jnp.exp(former[0] - new_peak) + latter[1] * jnp.exp(latter[0] - new_peak),
    )


def combine_many(peaks, totals):
    new_peak = jnp.max(peaks, axis=0)
    return (new_peak, jnp.sum(totals * jnp.exp(peaks - new_peak[None]), axis=0))


def split_exact(value):
    high = lax.reduce_precision(value, exponent_bits=8, mantissa_bits=7)
    rest = value - high
    middle = lax.reduce_precision(rest, exponent_bits=8, mantissa_bits=7)
    return (high, middle, rest - middle)


def pack_kernel(sizes_ref, scales_ref, bins_ref, images_ref, out_ref):
    slots, width = images_ref.shape
    row = lax.broadcasted_iota(jnp.int32, (slots, META), 0)
    column = lax.broadcasted_iota(jnp.int32, (slots, META), 1)
    start = jnp.int32(0)
    gain = jnp.zeros((slots, META), jnp.float32)
    live = jnp.zeros((slots, META), jnp.float32)
    for group in range(sizes_ref.shape[0]):
        size = sizes_ref[group]
        inside = (row >= start) & (row < start + size)
        gain = jnp.where(inside, scales_ref[group], gain)
        live = jnp.where(inside, 1.0, live)
        start = start + size
    bins = jnp.zeros((slots, META), jnp.float32)
    for slot in range(slots):
        bins = jnp.where(row == slot, bins_ref[slot].astype(jnp.float32), bins)
    high = gain.astype(jnp.bfloat16).astype(jnp.float32)
    rest = gain - high
    middle = rest.astype(jnp.bfloat16).astype(jnp.float32)
    fields = (high, middle, rest - middle, live, bins)
    meta = jnp.zeros((slots, META), jnp.float32)
    for index, field in enumerate(fields):
        meta = jnp.where(column == index, field, meta)
    out_ref[:, :width] = images_ref[...]
    out_ref[:, width:] = meta.astype(out_ref.dtype)


def pack_rows(particles, group_counts, group_scale, defocus_bin):
    slots, width = particles.shape
    scalar = pl.BlockSpec(memory_space=pltpu.SMEM)
    whole = pl.BlockSpec(memory_space=pltpu.VMEM)
    return pl.pallas_call(
        pack_kernel,
        out_shape=jax.ShapeDtypeStruct((slots, width + META), particles.dtype),
        in_specs=[scalar, scalar, scalar, whole],
        out_specs=whole,
    )(group_counts, group_scale, defocus_bin, particles)


def xor_gather(value, axis, size):
    pieces = [value] + [
        lax.ppermute(value, axis, [(i, i ^ k) for i in range(size)]) for k in range(1, size)
    ]
    return jnp.concatenate(pieces, axis=0)


def xor_reorder(value, step, axis):
    return jnp.concatenate(
        [lax.slice_in_dim(value, j ^ step, (j ^ step) + 1, axis=axis) for j in range(value.shape[axis])],
        axis=axis,
    )


def xor_butterfly(stats, axis, size):
    step = 1
    while step < size:
        other = lax.ppermute(stats, axis, [(i, i ^ step) for i in range(size)])
        stats = jnp.stack(combine_stats(stats, other))
        step *= 2
    return stats


def accumulate(pieces, scores, gain_rows, ctf_rows, live_mask, peak_score, totals):
    weights = (
        jnp.exp(scores - peak_score[:, None, None])
        / totals[:, None, None]
        * live_mask[:, None, None]
    )
    scaled = (weights * gain_rows[:, None, None]).astype(jnp.bfloat16)
    numerator = None
    start = 0
    for shifted in pieces:
        count = shifted.shape[0] // scaled.shape[1]
        part = lax.dot_general(
            scaled[start : start + count].reshape(shifted.shape[0], -1),
            shifted,
            (((0,), (0,)), ((), ())),
            preferred_element_type=jnp.float32,
        )
        numerator = part if numerator is None else numerator + part
        start += count
    summed = jnp.sum(weights, axis=1) * (gain_rows * gain_rows)[:, None]
    denominator = lax.dot_general(
        summed, ctf_rows * ctf_rows, (((0,), (0,)), ((), ())), precision=HIGHEST
    )
    return (numerator, denominator)


def block_rows(images, gains, bins, norms, ref_tile, ctf_table, cosine_table, sine_table):
    bin_rows = bin_matrix(bins)
    ctf_rows = jnp.dot(bin_rows, ctf_table, precision=HIGHEST)
    shifted = shifted_rows(images, ctf_rows, cosine_table, sine_table)
    scores = tile_scores(shifted, ref_tile, norms, gains, bin_rows)
    return (shifted, scores, ctf_rows)


def per_device(
    particles, references, ctf_table, spectral_reg, defocus_bin, group_counts, group_scale,
    *, n_blk, n_cls,
):
    cosine_table, sine_table = phase_tables()
    ctf_square = ctf_table * ctf_table
    batch_size, width = particles.shape
    ref_tile = references[0]
    own_norms = tile_norms(ref_tile, ctf_square)
    classes_here = ref_tile.shape[0]
    shifts_count = cosine_table.shape[0]

    small = n_blk <= 4 and n_blk & (n_blk - 1) == 0 and n_cls & (n_cls - 1) == 0
    tables = (ref_tile, ctf_table, cosine_table, sine_table)
    if small:
        packed = pack_rows(particles, group_counts, group_scale, defocus_bin)
        others = xor_gather(packed, "blk", n_blk)[batch_size:]
        own_rows = lax.optimization_barrier(packed.astype(jnp.float32))
        groups = []
        for rows in (own_rows, others):
            meta = rows[:, width : width + 5].astype(jnp.float32)
            gains = (meta[:, 0] + meta[:, 1]) + meta[:, 2]
            groups.append((rows[:, :width], gains, meta[:, 3], meta[:, 4]))
        live_mask = groups[0][2]
    else:
        gain_rows, live_mask = slot_weights(
            group_counts.reshape(1, -1), group_scale.reshape(1, -1), batch_size
        )
        groups = [(
            lax.all_gather(particles, "blk", axis=0, tiled=True),
            lax.all_gather(gain_rows, "blk", axis=0, tiled=True),
            lax.all_gather(live_mask, "blk", axis=0, tiled=True),
            lax.all_gather(defocus_bin.astype(jnp.float32), "blk", axis=0, tiled=True),
        )]
    results = [block_rows(images, gains, bins, own_norms, *tables) for images, gains, _, bins in groups]
    pieces = [shifted for shifted, _, _ in results]
    all_scores = jnp.concatenate([scores for _, scores, _ in results], axis=0)
    ctf_rows = jnp.concatenate([rows for _, _, rows in results], axis=0)
    gain_all = jnp.concatenate([group[1] for group in groups])
    live_all = jnp.concatenate([group[2] for group in groups])
    whole_count = all_scores.shape[0]
    flattened = all_scores.reshape(whole_count, -1)
    peak_all = jnp.max(flattened, axis=1)
    totals_all = jnp.sum(jnp.exp(flattened - peak_all[:, None]), axis=1)

    if small:
        stats = jnp.stack([peak_all, totals_all]).reshape(2, n_blk, batch_size)
        stats = xor_butterfly(stats, "cls", n_cls)
        parts = [stats] + [
            xor_reorder(lax.ppermute(stats, "blk", [(i, i ^ k) for i in range(n_blk)]), k, 1)
            for k in range(1, n_blk)
        ]
        parts = jnp.stack(parts)
        peak_all, totals_all = combine_many(parts[:, 0], parts[:, 1])
        peak_all = peak_all.reshape(-1)
        totals_all = totals_all.reshape(-1)
        peak_score = peak_all[:batch_size]
        totals = totals_all[:batch_size]
    else:
        gathered = lax.all_gather(jnp.stack([peak_all, totals_all]), ("blk", "cls"))
        peak_all, totals_all = combine_many(gathered[:, 0], gathered[:, 1])
        own_offset = lax.axis_index("blk") * batch_size
        peak_score = lax.dynamic_slice_in_dim(peak_all, own_offset, batch_size)
        totals = lax.dynamic_slice_in_dim(totals_all, own_offset, batch_size)

    numerator, denominator = accumulate(
        pieces, all_scores, gain_all, ctf_rows, live_all, peak_all, totals_all
    )
    log_evidence = jnp.where(live_mask > 0.5, peak_score + jnp.log(totals), 0.0)
    denominator = (
        jnp.concatenate([denominator, denominator], axis=1)
        + jnp.concatenate([spectral_reg, spectral_reg])[None, :]
    )
    class_average = (numerator / denominator)[None]
    return (class_average, log_evidence)


def solution(mesh):
    placed = (
        P(("groups", "blk"), None),
        P("blk", ("groups", "cls"), None),
        P("groups", None),
        P("groups"),
        P(("groups", "blk")),
        P(("groups", "blk")),
        P(("groups", "blk")),
    )
    body = lambda *args: per_device(*args, n_blk=mesh.shape["blk"], n_cls=mesh.shape["cls"])
    return jax.shard_map(
        body,
        mesh=mesh,
        in_specs=placed,
        out_specs=(P("blk", ("groups", "cls"), None), P(("groups", "blk"))),
        check_vma=False,
    )
```

```python
import math

import jax
import numpy as np
import jax.numpy as jnp
from jax import lax
from jax.experimental import pallas as pl
from jax.experimental.pallas import tpu as pltpu
from jax.sharding import PartitionSpec as P

KX = 32
KY = 64
IMG = 128
SIDE = 4
BINS = 16
META = 128


HIGHEST = lax.Precision.HIGHEST


def phase_tables():
    column = np.arange(KX * KY, dtype=np.int32)
    freq_x = (column % KX).astype(np.float32)
    freq_y = (column // KX - KY // 2).astype(np.float32)
    offsets = np.arange(SIDE, dtype=np.float32) - np.float32((SIDE - 1) / 2.0)
    shift_x = np.tile(offsets, SIDE)
    shift_y = np.repeat(offsets, SIDE)
    phases = np.float32(2.0 * math.pi / IMG) * (
        shift_x[:, None] * freq_x[None, :] + shift_y[:, None] * freq_y[None, :]
    )
    return (jnp.asarray(np.cos(phases)), jnp.asarray(np.sin(phases)))


def bin_matrix(bin_values):
    return (bin_values[:, None] == jnp.arange(BINS, dtype=jnp.float32)[None, :]).astype(jnp.float32)


def slot_weights(group_sizes, scale_rows, slots):
    group_ends = jnp.cumsum(group_sizes, axis=1)
    group_starts = group_ends - group_sizes
    slot_index = jnp.arange(slots, dtype=jnp.int32)
    membership = (
        (slot_index[None, :, None] >= group_starts[:, None, :])
        & (slot_index[None, :, None] < group_ends[:, None, :])
    ).astype(jnp.float32)
    gain_rows = jnp.sum(membership * scale_rows[:, None, :], axis=2)
    live_mask = jnp.sum(membership, axis=2)
    return (gain_rows.reshape(-1), live_mask.reshape(-1))


def shifted_rows(images, ctf_rows, cosine_table, sine_table):
    half_width = ctf_rows.shape[1]
    real_part = images[:, :half_width].astype(jnp.float32)[:, None, :]
    imag_part = images[:, half_width:].astype(jnp.float32)[:, None, :]
    ctf_wide = ctf_rows[:, None, :]
    new_real = (real_part * cosine_table + imag_part * sine_table) * ctf_wide
    new_imag = (imag_part * cosine_table - real_part * sine_table) * ctf_wide
    joined = jnp.concatenate([new_real, new_imag], axis=2).astype(jnp.bfloat16)
    return joined.reshape(images.shape[0] * cosine_table.shape[0], 2 * half_width)


def tile_norms(ref_rows, ctf_square):
    half_width = ctf_square.shape[1]
    values = ref_rows.astype(jnp.float32)
    power_sum = (
        values[:, :half_width] * values[:, :half_width]
        + values[:, half_width:] * values[:, half_width:]
    )
    return lax.dot_general(ctf_square, power_sum, (((1,), (1,)), ((), ())), precision=HIGHEST)


def tile_scores(shifted, ref_rows, norms, gain_rows, bin_rows):
    count_here = gain_rows.shape[0]
    products = lax.dot_general(
        shifted, ref_rows, (((1,), (1,)), ((), ())), preferred_element_type=jnp.float32
    )
    products = products.reshape(count_here, shifted.shape[0] // count_here, ref_rows.shape[0])
    norm_term = jnp.dot(bin_rows, norms, precision=HIGHEST)
    return (
        gain_rows[:, None, None] * products
        - 0.5 * (gain_rows * gain_rows)[:, None, None] * norm_term[:, None, :]
    )


def combine_stats(former, latter):
    new_peak = jnp.maximum(former[0], latter[0])
    return (
        new_peak,
        former[1] * jnp.exp(former[0] - new_peak) + latter[1] * jnp.exp(latter[0] - new_peak),
    )


def combine_many(peaks, totals):
    new_peak = jnp.max(peaks, axis=0)
    return (new_peak, jnp.sum(totals * jnp.exp(peaks - new_peak[None]), axis=0))


def split_exact(value):
    high = lax.reduce_precision(value, exponent_bits=8, mantissa_bits=7)
    rest = value - high
    middle = lax.reduce_precision(rest, exponent_bits=8, mantissa_bits=7)
    return (high, middle, rest - middle)


def pack_kernel(sizes_ref, scales_ref, bins_ref, images_ref, out_ref):
    slots, width = images_ref.shape
    row = lax.broadcasted_iota(jnp.int32, (slots, META), 0)
    column = lax.broadcasted_iota(jnp.int32, (slots, META), 1)
    start = jnp.int32(0)
    gain = jnp.zeros((slots, META), jnp.float32)
    live = jnp.zeros((slots, META), jnp.float32)
    for group in range(sizes_ref.shape[0]):
        size = sizes_ref[group]
        inside = (row >= start) & (row < start + size)
        gain = jnp.where(inside, scales_ref[group], gain)
        live = jnp.where(inside, 1.0, live)
        start = start + size
    bins = jnp.zeros((slots, META), jnp.float32)
    for slot in range(slots):
        bins = jnp.where(row == slot, bins_ref[slot].astype(jnp.float32), bins)
    high = gain.astype(jnp.bfloat16).astype(jnp.float32)
    rest = gain - high
    middle = rest.astype(jnp.bfloat16).astype(jnp.float32)
    fields = (high, middle, rest - middle, live, bins)
    meta = jnp.zeros((slots, META), jnp.float32)
    for index, field in enumerate(fields):
        meta = jnp.where(column == index, field, meta)
    out_ref[:, :width] = images_ref[...]
    out_ref[:, width:] = meta.astype(out_ref.dtype)


def pack_rows(particles, group_counts, group_scale, defocus_bin):
    slots, width = particles.shape
    scalar = pl.BlockSpec(memory_space=pltpu.SMEM)
    whole = pl.BlockSpec(memory_space=pltpu.VMEM)
    return pl.pallas_call(
        pack_kernel,
        out_shape=jax.ShapeDtypeStruct((slots, width + META), particles.dtype),
        in_specs=[scalar, scalar, scalar, whole],
        out_specs=whole,
    )(group_counts, group_scale, defocus_bin, particles)


def xor_gather_pieces(value, axis, size):
    return [value] + [
        lax.ppermute(value, axis, [(i, i ^ k) for i in range(size)]) for k in range(1, size)
    ]


def xor_reorder(value, step, axis):
    return jnp.concatenate(
        [lax.slice_in_dim(value, j ^ step, (j ^ step) + 1, axis=axis) for j in range(value.shape[axis])],
        axis=axis,
    )


def xor_butterfly(stats, axis, size):
    step = 1
    while step < size:
        other = lax.ppermute(stats, axis, [(i, i ^ step) for i in range(size)])
        stats = jnp.stack(combine_stats(stats, other))
        step *= 2
    return stats


def accumulate(pieces, scores, gain_rows, ctf_rows, live_mask, peak_score, totals):
    weights = (
        jnp.exp(scores - peak_score[:, None, None])
        / totals[:, None, None]
        * live_mask[:, None, None]
    )
    scaled = (weights * gain_rows[:, None, None]).astype(jnp.bfloat16)
    numerator = None
    start = 0
    for shifted in pieces:
        count = shifted.shape[0] // scaled.shape[1]
        part = lax.dot_general(
            scaled[start : start + count].reshape(shifted.shape[0], -1),
            shifted,
            (((0,), (0,)), ((), ())),
            preferred_element_type=jnp.float32,
        )
        numerator = part if numerator is None else numerator + part
        start += count
    summed = jnp.sum(weights, axis=1) * (gain_rows * gain_rows)[:, None]
    denominator = lax.dot_general(
        summed, ctf_rows * ctf_rows, (((0,), (0,)), ((), ())), precision=HIGHEST
    )
    return (numerator, denominator)


def block_rows(images, gains, bins, norms, ref_tile, ctf_table, cosine_table, sine_table):
    bin_rows = bin_matrix(bins)
    ctf_rows = jnp.dot(bin_rows, ctf_table, precision=HIGHEST)
    shifted = shifted_rows(images, ctf_rows, cosine_table, sine_table)
    scores = tile_scores(shifted, ref_tile, norms, gains, bin_rows)
    return (shifted, scores, ctf_rows)


def per_device(
    particles, references, ctf_table, spectral_reg, defocus_bin, group_counts, group_scale,
    *, n_blk, n_cls,
):
    cosine_table, sine_table = phase_tables()
    ctf_square = ctf_table * ctf_table
    batch_size, width = particles.shape
    ref_tile = references[0]
    own_norms = tile_norms(ref_tile, ctf_square)
    classes_here = ref_tile.shape[0]
    shifts_count = cosine_table.shape[0]

    small = n_blk <= 4 and n_blk & (n_blk - 1) == 0 and n_cls & (n_cls - 1) == 0
    tables = (ref_tile, ctf_table, cosine_table, sine_table)
    if small:
        packed = pack_rows(particles, group_counts, group_scale, defocus_bin)
        pieces = xor_gather_pieces(packed, "blk", n_blk)
        others = [pieces[1]] + ([jnp.concatenate(pieces[2:], axis=0)] if n_blk > 2 else [])
        own_rows = lax.optimization_barrier(packed.astype(jnp.float32))
        raw_groups = [own_rows, *others]
    else:
        gain_rows, live_mask = slot_weights(
            group_counts.reshape(1, -1), group_scale.reshape(1, -1), batch_size
        )
        raw_groups = []
        groups = [(
            lax.all_gather(particles, "blk", axis=0, tiled=True),
            lax.all_gather(gain_rows, "blk", axis=0, tiled=True),
            lax.all_gather(live_mask, "blk", axis=0, tiled=True),
            lax.all_gather(defocus_bin.astype(jnp.float32), "blk", axis=0, tiled=True),
        )]
    results = []
    if small:
        groups = []
        for rows in raw_groups:
            if results:
                rows, _ = lax.optimization_barrier((rows, results[-1][1]))
            meta = rows[:, width : width + 5].astype(jnp.float32)
            gains = (meta[:, 0] + meta[:, 1]) + meta[:, 2]
            groups.append((rows[:, :width], gains, meta[:, 3], meta[:, 4]))
            results.append(block_rows(rows[:, :width], gains, meta[:, 4], own_norms, *tables))
        live_mask = groups[0][2]
    else:
        results = [block_rows(images, gains, bins, own_norms, *tables) for images, gains, _, bins in groups]
    pieces = [shifted for shifted, _, _ in results]
    all_scores = jnp.concatenate([scores for _, scores, _ in results], axis=0)
    ctf_rows = jnp.concatenate([rows for _, _, rows in results], axis=0)
    gain_all = jnp.concatenate([group[1] for group in groups])
    live_all = jnp.concatenate([group[2] for group in groups])
    whole_count = all_scores.shape[0]
    flattened = all_scores.reshape(whole_count, -1)
    peak_all = jnp.max(flattened, axis=1)
    totals_all = jnp.sum(jnp.exp(flattened - peak_all[:, None]), axis=1)

    if small:
        stats = jnp.stack([peak_all, totals_all]).reshape(2, n_blk, batch_size)
        stats = xor_butterfly(stats, "cls", n_cls)
        parts = [stats] + [
            xor_reorder(lax.ppermute(stats, "blk", [(i, i ^ k) for i in range(n_blk)]), k, 1)
            for k in range(1, n_blk)
        ]
        parts = jnp.stack(parts)
        peak_all, totals_all = combine_many(parts[:, 0], parts[:, 1])
        peak_all = peak_all.reshape(-1)
        totals_all = totals_all.reshape(-1)
        peak_score = peak_all[:batch_size]
        totals = totals_all[:batch_size]
    else:
        gathered = lax.all_gather(jnp.stack([peak_all, totals_all]), ("blk", "cls"))
        peak_all, totals_all = combine_many(gathered[:, 0], gathered[:, 1])
        own_offset = lax.axis_index("blk") * batch_size
        peak_score = lax.dynamic_slice_in_dim(peak_all, own_offset, batch_size)
        totals = lax.dynamic_slice_in_dim(totals_all, own_offset, batch_size)

    numerator, denominator = accumulate(
        pieces, all_scores, gain_all, ctf_rows, live_all, peak_all, totals_all
    )
    log_evidence = jnp.where(live_mask > 0.5, peak_score + jnp.log(totals), 0.0)
    denominator = (
        jnp.concatenate([denominator, denominator], axis=1)
        + jnp.concatenate([spectral_reg, spectral_reg])[None, :]
    )
    class_average = (numerator / denominator)[None]
    return (class_average, log_evidence)


def solution(mesh):
    placed = (
        P(("groups", "blk"), None),
        P("blk", ("groups", "cls"), None),
        P("groups", None),
        P("groups"),
        P(("groups", "blk")),
        P(("groups", "blk")),
        P(("groups", "blk")),
    )
    body = lambda *args: per_device(*args, n_blk=mesh.shape["blk"], n_cls=mesh.shape["cls"])
    return jax.shard_map(
        body,
        mesh=mesh,
        in_specs=placed,
        out_specs=(P("blk", ("groups", "cls"), None), P(("groups", "blk"))),
        check_vma=False,
    )
```

```python
import math

import jax
import numpy as np
import jax.numpy as jnp
from jax import lax
from jax.experimental import pallas as pl
from jax.experimental.pallas import tpu as pltpu
from jax.sharding import PartitionSpec as P

KX = 32
KY = 64
IMG = 128
SIDE = 4
BINS = 16
META = 128


HIGHEST = lax.Precision.HIGHEST


def phase_tables():
    column = np.arange(KX * KY, dtype=np.int32)
    freq_x = (column % KX).astype(np.float32)
    freq_y = (column // KX - KY // 2).astype(np.float32)
    offsets = np.arange(SIDE, dtype=np.float32) - np.float32((SIDE - 1) / 2.0)
    shift_x = np.tile(offsets, SIDE)
    shift_y = np.repeat(offsets, SIDE)
    phases = np.float32(2.0 * math.pi / IMG) * (
        shift_x[:, None] * freq_x[None, :] + shift_y[:, None] * freq_y[None, :]
    )
    return (jnp.asarray(np.cos(phases)), jnp.asarray(np.sin(phases)))


def bin_matrix(bin_values):
    return (bin_values[:, None] == jnp.arange(BINS, dtype=jnp.float32)[None, :]).astype(jnp.float32)


def slot_weights(group_sizes, scale_rows, slots):
    group_ends = jnp.cumsum(group_sizes, axis=1)
    group_starts = group_ends - group_sizes
    slot_index = jnp.arange(slots, dtype=jnp.int32)
    membership = (
        (slot_index[None, :, None] >= group_starts[:, None, :])
        & (slot_index[None, :, None] < group_ends[:, None, :])
    ).astype(jnp.float32)
    gain_rows = jnp.sum(membership * scale_rows[:, None, :], axis=2)
    live_mask = jnp.sum(membership, axis=2)
    return (gain_rows.reshape(-1), live_mask.reshape(-1))


def shifted_rows(images, ctf_rows, cosine_table, sine_table):
    half_width = ctf_rows.shape[1]
    real_part = images[:, :half_width].astype(jnp.float32)[:, None, :]
    imag_part = images[:, half_width:].astype(jnp.float32)[:, None, :]
    ctf_wide = ctf_rows[:, None, :]
    new_real = (real_part * cosine_table + imag_part * sine_table) * ctf_wide
    new_imag = (imag_part * cosine_table - real_part * sine_table) * ctf_wide
    joined = jnp.concatenate([new_real, new_imag], axis=2).astype(jnp.bfloat16)
    return joined.reshape(images.shape[0] * cosine_table.shape[0], 2 * half_width)


def tile_norms(ref_rows, ctf_square):
    half_width = ctf_square.shape[1]
    values = ref_rows.astype(jnp.float32)
    power_sum = (
        values[:, :half_width] * values[:, :half_width]
        + values[:, half_width:] * values[:, half_width:]
    )
    return lax.dot_general(ctf_square, power_sum, (((1,), (1,)), ((), ())), precision=HIGHEST)


def tile_scores(shifted, ref_rows, norms, gain_rows, bin_rows):
    count_here = gain_rows.shape[0]
    products = lax.dot_general(
        shifted, ref_rows, (((1,), (1,)), ((), ())), preferred_element_type=jnp.float32
    )
    products = products.reshape(count_here, shifted.shape[0] // count_here, ref_rows.shape[0])
    norm_term = jnp.dot(bin_rows, norms, precision=HIGHEST)
    return (
        gain_rows[:, None, None] * products
        - 0.5 * (gain_rows * gain_rows)[:, None, None] * norm_term[:, None, :]
    )


def combine_stats(former, latter):
    new_peak = jnp.maximum(former[0], latter[0])
    return (
        new_peak,
        former[1] * jnp.exp(former[0] - new_peak) + latter[1] * jnp.exp(latter[0] - new_peak),
    )


def combine_many(peaks, totals):
    new_peak = jnp.max(peaks, axis=0)
    return (new_peak, jnp.sum(totals * jnp.exp(peaks - new_peak[None]), axis=0))


def split_exact(value):
    high = lax.reduce_precision(value, exponent_bits=8, mantissa_bits=7)
    rest = value - high
    middle = lax.reduce_precision(rest, exponent_bits=8, mantissa_bits=7)
    return (high, middle, rest - middle)


def pack_kernel(sizes_ref, scales_ref, bins_ref, images_ref, out_ref):
    slots, width = images_ref.shape
    row = lax.broadcasted_iota(jnp.int32, (slots, META), 0)
    column = lax.broadcasted_iota(jnp.int32, (slots, META), 1)
    start = jnp.int32(0)
    gain = jnp.zeros((slots, META), jnp.float32)
    live = jnp.zeros((slots, META), jnp.float32)
    for group in range(sizes_ref.shape[0]):
        size = sizes_ref[group]
        inside = (row >= start) & (row < start + size)
        gain = jnp.where(inside, scales_ref[group], gain)
        live = jnp.where(inside, 1.0, live)
        start = start + size
    bins = jnp.zeros((slots, META), jnp.float32)
    for slot in range(slots):
        bins = jnp.where(row == slot, bins_ref[slot].astype(jnp.float32), bins)
    high = gain.astype(jnp.bfloat16).astype(jnp.float32)
    rest = gain - high
    middle = rest.astype(jnp.bfloat16).astype(jnp.float32)
    fields = (high, middle, rest - middle, live, bins)
    meta = jnp.zeros((slots, META), jnp.float32)
    for index, field in enumerate(fields):
        meta = jnp.where(column == index, field, meta)
    out_ref[:, :width] = images_ref[...]
    out_ref[:, width:] = meta.astype(out_ref.dtype)


def pack_rows(particles, group_counts, group_scale, defocus_bin):
    slots, width = particles.shape
    scalar = pl.BlockSpec(memory_space=pltpu.SMEM)
    whole = pl.BlockSpec(memory_space=pltpu.VMEM)
    return pl.pallas_call(
        pack_kernel,
        out_shape=jax.ShapeDtypeStruct((slots, width + META), particles.dtype),
        in_specs=[scalar, scalar, scalar, whole],
        out_specs=whole,
    )(group_counts, group_scale, defocus_bin, particles)


def xor_gather(value, axis, size):
    pieces = [value] + [
        lax.ppermute(value, axis, [(i, i ^ k) for i in range(size)]) for k in range(1, size)
    ]
    return jnp.concatenate(pieces, axis=0)


def xor_reorder(value, step, axis):
    return jnp.concatenate(
        [lax.slice_in_dim(value, j ^ step, (j ^ step) + 1, axis=axis) for j in range(value.shape[axis])],
        axis=axis,
    )


def xor_butterfly(stats, axis, size):
    step = 1
    while step < size:
        other = lax.ppermute(stats, axis, [(i, i ^ step) for i in range(size)])
        stats = jnp.stack(combine_stats(stats, other))
        step *= 2
    return stats


def accumulate(pieces, scores, gain_rows, ctf_rows, live_mask, peak_score, totals):
    weights = (
        jnp.exp(scores - peak_score[:, None, None])
        / totals[:, None, None]
        * live_mask[:, None, None]
    )
    scaled = (weights * gain_rows[:, None, None]).astype(jnp.bfloat16)
    numerator = None
    start = 0
    for shifted in pieces:
        count = shifted.shape[0] // scaled.shape[1]
        part = lax.dot_general(
            scaled[start : start + count].reshape(shifted.shape[0], -1),
            shifted,
            (((0,), (0,)), ((), ())),
            preferred_element_type=jnp.float32,
        )
        numerator = part if numerator is None else numerator + part
        start += count
    summed = jnp.sum(weights, axis=1) * (gain_rows * gain_rows)[:, None]
    denominator = lax.dot_general(
        summed, ctf_rows * ctf_rows, (((0,), (0,)), ((), ())), precision=HIGHEST
    )
    return (numerator, denominator)


def block_rows(images, gains, bins, norms, ref_tile, ctf_table, cosine_table, sine_table):
    bin_rows = bin_matrix(bins)
    ctf_rows = jnp.dot(bin_rows, ctf_table, precision=HIGHEST)
    shifted = shifted_rows(images, ctf_rows, cosine_table, sine_table)
    scores = tile_scores(shifted, ref_tile, norms, gains, bin_rows)
    return (shifted, scores, ctf_rows)


def per_device(
    particles, references, ctf_table, spectral_reg, defocus_bin, group_counts, group_scale,
    *, n_blk, n_cls,
):
    cosine_table, sine_table = phase_tables()
    ctf_square = ctf_table * ctf_table
    batch_size, width = particles.shape
    ref_tile = references[0]
    own_norms = tile_norms(ref_tile, ctf_square)
    classes_here = ref_tile.shape[0]
    shifts_count = cosine_table.shape[0]

    small = n_blk <= 4 and n_blk & (n_blk - 1) == 0 and n_cls & (n_cls - 1) == 0
    tables = (ref_tile, ctf_table, cosine_table, sine_table)
    if small:
        packed = pack_rows(particles, group_counts, group_scale, defocus_bin)
        others = xor_gather(packed, "blk", n_blk)[batch_size:]
        own_rows = lax.optimization_barrier(packed.astype(jnp.float32))
        groups = []
        for rows in (own_rows, others):
            meta = rows[:, width : width + 5].astype(jnp.float32)
            gains = (meta[:, 0] + meta[:, 1]) + meta[:, 2]
            groups.append((rows[:, :width], gains, meta[:, 3], meta[:, 4]))
        live_mask = groups[0][2]
    else:
        gain_rows, live_mask = slot_weights(
            group_counts.reshape(1, -1), group_scale.reshape(1, -1), batch_size
        )
        groups = [(
            lax.all_gather(particles, "blk", axis=0, tiled=True),
            lax.all_gather(gain_rows, "blk", axis=0, tiled=True),
            lax.all_gather(live_mask, "blk", axis=0, tiled=True),
            lax.all_gather(defocus_bin.astype(jnp.float32), "blk", axis=0, tiled=True),
        )]
    results = [block_rows(images, gains, bins, own_norms, *tables) for images, gains, _, bins in groups]
    pieces = [shifted for shifted, _, _ in results]
    all_scores = jnp.concatenate([scores for _, scores, _ in results], axis=0)
    ctf_rows = jnp.concatenate([rows for _, _, rows in results], axis=0)
    gain_all = jnp.concatenate([group[1] for group in groups])
    live_all = jnp.concatenate([group[2] for group in groups])
    whole_count = all_scores.shape[0]
    flattened = all_scores.reshape(whole_count, -1)
    peak_all = jnp.max(flattened, axis=1)
    totals_all = jnp.sum(jnp.exp(flattened - peak_all[:, None]), axis=1)

    if small:
        stats = jnp.stack([peak_all, totals_all]).reshape(2, n_blk, batch_size)
        stats = xor_butterfly(stats, "cls", n_cls)
        step = 1
        while step < n_blk:
            other = xor_reorder(lax.ppermute(stats, "blk", [(i, i ^ step) for i in range(n_blk)]), step, 1)
            stats = jnp.stack(combine_stats(stats, other))
            step *= 2
        peak_all, totals_all = stats[0], stats[1]
        peak_all = peak_all.reshape(-1)
        totals_all = totals_all.reshape(-1)
        peak_score = peak_all[:batch_size]
        totals = totals_all[:batch_size]
    else:
        gathered = lax.all_gather(jnp.stack([peak_all, totals_all]), ("blk", "cls"))
        peak_all, totals_all = combine_many(gathered[:, 0], gathered[:, 1])
        own_offset = lax.axis_index("blk") * batch_size
        peak_score = lax.dynamic_slice_in_dim(peak_all, own_offset, batch_size)
        totals = lax.dynamic_slice_in_dim(totals_all, own_offset, batch_size)

    numerator, denominator = accumulate(
        pieces, all_scores, gain_all, ctf_rows, live_all, peak_all, totals_all
    )
    log_evidence = jnp.where(live_mask > 0.5, peak_score + jnp.log(totals), 0.0)
    denominator = (
        jnp.concatenate([denominator, denominator], axis=1)
        + jnp.concatenate([spectral_reg, spectral_reg])[None, :]
    )
    class_average = (numerator / denominator)[None]
    return (class_average, log_evidence)


def solution(mesh):
    placed = (
        P(("groups", "blk"), None),
        P("blk", ("groups", "cls"), None),
        P("groups", None),
        P("groups"),
        P(("groups", "blk")),
        P(("groups", "blk")),
        P(("groups", "blk")),
    )
    body = lambda *args: per_device(*args, n_blk=mesh.shape["blk"], n_cls=mesh.shape["cls"])
    return jax.shard_map(
        body,
        mesh=mesh,
        in_specs=placed,
        out_specs=(P("blk", ("groups", "cls"), None), P(("groups", "blk"))),
        check_vma=False,
    )
```

```python
import math

import jax
import numpy as np
import jax.numpy as jnp
from jax import lax
from jax.experimental import pallas as pl
from jax.experimental.pallas import tpu as pltpu
from jax.sharding import PartitionSpec as P

KX = 32
KY = 64
IMG = 128
SIDE = 4
BINS = 16
META = 128


HIGHEST = lax.Precision.HIGHEST


def phase_tables():
    column = np.arange(KX * KY, dtype=np.int32)
    freq_x = (column % KX).astype(np.float32)
    freq_y = (column // KX - KY // 2).astype(np.float32)
    offsets = np.arange(SIDE, dtype=np.float32) - np.float32((SIDE - 1) / 2.0)
    shift_x = np.tile(offsets, SIDE)
    shift_y = np.repeat(offsets, SIDE)
    phases = np.float32(2.0 * math.pi / IMG) * (
        shift_x[:, None] * freq_x[None, :] + shift_y[:, None] * freq_y[None, :]
    )
    return (jnp.asarray(np.cos(phases)), jnp.asarray(np.sin(phases)))


def bin_matrix(bin_values):
    return (bin_values[:, None] == jnp.arange(BINS, dtype=jnp.float32)[None, :]).astype(jnp.float32)


def slot_weights(group_sizes, scale_rows, slots):
    group_ends = jnp.cumsum(group_sizes, axis=1)
    group_starts = group_ends - group_sizes
    slot_index = jnp.arange(slots, dtype=jnp.int32)
    membership = (
        (slot_index[None, :, None] >= group_starts[:, None, :])
        & (slot_index[None, :, None] < group_ends[:, None, :])
    ).astype(jnp.float32)
    gain_rows = jnp.sum(membership * scale_rows[:, None, :], axis=2)
    live_mask = jnp.sum(membership, axis=2)
    return (gain_rows.reshape(-1), live_mask.reshape(-1))


def shifted_rows(images, ctf_rows, cosine_table, sine_table):
    half_width = ctf_rows.shape[1]
    real_part = images[:, :half_width].astype(jnp.float32)[:, None, :]
    imag_part = images[:, half_width:].astype(jnp.float32)[:, None, :]
    ctf_wide = ctf_rows[:, None, :]
    new_real = (real_part * cosine_table + imag_part * sine_table) * ctf_wide
    new_imag = (imag_part * cosine_table - real_part * sine_table) * ctf_wide
    joined = jnp.concatenate([new_real, new_imag], axis=2).astype(jnp.bfloat16)
    return joined.reshape(images.shape[0] * cosine_table.shape[0], 2 * half_width)


def tile_norms(ref_rows, ctf_square):
    half_width = ctf_square.shape[1]
    values = ref_rows.astype(jnp.float32)
    power_sum = (
        values[:, :half_width] * values[:, :half_width]
        + values[:, half_width:] * values[:, half_width:]
    )
    return lax.dot_general(ctf_square, power_sum, (((1,), (1,)), ((), ())), precision=HIGHEST)


def tile_scores(shifted, ref_rows, norms, gain_rows, bin_rows):
    count_here = gain_rows.shape[0]
    products = lax.dot_general(
        shifted, ref_rows, (((1,), (1,)), ((), ())), preferred_element_type=jnp.float32
    )
    products = products.reshape(count_here, shifted.shape[0] // count_here, ref_rows.shape[0])
    norm_term = jnp.dot(bin_rows, norms, precision=HIGHEST)
    return (
        gain_rows[:, None, None] * products
        - 0.5 * (gain_rows * gain_rows)[:, None, None] * norm_term[:, None, :]
    )


def combine_stats(former, latter):
    new_peak = jnp.maximum(former[0], latter[0])
    return (
        new_peak,
        former[1] * jnp.exp(former[0] - new_peak) + latter[1] * jnp.exp(latter[0] - new_peak),
    )


def combine_many(peaks, totals):
    new_peak = jnp.max(peaks, axis=0)
    return (new_peak, jnp.sum(totals * jnp.exp(peaks - new_peak[None]), axis=0))


def split_exact(value):
    high = lax.reduce_precision(value, exponent_bits=8, mantissa_bits=7)
    rest = value - high
    middle = lax.reduce_precision(rest, exponent_bits=8, mantissa_bits=7)
    return (high, middle, rest - middle)


def pack_kernel(sizes_ref, scales_ref, bins_ref, images_ref, out_ref):
    slots, width = images_ref.shape
    row = lax.broadcasted_iota(jnp.int32, (slots, META), 0)
    column = lax.broadcasted_iota(jnp.int32, (slots, META), 1)
    start = jnp.int32(0)
    gain = jnp.zeros((slots, META), jnp.float32)
    live = jnp.zeros((slots, META), jnp.float32)
    for group in range(sizes_ref.shape[0]):
        size = sizes_ref[group]
        inside = (row >= start) & (row < start + size)
        gain = jnp.where(inside, scales_ref[group], gain)
        live = jnp.where(inside, 1.0, live)
        start = start + size
    bins = jnp.zeros((slots, META), jnp.float32)
    for slot in range(slots):
        bins = jnp.where(row == slot, bins_ref[slot].astype(jnp.float32), bins)
    high = gain.astype(jnp.bfloat16).astype(jnp.float32)
    rest = gain - high
    middle = rest.astype(jnp.bfloat16).astype(jnp.float32)
    fields = (high, middle, rest - middle, live, bins)
    meta = jnp.zeros((slots, META), jnp.float32)
    for index, field in enumerate(fields):
        meta = jnp.where(column == index, field, meta)
    out_ref[:, :width] = images_ref[...]
    out_ref[:, width:] = meta.astype(out_ref.dtype)


def pack_rows(particles, group_counts, group_scale, defocus_bin):
    slots, width = particles.shape
    scalar = pl.BlockSpec(memory_space=pltpu.SMEM)
    whole = pl.BlockSpec(memory_space=pltpu.VMEM)
    return pl.pallas_call(
        pack_kernel,
        out_shape=jax.ShapeDtypeStruct((slots, width + META), particles.dtype),
        in_specs=[scalar, scalar, scalar, whole],
        out_specs=whole,
    )(group_counts, group_scale, defocus_bin, particles)


def xor_gather(value, axis, size):
    pieces = [value] + [
        lax.ppermute(value, axis, [(i, i ^ k) for i in range(size)]) for k in range(1, size)
    ]
    return jnp.concatenate(pieces, axis=0)


def xor_reorder(value, step, axis):
    return jnp.concatenate(
        [lax.slice_in_dim(value, j ^ step, (j ^ step) + 1, axis=axis) for j in range(value.shape[axis])],
        axis=axis,
    )


def xor_butterfly(stats, axis, size):
    step = 1
    while step < size:
        other = lax.ppermute(stats, axis, [(i, i ^ step) for i in range(size)])
        stats = jnp.stack(combine_stats(stats, other))
        step *= 2
    return stats


def accumulate(pieces, scores, gain_rows, ctf_rows, live_mask, peak_score, totals):
    weights = (
        jnp.exp(scores - peak_score[:, None, None])
        / totals[:, None, None]
        * live_mask[:, None, None]
    )
    scaled = (weights * gain_rows[:, None, None]).astype(jnp.bfloat16)
    numerator = None
    start = 0
    for shifted in pieces:
        count = shifted.shape[0] // scaled.shape[1]
        part = lax.dot_general(
            scaled[start : start + count].reshape(shifted.shape[0], -1),
            shifted,
            (((0,), (0,)), ((), ())),
            preferred_element_type=jnp.float32,
        )
        numerator = part if numerator is None else numerator + part
        start += count
    summed = jnp.sum(weights, axis=1) * (gain_rows * gain_rows)[:, None]
    denominator = lax.dot_general(
        summed, ctf_rows * ctf_rows, (((0,), (0,)), ((), ())), precision=HIGHEST
    )
    return (numerator, denominator)


def block_rows(images, gains, bins, norms, ref_tile, ctf_table, cosine_table, sine_table):
    bin_rows = bin_matrix(bins)
    ctf_rows = jnp.dot(bin_rows, ctf_table, precision=HIGHEST)
    shifted = shifted_rows(images, ctf_rows, cosine_table, sine_table)
    scores = tile_scores(shifted, ref_tile, norms, gains, bin_rows)
    return (shifted, scores, ctf_rows)


def divide_kernel(numerator_ref, denominator_ref, reg_ref, out_ref):
    half = denominator_ref.shape[1]
    denominator = denominator_ref[...] + reg_ref[...]
    out_ref[:, :, :half] = (numerator_ref[:, :half] / denominator)[:, None, :]
    out_ref[:, :, half:] = (numerator_ref[:, half:] / denominator)[:, None, :]


def finish_average(numerator, denominator, spectral_reg):
    rows, width = numerator.shape
    whole = pl.BlockSpec(memory_space=pltpu.VMEM)
    out = pl.pallas_call(
        divide_kernel,
        out_shape=jax.ShapeDtypeStruct((rows, 1, width), numerator.dtype),
        in_specs=[whole, whole, whole],
        out_specs=whole,
    )(numerator, denominator, spectral_reg[None, :])
    return out.transpose(1, 0, 2)


def per_device(
    particles, references, ctf_table, spectral_reg, defocus_bin, group_counts, group_scale,
    *, n_blk, n_cls,
):
    cosine_table, sine_table = phase_tables()
    ctf_square = ctf_table * ctf_table
    batch_size, width = particles.shape
    ref_tile = references[0]
    own_norms = tile_norms(ref_tile, ctf_square)
    classes_here = ref_tile.shape[0]
    shifts_count = cosine_table.shape[0]

    small = n_blk <= 4 and n_blk & (n_blk - 1) == 0 and n_cls & (n_cls - 1) == 0
    tables = (ref_tile, ctf_table, cosine_table, sine_table)
    if small:
        packed = pack_rows(particles, group_counts, group_scale, defocus_bin)
        others = xor_gather(packed, "blk", n_blk)[batch_size:]
        own_rows = lax.optimization_barrier(packed.astype(jnp.float32))
        groups = []
        for rows in (own_rows, others):
            meta = rows[:, width : width + 5].astype(jnp.float32)
            gains = (meta[:, 0] + meta[:, 1]) + meta[:, 2]
            groups.append((rows[:, :width], gains, meta[:, 3], meta[:, 4]))
        live_mask = groups[0][2]
    else:
        gain_rows, live_mask = slot_weights(
            group_counts.reshape(1, -1), group_scale.reshape(1, -1), batch_size
        )
        groups = [(
            lax.all_gather(particles, "blk", axis=0, tiled=True),
            lax.all_gather(gain_rows, "blk", axis=0, tiled=True),
            lax.all_gather(live_mask, "blk", axis=0, tiled=True),
            lax.all_gather(defocus_bin.astype(jnp.float32), "blk", axis=0, tiled=True),
        )]
    results = [block_rows(images, gains, bins, own_norms, *tables) for images, gains, _, bins in groups]
    pieces = [shifted for shifted, _, _ in results]
    all_scores = jnp.concatenate([scores for _, scores, _ in results], axis=0)
    ctf_rows = jnp.concatenate([rows for _, _, rows in results], axis=0)
    gain_all = jnp.concatenate([group[1] for group in groups])
    live_all = jnp.concatenate([group[2] for group in groups])
    whole_count = all_scores.shape[0]
    flattened = all_scores.reshape(whole_count, -1)
    peak_all = jnp.max(flattened, axis=1)
    totals_all = jnp.sum(jnp.exp(flattened - peak_all[:, None]), axis=1)

    if small:
        stats = jnp.stack([peak_all, totals_all]).reshape(2, n_blk, batch_size)
        stats = xor_butterfly(stats, "cls", n_cls)
        parts = [stats] + [
            xor_reorder(lax.ppermute(stats, "blk", [(i, i ^ k) for i in range(n_blk)]), k, 1)
            for k in range(1, n_blk)
        ]
        parts = jnp.stack(parts)
        peak_all, totals_all = combine_many(parts[:, 0], parts[:, 1])
        peak_all = peak_all.reshape(-1)
        totals_all = totals_all.reshape(-1)
        peak_score = peak_all[:batch_size]
        totals = totals_all[:batch_size]
    else:
        gathered = lax.all_gather(jnp.stack([peak_all, totals_all]), ("blk", "cls"))
        peak_all, totals_all = combine_many(gathered[:, 0], gathered[:, 1])
        own_offset = lax.axis_index("blk") * batch_size
        peak_score = lax.dynamic_slice_in_dim(peak_all, own_offset, batch_size)
        totals = lax.dynamic_slice_in_dim(totals_all, own_offset, batch_size)

    numerator, denominator = accumulate(
        pieces, all_scores, gain_all, ctf_rows, live_all, peak_all, totals_all
    )
    log_evidence = jnp.where(live_mask > 0.5, peak_score + jnp.log(totals), 0.0)
    class_average = finish_average(numerator, denominator, spectral_reg)
    return (class_average, log_evidence)


def solution(mesh):
    placed = (
        P(("groups", "blk"), None),
        P("blk", ("groups", "cls"), None),
        P("groups", None),
        P("groups"),
        P(("groups", "blk")),
        P(("groups", "blk")),
        P(("groups", "blk")),
    )
    body = lambda *args: per_device(*args, n_blk=mesh.shape["blk"], n_cls=mesh.shape["cls"])
    return jax.shard_map(
        body,
        mesh=mesh,
        in_specs=placed,
        out_specs=(P("blk", ("groups", "cls"), None), P(("groups", "blk"))),
        check_vma=False,
    )
```

```python
import math

import jax
import numpy as np
import jax.numpy as jnp
from jax import lax
from jax.experimental import pallas as pl
from jax.experimental.pallas import tpu as pltpu
from jax.sharding import PartitionSpec as P

KX = 32
KY = 64
IMG = 128
SIDE = 4
BINS = 16
META = 128


HIGHEST = lax.Precision.HIGHEST


def phase_tables():
    column = np.arange(KX * KY, dtype=np.int32)
    freq_x = (column % KX).astype(np.float32)
    freq_y = (column // KX - KY // 2).astype(np.float32)
    offsets = np.arange(SIDE, dtype=np.float32) - np.float32((SIDE - 1) / 2.0)
    shift_x = np.tile(offsets, SIDE)
    shift_y = np.repeat(offsets, SIDE)
    phases = np.float32(2.0 * math.pi / IMG) * (
        shift_x[:, None] * freq_x[None, :] + shift_y[:, None] * freq_y[None, :]
    )
    return (jnp.asarray(np.cos(phases)), jnp.asarray(np.sin(phases)))


def bin_matrix(bin_values):
    return (bin_values[:, None] == jnp.arange(BINS, dtype=jnp.float32)[None, :]).astype(jnp.float32)


def slot_weights(group_sizes, scale_rows, slots):
    group_ends = jnp.cumsum(group_sizes, axis=1)
    group_starts = group_ends - group_sizes
    slot_index = jnp.arange(slots, dtype=jnp.int32)
    membership = (
        (slot_index[None, :, None] >= group_starts[:, None, :])
        & (slot_index[None, :, None] < group_ends[:, None, :])
    ).astype(jnp.float32)
    gain_rows = jnp.sum(membership * scale_rows[:, None, :], axis=2)
    live_mask = jnp.sum(membership, axis=2)
    return (gain_rows.reshape(-1), live_mask.reshape(-1))


def shifted_rows(images, ctf_rows, cosine_table, sine_table):
    half_width = ctf_rows.shape[1]
    real_part = images[:, :half_width].astype(jnp.float32)[:, None, :]
    imag_part = images[:, half_width:].astype(jnp.float32)[:, None, :]
    ctf_wide = ctf_rows[:, None, :]
    new_real = (real_part * cosine_table + imag_part * sine_table) * ctf_wide
    new_imag = (imag_part * cosine_table - real_part * sine_table) * ctf_wide
    joined = jnp.concatenate([new_real, new_imag], axis=2).astype(jnp.bfloat16)
    return joined.reshape(images.shape[0] * cosine_table.shape[0], 2 * half_width)


def tile_norms(ref_rows, ctf_square):
    half_width = ctf_square.shape[1]
    values = ref_rows.astype(jnp.float32)
    power_sum = (
        values[:, :half_width] * values[:, :half_width]
        + values[:, half_width:] * values[:, half_width:]
    )
    return lax.dot_general(ctf_square, power_sum, (((1,), (1,)), ((), ())), precision=HIGHEST)


def tile_scores(shifted, ref_rows, norms, gain_rows, bin_rows):
    count_here = gain_rows.shape[0]
    products = lax.dot_general(
        shifted, ref_rows, (((1,), (1,)), ((), ())), preferred_element_type=jnp.float32
    )
    products = products.reshape(count_here, shifted.shape[0] // count_here, ref_rows.shape[0])
    norm_term = jnp.dot(bin_rows, norms, precision=HIGHEST)
    return (
        gain_rows[:, None, None] * products
        - 0.5 * (gain_rows * gain_rows)[:, None, None] * norm_term[:, None, :]
    )


def combine_stats(former, latter):
    new_peak = jnp.maximum(former[0], latter[0])
    return (
        new_peak,
        former[1] * jnp.exp(former[0] - new_peak) + latter[1] * jnp.exp(latter[0] - new_peak),
    )


def combine_many(peaks, totals):
    new_peak = jnp.max(peaks, axis=0)
    return (new_peak, jnp.sum(totals * jnp.exp(peaks - new_peak[None]), axis=0))


def merge_pair(former, latter):
    new_peak = jnp.maximum(former[0], latter[0])
    scale_former = jnp.where(former[0] == new_peak, 1.0, jnp.exp(former[0] - new_peak))
    scale_latter = jnp.where(latter[0] == new_peak, 1.0, jnp.exp(latter[0] - new_peak))
    return (new_peak, former[1] * scale_former + latter[1] * scale_latter)


def local_stats(flattened):
    return lax.reduce(
        (flattened, jnp.ones_like(flattened)),
        (jnp.float32(-jnp.inf), jnp.float32(0.0)),
        merge_pair,
        (1,),
    )


def split_exact(value):
    high = lax.reduce_precision(value, exponent_bits=8, mantissa_bits=7)
    rest = value - high
    middle = lax.reduce_precision(rest, exponent_bits=8, mantissa_bits=7)
    return (high, middle, rest - middle)


def pack_kernel(sizes_ref, scales_ref, bins_ref, images_ref, out_ref):
    slots, width = images_ref.shape
    row = lax.broadcasted_iota(jnp.int32, (slots, META), 0)
    column = lax.broadcasted_iota(jnp.int32, (slots, META), 1)
    start = jnp.int32(0)
    gain = jnp.zeros((slots, META), jnp.float32)
    live = jnp.zeros((slots, META), jnp.float32)
    for group in range(sizes_ref.shape[0]):
        size = sizes_ref[group]
        inside = (row >= start) & (row < start + size)
        gain = jnp.where(inside, scales_ref[group], gain)
        live = jnp.where(inside, 1.0, live)
        start = start + size
    bins = jnp.zeros((slots, META), jnp.float32)
    for slot in range(slots):
        bins = jnp.where(row == slot, bins_ref[slot].astype(jnp.float32), bins)
    high = gain.astype(jnp.bfloat16).astype(jnp.float32)
    rest = gain - high
    middle = rest.astype(jnp.bfloat16).astype(jnp.float32)
    fields = (high, middle, rest - middle, live, bins)
    meta = jnp.zeros((slots, META), jnp.float32)
    for index, field in enumerate(fields):
        meta = jnp.where(column == index, field, meta)
    out_ref[:, :width] = images_ref[...]
    out_ref[:, width:] = meta.astype(out_ref.dtype)


def pack_rows(particles, group_counts, group_scale, defocus_bin):
    slots, width = particles.shape
    scalar = pl.BlockSpec(memory_space=pltpu.SMEM)
    whole = pl.BlockSpec(memory_space=pltpu.VMEM)
    return pl.pallas_call(
        pack_kernel,
        out_shape=jax.ShapeDtypeStruct((slots, width + META), particles.dtype),
        in_specs=[scalar, scalar, scalar, whole],
        out_specs=whole,
    )(group_counts, group_scale, defocus_bin, particles)


def xor_gather(value, axis, size):
    pieces = [value] + [
        lax.ppermute(value, axis, [(i, i ^ k) for i in range(size)]) for k in range(1, size)
    ]
    return jnp.concatenate(pieces, axis=0)


def xor_reorder(value, step, axis):
    return jnp.concatenate(
        [lax.slice_in_dim(value, j ^ step, (j ^ step) + 1, axis=axis) for j in range(value.shape[axis])],
        axis=axis,
    )


def xor_butterfly(stats, axis, size):
    step = 1
    while step < size:
        other = lax.ppermute(stats, axis, [(i, i ^ step) for i in range(size)])
        stats = jnp.stack(combine_stats(stats, other))
        step *= 2
    return stats


def accumulate(pieces, scores, gain_rows, ctf_rows, live_mask, peak_score, totals):
    weights = (
        jnp.exp(scores - peak_score[:, None, None])
        / totals[:, None, None]
        * live_mask[:, None, None]
    )
    scaled = (weights * gain_rows[:, None, None]).astype(jnp.bfloat16)
    numerator = None
    start = 0
    for shifted in pieces:
        count = shifted.shape[0] // scaled.shape[1]
        part = lax.dot_general(
            scaled[start : start + count].reshape(shifted.shape[0], -1),
            shifted,
            (((0,), (0,)), ((), ())),
            preferred_element_type=jnp.float32,
        )
        numerator = part if numerator is None else numerator + part
        start += count
    summed = jnp.sum(weights, axis=1) * (gain_rows * gain_rows)[:, None]
    denominator = lax.dot_general(
        summed, ctf_rows * ctf_rows, (((0,), (0,)), ((), ())), precision=HIGHEST
    )
    return (numerator, denominator)


def block_rows(images, gains, bins, norms, ref_tile, ctf_table, cosine_table, sine_table):
    bin_rows = bin_matrix(bins)
    ctf_rows = jnp.dot(bin_rows, ctf_table, precision=HIGHEST)
    shifted = shifted_rows(images, ctf_rows, cosine_table, sine_table)
    scores = tile_scores(shifted, ref_tile, norms, gains, bin_rows)
    return (shifted, scores, ctf_rows)


def per_device(
    particles, references, ctf_table, spectral_reg, defocus_bin, group_counts, group_scale,
    *, n_blk, n_cls,
):
    cosine_table, sine_table = phase_tables()
    ctf_square = ctf_table * ctf_table
    batch_size, width = particles.shape
    ref_tile = references[0]
    own_norms = tile_norms(ref_tile, ctf_square)
    classes_here = ref_tile.shape[0]
    shifts_count = cosine_table.shape[0]

    small = n_blk <= 4 and n_blk & (n_blk - 1) == 0 and n_cls & (n_cls - 1) == 0
    tables = (ref_tile, ctf_table, cosine_table, sine_table)
    if small:
        packed = pack_rows(particles, group_counts, group_scale, defocus_bin)
        others = xor_gather(packed, "blk", n_blk)[batch_size:]
        own_rows = lax.optimization_barrier(packed.astype(jnp.float32))
        groups = []
        for rows in (own_rows, others):
            meta = rows[:, width : width + 5].astype(jnp.float32)
            gains = (meta[:, 0] + meta[:, 1]) + meta[:, 2]
            groups.append((rows[:, :width], gains, meta[:, 3], meta[:, 4]))
        live_mask = groups[0][2]
    else:
        gain_rows, live_mask = slot_weights(
            group_counts.reshape(1, -1), group_scale.reshape(1, -1), batch_size
        )
        groups = [(
            lax.all_gather(particles, "blk", axis=0, tiled=True),
            lax.all_gather(gain_rows, "blk", axis=0, tiled=True),
            lax.all_gather(live_mask, "blk", axis=0, tiled=True),
            lax.all_gather(defocus_bin.astype(jnp.float32), "blk", axis=0, tiled=True),
        )]
    results = [block_rows(images, gains, bins, own_norms, *tables) for images, gains, _, bins in groups]
    pieces = [shifted for shifted, _, _ in results]
    all_scores = jnp.concatenate([scores for _, scores, _ in results], axis=0)
    ctf_rows = jnp.concatenate([rows for _, _, rows in results], axis=0)
    gain_all = jnp.concatenate([group[1] for group in groups])
    live_all = jnp.concatenate([group[2] for group in groups])
    whole_count = all_scores.shape[0]
    flattened = all_scores.reshape(whole_count, -1)
    peak_all, totals_all = local_stats(flattened)

    if small:
        stats = jnp.stack([peak_all, totals_all]).reshape(2, n_blk, batch_size)
        stats = xor_butterfly(stats, "cls", n_cls)
        parts = [stats] + [
            xor_reorder(lax.ppermute(stats, "blk", [(i, i ^ k) for i in range(n_blk)]), k, 1)
            for k in range(1, n_blk)
        ]
        parts = jnp.stack(parts)
        peak_all, totals_all = combine_many(parts[:, 0], parts[:, 1])
        peak_all = peak_all.reshape(-1)
        totals_all = totals_all.reshape(-1)
        peak_score = peak_all[:batch_size]
        totals = totals_all[:batch_size]
    else:
        gathered = lax.all_gather(jnp.stack([peak_all, totals_all]), ("blk", "cls"))
        peak_all, totals_all = combine_many(gathered[:, 0], gathered[:, 1])
        own_offset = lax.axis_index("blk") * batch_size
        peak_score = lax.dynamic_slice_in_dim(peak_all, own_offset, batch_size)
        totals = lax.dynamic_slice_in_dim(totals_all, own_offset, batch_size)

    numerator, denominator = accumulate(
        pieces, all_scores, gain_all, ctf_rows, live_all, peak_all, totals_all
    )
    log_evidence = jnp.where(live_mask > 0.5, peak_score + jnp.log(totals), 0.0)
    denominator = (
        jnp.concatenate([denominator, denominator], axis=1)
        + jnp.concatenate([spectral_reg, spectral_reg])[None, :]
    )
    class_average = (numerator / denominator)[None]
    return (class_average, log_evidence)


def solution(mesh):
    placed = (
        P(("groups", "blk"), None),
        P("blk", ("groups", "cls"), None),
        P("groups", None),
        P("groups"),
        P(("groups", "blk")),
        P(("groups", "blk")),
        P(("groups", "blk")),
    )
    body = lambda *args: per_device(*args, n_blk=mesh.shape["blk"], n_cls=mesh.shape["cls"])
    return jax.shard_map(
        body,
        mesh=mesh,
        in_specs=placed,
        out_specs=(P("blk", ("groups", "cls"), None), P(("groups", "blk"))),
        check_vma=False,
    )
```

```python
import math

import jax
import numpy as np
import jax.numpy as jnp
from jax import lax
from jax.experimental import pallas as pl
from jax.experimental.pallas import tpu as pltpu
from jax.sharding import PartitionSpec as P

KX = 32
KY = 64
IMG = 128
SIDE = 4
BINS = 16
META = 128


HIGHEST = lax.Precision.HIGHEST


def phase_tables():
    column = np.arange(KX * KY, dtype=np.int32)
    freq_x = (column % KX).astype(np.float32)
    freq_y = (column // KX - KY // 2).astype(np.float32)
    offsets = np.arange(SIDE, dtype=np.float32) - np.float32((SIDE - 1) / 2.0)
    shift_x = np.tile(offsets, SIDE)
    shift_y = np.repeat(offsets, SIDE)
    phases = np.float32(2.0 * math.pi / IMG) * (
        shift_x[:, None] * freq_x[None, :] + shift_y[:, None] * freq_y[None, :]
    )
    return (jnp.asarray(np.cos(phases)), jnp.asarray(np.sin(phases)))


def bin_matrix(bin_values):
    return (bin_values[:, None] == jnp.arange(BINS, dtype=jnp.float32)[None, :]).astype(jnp.float32)


def slot_weights(group_sizes, scale_rows, slots):
    group_ends = jnp.cumsum(group_sizes, axis=1)
    group_starts = group_ends - group_sizes
    slot_index = jnp.arange(slots, dtype=jnp.int32)
    membership = (
        (slot_index[None, :, None] >= group_starts[:, None, :])
        & (slot_index[None, :, None] < group_ends[:, None, :])
    ).astype(jnp.float32)
    gain_rows = jnp.sum(membership * scale_rows[:, None, :], axis=2)
    live_mask = jnp.sum(membership, axis=2)
    return (gain_rows.reshape(-1), live_mask.reshape(-1))


def shifted_rows(images, ctf_rows, cosine_table, sine_table):
    half_width = ctf_rows.shape[1]
    real_part = images[:, :half_width].astype(jnp.float32)[:, None, :]
    imag_part = images[:, half_width:].astype(jnp.float32)[:, None, :]
    ctf_wide = ctf_rows[:, None, :]
    new_real = (real_part * cosine_table + imag_part * sine_table) * ctf_wide
    new_imag = (imag_part * cosine_table - real_part * sine_table) * ctf_wide
    joined = jnp.concatenate([new_real, new_imag], axis=2).astype(jnp.bfloat16)
    return joined.reshape(images.shape[0] * cosine_table.shape[0], 2 * half_width)


def tile_norms(ref_rows, ctf_square):
    half_width = ctf_square.shape[1]
    values = ref_rows.astype(jnp.float32)
    power_sum = (
        values[:, :half_width] * values[:, :half_width]
        + values[:, half_width:] * values[:, half_width:]
    )
    return lax.dot_general(ctf_square, power_sum, (((1,), (1,)), ((), ())), precision=HIGHEST)


def tile_scores(shifted, ref_rows, norm_term, gain_rows):
    count_here = gain_rows.shape[0]
    products = lax.dot_general(
        shifted, ref_rows, (((1,), (1,)), ((), ())), preferred_element_type=jnp.float32
    )
    products = products.reshape(count_here, shifted.shape[0] // count_here, ref_rows.shape[0])
    return (
        gain_rows[:, None, None] * products
        - 0.5 * (gain_rows * gain_rows)[:, None, None] * norm_term[:, None, :]
    )


def combine_stats(former, latter):
    new_peak = jnp.maximum(former[0], latter[0])
    return (
        new_peak,
        former[1] * jnp.exp(former[0] - new_peak) + latter[1] * jnp.exp(latter[0] - new_peak),
    )


def combine_many(peaks, totals):
    new_peak = jnp.max(peaks, axis=0)
    return (new_peak, jnp.sum(totals * jnp.exp(peaks - new_peak[None]), axis=0))


def merge_pair(former, latter):
    new_peak = jnp.maximum(former[0], latter[0])
    scale_former = jnp.where(former[0] == new_peak, 1.0, jnp.exp(former[0] - new_peak))
    scale_latter = jnp.where(latter[0] == new_peak, 1.0, jnp.exp(latter[0] - new_peak))
    return (new_peak, former[1] * scale_former + latter[1] * scale_latter)


def local_stats(flattened):
    return lax.reduce(
        (flattened, jnp.ones_like(flattened)),
        (jnp.float32(-jnp.inf), jnp.float32(0.0)),
        merge_pair,
        (1,),
    )


def split_exact(value):
    high = lax.reduce_precision(value, exponent_bits=8, mantissa_bits=7)
    rest = value - high
    middle = lax.reduce_precision(rest, exponent_bits=8, mantissa_bits=7)
    return (high, middle, rest - middle)


def pack_kernel(sizes_ref, scales_ref, bins_ref, images_ref, out_ref):
    slots, width = images_ref.shape
    row = lax.broadcasted_iota(jnp.int32, (slots, META), 0)
    column = lax.broadcasted_iota(jnp.int32, (slots, META), 1)
    start = jnp.int32(0)
    gain = jnp.zeros((slots, META), jnp.float32)
    live = jnp.zeros((slots, META), jnp.float32)
    for group in range(sizes_ref.shape[0]):
        size = sizes_ref[group]
        inside = (row >= start) & (row < start + size)
        gain = jnp.where(inside, scales_ref[group], gain)
        live = jnp.where(inside, 1.0, live)
        start = start + size
    bins = jnp.zeros((slots, META), jnp.float32)
    for slot in range(slots):
        bins = jnp.where(row == slot, bins_ref[slot].astype(jnp.float32), bins)
    high = gain.astype(jnp.bfloat16).astype(jnp.float32)
    rest = gain - high
    middle = rest.astype(jnp.bfloat16).astype(jnp.float32)
    fields = (high, middle, rest - middle, live, bins)
    meta = jnp.zeros((slots, META), jnp.float32)
    for index, field in enumerate(fields):
        meta = jnp.where(column == index, field, meta)
    out_ref[:, :width] = images_ref[...]
    out_ref[:, width:] = meta.astype(out_ref.dtype)


def pack_rows(particles, group_counts, group_scale, defocus_bin):
    slots, width = particles.shape
    scalar = pl.BlockSpec(memory_space=pltpu.SMEM)
    whole = pl.BlockSpec(memory_space=pltpu.VMEM)
    return pl.pallas_call(
        pack_kernel,
        out_shape=jax.ShapeDtypeStruct((slots, width + META), particles.dtype),
        in_specs=[scalar, scalar, scalar, whole],
        out_specs=whole,
    )(group_counts, group_scale, defocus_bin, particles)


def xor_gather(value, axis, size):
    pieces = [value] + [
        lax.ppermute(value, axis, [(i, i ^ k) for i in range(size)]) for k in range(1, size)
    ]
    return jnp.concatenate(pieces, axis=0)


def xor_reorder(value, step, axis):
    return jnp.concatenate(
        [lax.slice_in_dim(value, j ^ step, (j ^ step) + 1, axis=axis) for j in range(value.shape[axis])],
        axis=axis,
    )


def xor_butterfly(stats, axis, size):
    step = 1
    while step < size:
        other = lax.ppermute(stats, axis, [(i, i ^ step) for i in range(size)])
        stats = jnp.stack(combine_stats(stats, other))
        step *= 2
    return stats


def accumulate(pieces, scores, gain_rows, ctf_rows, live_mask, peak_score, totals):
    weights = (
        jnp.exp(scores - peak_score[:, None, None])
        / totals[:, None, None]
        * live_mask[:, None, None]
    )
    scaled = (weights * gain_rows[:, None, None]).astype(jnp.bfloat16)
    numerator = None
    start = 0
    for shifted in pieces:
        count = shifted.shape[0] // scaled.shape[1]
        part = lax.dot_general(
            scaled[start : start + count].reshape(shifted.shape[0], -1),
            shifted,
            (((0,), (0,)), ((), ())),
            preferred_element_type=jnp.float32,
        )
        numerator = part if numerator is None else numerator + part
        start += count
    summed = jnp.sum(weights, axis=1) * (gain_rows * gain_rows)[:, None]
    denominator = lax.dot_general(
        summed, ctf_rows * ctf_rows, (((0,), (0,)), ((), ())), precision=HIGHEST
    )
    return (numerator, denominator)


def block_rows(images, gains, bins, bin_table, ref_tile, cosine_table, sine_table):
    half_width = images.shape[1] // 2
    picked = jnp.dot(bin_matrix(bins), bin_table, precision=HIGHEST)
    ctf_rows = picked[:, :half_width]
    shifted = shifted_rows(images, ctf_rows, cosine_table, sine_table)
    scores = tile_scores(shifted, ref_tile, picked[:, half_width:], gains)
    return (shifted, scores, ctf_rows)


def per_device(
    particles, references, ctf_table, spectral_reg, defocus_bin, group_counts, group_scale,
    *, n_blk, n_cls,
):
    cosine_table, sine_table = phase_tables()
    ctf_square = ctf_table * ctf_table
    batch_size, width = particles.shape
    ref_tile = references[0]
    own_norms = tile_norms(ref_tile, ctf_square)
    classes_here = ref_tile.shape[0]
    shifts_count = cosine_table.shape[0]

    small = n_blk <= 4 and n_blk & (n_blk - 1) == 0 and n_cls & (n_cls - 1) == 0
    tables = (jnp.concatenate([ctf_table, own_norms], axis=1), ref_tile, cosine_table, sine_table)
    if small:
        packed = pack_rows(particles, group_counts, group_scale, defocus_bin)
        others = xor_gather(packed, "blk", n_blk)[batch_size:]
        own_rows = lax.optimization_barrier(packed.astype(jnp.float32))
        groups = []
        for rows in (own_rows, others):
            meta = rows[:, width : width + 5].astype(jnp.float32)
            gains = (meta[:, 0] + meta[:, 1]) + meta[:, 2]
            groups.append((rows[:, :width], gains, meta[:, 3], meta[:, 4]))
        live_mask = groups[0][2]
    else:
        gain_rows, live_mask = slot_weights(
            group_counts.reshape(1, -1), group_scale.reshape(1, -1), batch_size
        )
        groups = [(
            lax.all_gather(particles, "blk", axis=0, tiled=True),
            lax.all_gather(gain_rows, "blk", axis=0, tiled=True),
            lax.all_gather(live_mask, "blk", axis=0, tiled=True),
            lax.all_gather(defocus_bin.astype(jnp.float32), "blk", axis=0, tiled=True),
        )]
    results = [block_rows(images, gains, bins, *tables) for images, gains, _, bins in groups]
    pieces = [shifted for shifted, _, _ in results]
    all_scores = jnp.concatenate([scores for _, scores, _ in results], axis=0)
    ctf_rows = jnp.concatenate([rows for _, _, rows in results], axis=0)
    gain_all = jnp.concatenate([group[1] for group in groups])
    live_all = jnp.concatenate([group[2] for group in groups])
    whole_count = all_scores.shape[0]
    flattened = all_scores.reshape(whole_count, -1)
    peak_all, totals_all = local_stats(flattened)

    if small:
        stats = jnp.stack([peak_all, totals_all]).reshape(2, n_blk, batch_size)
        stats = xor_butterfly(stats, "cls", n_cls)
        parts = [stats] + [
            xor_reorder(lax.ppermute(stats, "blk", [(i, i ^ k) for i in range(n_blk)]), k, 1)
            for k in range(1, n_blk)
        ]
        parts = jnp.stack(parts)
        peak_all, totals_all = combine_many(parts[:, 0], parts[:, 1])
        peak_all = peak_all.reshape(-1)
        totals_all = totals_all.reshape(-1)
        peak_score = peak_all[:batch_size]
        totals = totals_all[:batch_size]
    else:
        gathered = lax.all_gather(jnp.stack([peak_all, totals_all]), ("blk", "cls"))
        peak_all, totals_all = combine_many(gathered[:, 0], gathered[:, 1])
        own_offset = lax.axis_index("blk") * batch_size
        peak_score = lax.dynamic_slice_in_dim(peak_all, own_offset, batch_size)
        totals = lax.dynamic_slice_in_dim(totals_all, own_offset, batch_size)

    numerator, denominator = accumulate(
        pieces, all_scores, gain_all, ctf_rows, live_all, peak_all, totals_all
    )
    log_evidence = jnp.where(live_mask > 0.5, peak_score + jnp.log(totals), 0.0)
    denominator = (
        jnp.concatenate([denominator, denominator], axis=1)
        + jnp.concatenate([spectral_reg, spectral_reg])[None, :]
    )
    class_average = (numerator / denominator)[None]
    return (class_average, log_evidence)


def solution(mesh):
    placed = (
        P(("groups", "blk"), None),
        P("blk", ("groups", "cls"), None),
        P("groups", None),
        P("groups"),
        P(("groups", "blk")),
        P(("groups", "blk")),
        P(("groups", "blk")),
    )
    body = lambda *args: per_device(*args, n_blk=mesh.shape["blk"], n_cls=mesh.shape["cls"])
    return jax.shard_map(
        body,
        mesh=mesh,
        in_specs=placed,
        out_specs=(P("blk", ("groups", "cls"), None), P(("groups", "blk"))),
        check_vma=False,
    )
```

```python
import math

import jax
import numpy as np
import jax.numpy as jnp
from jax import lax
from jax.experimental import pallas as pl
from jax.experimental.pallas import tpu as pltpu
from jax.sharding import PartitionSpec as P

KX = 32
KY = 64
IMG = 128
SIDE = 4
BINS = 16
META = 128


HIGHEST = lax.Precision.HIGHEST


def phase_tables():
    column = np.arange(KX * KY, dtype=np.int32)
    freq_x = (column % KX).astype(np.float32)
    freq_y = (column // KX - KY // 2).astype(np.float32)
    offsets = np.arange(SIDE, dtype=np.float32) - np.float32((SIDE - 1) / 2.0)
    shift_x = np.tile(offsets, SIDE)
    shift_y = np.repeat(offsets, SIDE)
    phases = np.float32(2.0 * math.pi / IMG) * (
        shift_x[:, None] * freq_x[None, :] + shift_y[:, None] * freq_y[None, :]
    )
    return (jnp.asarray(np.cos(phases)), jnp.asarray(np.sin(phases)))


def bin_matrix(bin_values):
    return (bin_values[:, None] == jnp.arange(BINS, dtype=jnp.float32)[None, :]).astype(jnp.float32)


def slot_weights(group_sizes, scale_rows, slots):
    group_ends = jnp.cumsum(group_sizes, axis=1)
    group_starts = group_ends - group_sizes
    slot_index = jnp.arange(slots, dtype=jnp.int32)
    membership = (
        (slot_index[None, :, None] >= group_starts[:, None, :])
        & (slot_index[None, :, None] < group_ends[:, None, :])
    ).astype(jnp.float32)
    gain_rows = jnp.sum(membership * scale_rows[:, None, :], axis=2)
    live_mask = jnp.sum(membership, axis=2)
    return (gain_rows.reshape(-1), live_mask.reshape(-1))


def shifted_rows(images, ctf_rows, cosine_table, sine_table):
    half_width = ctf_rows.shape[1]
    real_part = images[:, :half_width].astype(jnp.float32)[:, None, :]
    imag_part = images[:, half_width:].astype(jnp.float32)[:, None, :]
    ctf_wide = ctf_rows[:, None, :]
    new_real = (real_part * cosine_table + imag_part * sine_table) * ctf_wide
    new_imag = (imag_part * cosine_table - real_part * sine_table) * ctf_wide
    joined = jnp.concatenate([new_real, new_imag], axis=2).astype(jnp.bfloat16)
    return joined.reshape(images.shape[0] * cosine_table.shape[0], 2 * half_width)


def tile_norms(ref_rows, ctf_square):
    half_width = ctf_square.shape[1]
    values = ref_rows.astype(jnp.float32)
    power_sum = (
        values[:, :half_width] * values[:, :half_width]
        + values[:, half_width:] * values[:, half_width:]
    )
    return lax.dot_general(ctf_square, power_sum, (((1,), (1,)), ((), ())), precision=HIGHEST)


def tile_scores(shifted, ref_rows, norm_term, gain_rows):
    count_here = gain_rows.shape[0]
    products = lax.dot_general(
        shifted, ref_rows, (((1,), (1,)), ((), ())), preferred_element_type=jnp.float32
    )
    products = products.reshape(count_here, shifted.shape[0] // count_here, ref_rows.shape[0])
    return (
        gain_rows[:, None, None] * products
        - 0.5 * (gain_rows * gain_rows)[:, None, None] * norm_term[:, None, :]
    )


def combine_stats(former, latter):
    new_peak = jnp.maximum(former[0], latter[0])
    return (
        new_peak,
        former[1] * jnp.exp(former[0] - new_peak) + latter[1] * jnp.exp(latter[0] - new_peak),
    )


def combine_many(peaks, totals):
    new_peak = jnp.max(peaks, axis=0)
    return (new_peak, jnp.sum(totals * jnp.exp(peaks - new_peak[None]), axis=0))


def merge_pair(former, latter):
    new_peak = jnp.maximum(former[0], latter[0])
    scale_former = jnp.where(former[0] == new_peak, 1.0, jnp.exp(former[0] - new_peak))
    scale_latter = jnp.where(latter[0] == new_peak, 1.0, jnp.exp(latter[0] - new_peak))
    return (new_peak, former[1] * scale_former + latter[1] * scale_latter)


def local_stats(flattened):
    return lax.reduce(
        (flattened, jnp.ones_like(flattened)),
        (jnp.float32(-jnp.inf), jnp.float32(0.0)),
        merge_pair,
        (1,),
    )


def split_exact(value):
    high = lax.reduce_precision(value, exponent_bits=8, mantissa_bits=7)
    rest = value - high
    middle = lax.reduce_precision(rest, exponent_bits=8, mantissa_bits=7)
    return (high, middle, rest - middle)


def pack_kernel(sizes_ref, scales_ref, bins_ref, images_ref, out_ref):
    slots, width = images_ref.shape
    row = lax.broadcasted_iota(jnp.int32, (slots, META), 0)
    column = lax.broadcasted_iota(jnp.int32, (slots, META), 1)
    start = jnp.int32(0)
    gain = jnp.zeros((slots, META), jnp.float32)
    live = jnp.zeros((slots, META), jnp.float32)
    for group in range(sizes_ref.shape[0]):
        size = sizes_ref[group]
        inside = (row >= start) & (row < start + size)
        gain = jnp.where(inside, scales_ref[group], gain)
        live = jnp.where(inside, 1.0, live)
        start = start + size
    bins = jnp.zeros((slots, META), jnp.float32)
    for slot in range(slots):
        bins = jnp.where(row == slot, bins_ref[slot].astype(jnp.float32), bins)
    high = gain.astype(jnp.bfloat16).astype(jnp.float32)
    rest = gain - high
    middle = rest.astype(jnp.bfloat16).astype(jnp.float32)
    fields = (high, middle, rest - middle, live, bins)
    meta = jnp.zeros((slots, META), jnp.float32)
    for index, field in enumerate(fields):
        meta = jnp.where(column == index, field, meta)
    out_ref[:, :width] = images_ref[...]
    out_ref[:, width:] = meta.astype(out_ref.dtype)


def pack_rows(particles, group_counts, group_scale, defocus_bin):
    slots, width = particles.shape
    scalar = pl.BlockSpec(memory_space=pltpu.SMEM)
    whole = pl.BlockSpec(memory_space=pltpu.VMEM)
    return pl.pallas_call(
        pack_kernel,
        out_shape=jax.ShapeDtypeStruct((slots, width + META), particles.dtype),
        in_specs=[scalar, scalar, scalar, whole],
        out_specs=whole,
    )(group_counts, group_scale, defocus_bin, particles)


def xor_gather(value, axis, size):
    pieces = [value] + [
        lax.ppermute(value, axis, [(i, i ^ k) for i in range(size)]) for k in range(1, size)
    ]
    return jnp.concatenate(pieces, axis=0)


def xor_reorder(value, step, axis):
    return jnp.concatenate(
        [lax.slice_in_dim(value, j ^ step, (j ^ step) + 1, axis=axis) for j in range(value.shape[axis])],
        axis=axis,
    )


def xor_butterfly(stats, axis, size):
    step = 1
    while step < size:
        other = lax.ppermute(stats, axis, [(i, i ^ step) for i in range(size)])
        stats = jnp.stack(combine_stats(stats, other))
        step *= 2
    return stats


def accumulate(pieces, scores, gain_rows, ctf_rows, live_mask, peak_score, totals):
    weights = (
        jnp.exp(scores - peak_score[:, None, None])
        / totals[:, None, None]
        * live_mask[:, None, None]
    )
    scaled = (weights * gain_rows[:, None, None]).astype(jnp.bfloat16)
    numerator = None
    start = 0
    for shifted in pieces:
        count = shifted.shape[0] // scaled.shape[1]
        part = lax.dot_general(
            scaled[start : start + count].reshape(shifted.shape[0], -1),
            shifted,
            (((0,), (0,)), ((), ())),
            preferred_element_type=jnp.float32,
        )
        numerator = part if numerator is None else numerator + part
        start += count
    summed = jnp.sum(weights, axis=1) * (gain_rows * gain_rows)[:, None]
    denominator = lax.dot_general(
        summed, ctf_rows * ctf_rows, (((0,), (0,)), ((), ())), precision=HIGHEST
    )
    return (numerator, denominator)


def block_rows(images, gains, bins, bin_table, ref_tile, cosine_table, sine_table):
    half_width = images.shape[1] // 2
    picked = jnp.dot(bin_matrix(bins), bin_table, precision=HIGHEST)
    ctf_rows = picked[:, :half_width]
    shifted = shifted_rows(images, ctf_rows, cosine_table, sine_table)
    scores = tile_scores(shifted, ref_tile, picked[:, half_width:], gains)
    return (shifted, scores, ctf_rows)


def per_device(
    particles, references, ctf_table, spectral_reg, defocus_bin, group_counts, group_scale,
    *, n_blk, n_cls,
):
    cosine_table, sine_table = phase_tables()
    ctf_square = ctf_table * ctf_table
    batch_size, width = particles.shape
    ref_tile = references[0]
    own_norms = tile_norms(ref_tile, ctf_square)
    classes_here = ref_tile.shape[0]
    shifts_count = cosine_table.shape[0]

    small = n_blk <= 4 and n_blk & (n_blk - 1) == 0 and n_cls & (n_cls - 1) == 0
    tables = (jnp.concatenate([ctf_table, own_norms], axis=1), ref_tile, cosine_table, sine_table)
    if small:
        packed = pack_rows(particles, group_counts, group_scale, defocus_bin)
        others = xor_gather(packed, "blk", n_blk)[batch_size:]
        own_rows = lax.optimization_barrier(packed.astype(jnp.float32))
        groups = []
        for rows in (own_rows, others):
            meta = rows[:, width : width + 5].astype(jnp.float32)
            gains = (meta[:, 0] + meta[:, 1]) + meta[:, 2]
            groups.append((rows[:, :width], gains, meta[:, 3], meta[:, 4]))
        live_mask = groups[0][2]
    else:
        gain_rows, live_mask = slot_weights(
            group_counts.reshape(1, -1), group_scale.reshape(1, -1), batch_size
        )
        groups = [(
            lax.all_gather(particles, "blk", axis=0, tiled=True),
            lax.all_gather(gain_rows, "blk", axis=0, tiled=True),
            lax.all_gather(live_mask, "blk", axis=0, tiled=True),
            lax.all_gather(defocus_bin.astype(jnp.float32), "blk", axis=0, tiled=True),
        )]
    results = [block_rows(images, gains, bins, *tables) for images, gains, _, bins in groups]
    pieces = [shifted for shifted, _, _ in results]
    all_scores = jnp.concatenate([scores for _, scores, _ in results], axis=0)
    ctf_rows = jnp.concatenate([rows for _, _, rows in results], axis=0)
    gain_all = jnp.concatenate([group[1] for group in groups])
    live_all = jnp.concatenate([group[2] for group in groups])
    whole_count = all_scores.shape[0]
    flattened = all_scores.reshape(whole_count, -1)
    peak_all, totals_all = local_stats(flattened)

    if small:
        stats = jnp.stack([peak_all, totals_all]).reshape(2, n_blk, batch_size)
        parts = [stats] + [
            xor_reorder(lax.ppermute(stats, "blk", [(i, i ^ k) for i in range(n_blk)]), k, 1)
            for k in range(1, n_blk)
        ]
        parts = jnp.stack(parts)
        stats = jnp.stack(combine_many(parts[:, 0], parts[:, 1]))
        peak_all, totals_all = xor_butterfly(stats, "cls", n_cls)
        peak_all = peak_all.reshape(-1)
        totals_all = totals_all.reshape(-1)
        peak_score = peak_all[:batch_size]
        totals = totals_all[:batch_size]
    else:
        gathered = lax.all_gather(jnp.stack([peak_all, totals_all]), ("blk", "cls"))
        peak_all, totals_all = combine_many(gathered[:, 0], gathered[:, 1])
        own_offset = lax.axis_index("blk") * batch_size
        peak_score = lax.dynamic_slice_in_dim(peak_all, own_offset, batch_size)
        totals = lax.dynamic_slice_in_dim(totals_all, own_offset, batch_size)

    numerator, denominator = accumulate(
        pieces, all_scores, gain_all, ctf_rows, live_all, peak_all, totals_all
    )
    log_evidence = jnp.where(live_mask > 0.5, peak_score + jnp.log(totals), 0.0)
    denominator = (
        jnp.concatenate([denominator, denominator], axis=1)
        + jnp.concatenate([spectral_reg, spectral_reg])[None, :]
    )
    class_average = (numerator / denominator)[None]
    return (class_average, log_evidence)


def solution(mesh):
    placed = (
        P(("groups", "blk"), None),
        P("blk", ("groups", "cls"), None),
        P("groups", None),
        P("groups"),
        P(("groups", "blk")),
        P(("groups", "blk")),
        P(("groups", "blk")),
    )
    body = lambda *args: per_device(*args, n_blk=mesh.shape["blk"], n_cls=mesh.shape["cls"])
    return jax.shard_map(
        body,
        mesh=mesh,
        in_specs=placed,
        out_specs=(P("blk", ("groups", "cls"), None), P(("groups", "blk"))),
        check_vma=False,
    )
```

```python
import math

import jax
import numpy as np
import jax.numpy as jnp
from jax import lax
from jax.experimental import pallas as pl
from jax.experimental.pallas import tpu as pltpu
from jax.sharding import PartitionSpec as P

KX = 32
KY = 64
IMG = 128
SIDE = 4
BINS = 16
META = 128


HIGHEST = lax.Precision.HIGHEST


def phase_tables():
    column = np.arange(KX * KY, dtype=np.int32)
    freq_x = (column % KX).astype(np.float32)
    freq_y = (column // KX - KY // 2).astype(np.float32)
    offsets = np.arange(SIDE, dtype=np.float32) - np.float32((SIDE - 1) / 2.0)
    shift_x = np.tile(offsets, SIDE)
    shift_y = np.repeat(offsets, SIDE)
    phases = np.float32(2.0 * math.pi / IMG) * (
        shift_x[:, None] * freq_x[None, :] + shift_y[:, None] * freq_y[None, :]
    )
    return (jnp.asarray(np.cos(phases)), jnp.asarray(np.sin(phases)))


def bin_matrix(bin_values):
    return (bin_values[:, None] == jnp.arange(BINS, dtype=jnp.float32)[None, :]).astype(jnp.float32)


def slot_weights(group_sizes, scale_rows, slots):
    group_ends = jnp.cumsum(group_sizes, axis=1)
    group_starts = group_ends - group_sizes
    slot_index = jnp.arange(slots, dtype=jnp.int32)
    membership = (
        (slot_index[None, :, None] >= group_starts[:, None, :])
        & (slot_index[None, :, None] < group_ends[:, None, :])
    ).astype(jnp.float32)
    gain_rows = jnp.sum(membership * scale_rows[:, None, :], axis=2)
    live_mask = jnp.sum(membership, axis=2)
    return (gain_rows.reshape(-1), live_mask.reshape(-1))


def shifted_rows(images, ctf_rows, cosine_table, sine_table):
    half_width = ctf_rows.shape[1]
    real_part = images[:, :half_width].astype(jnp.float32)[:, None, :]
    imag_part = images[:, half_width:].astype(jnp.float32)[:, None, :]
    ctf_wide = ctf_rows[:, None, :]
    new_real = (real_part * cosine_table + imag_part * sine_table) * ctf_wide
    new_imag = (imag_part * cosine_table - real_part * sine_table) * ctf_wide
    joined = jnp.concatenate([new_real, new_imag], axis=2).astype(jnp.bfloat16)
    return joined.reshape(images.shape[0] * cosine_table.shape[0], 2 * half_width)


def tile_norms(ref_rows, ctf_square):
    half_width = ctf_square.shape[1]
    values = ref_rows.astype(jnp.float32)
    power_sum = (
        values[:, :half_width] * values[:, :half_width]
        + values[:, half_width:] * values[:, half_width:]
    )
    return lax.dot_general(ctf_square, power_sum, (((1,), (1,)), ((), ())), precision=HIGHEST)


def tile_scores(shifted, ref_rows, norm_term, gain_rows):
    count_here = gain_rows.shape[0]
    products = lax.dot_general(
        shifted, ref_rows, (((1,), (1,)), ((), ())), preferred_element_type=jnp.float32
    )
    products = products.reshape(count_here, shifted.shape[0] // count_here, ref_rows.shape[0])
    return (
        gain_rows[:, None, None] * products
        - 0.5 * (gain_rows * gain_rows)[:, None, None] * norm_term[:, None, :]
    )


def combine_stats(former, latter):
    new_peak = jnp.maximum(former[0], latter[0])
    return (
        new_peak,
        former[1] * jnp.exp(former[0] - new_peak) + latter[1] * jnp.exp(latter[0] - new_peak),
    )


def combine_many(peaks, totals):
    new_peak = jnp.max(peaks, axis=0)
    return (new_peak, jnp.sum(totals * jnp.exp(peaks - new_peak[None]), axis=0))


def merge_pair(former, latter):
    new_peak = jnp.maximum(former[0], latter[0])
    scale_former = jnp.where(former[0] == new_peak, 1.0, jnp.exp(former[0] - new_peak))
    scale_latter = jnp.where(latter[0] == new_peak, 1.0, jnp.exp(latter[0] - new_peak))
    return (new_peak, former[1] * scale_former + latter[1] * scale_latter)


def local_stats(flattened):
    return lax.reduce(
        (flattened, jnp.ones_like(flattened)),
        (jnp.float32(-jnp.inf), jnp.float32(0.0)),
        merge_pair,
        (1,),
    )


def split_exact(value):
    high = lax.reduce_precision(value, exponent_bits=8, mantissa_bits=7)
    rest = value - high
    middle = lax.reduce_precision(rest, exponent_bits=8, mantissa_bits=7)
    return (high, middle, rest - middle)


def pack_kernel(sizes_ref, scales_ref, bins_ref, images_ref, out_ref, half_ref):
    slots, width = images_ref.shape
    row = lax.broadcasted_iota(jnp.int32, (slots, META), 0)
    column = lax.broadcasted_iota(jnp.int32, (slots, META), 1)
    start = jnp.int32(0)
    gain = jnp.zeros((slots, META), jnp.float32)
    live = jnp.zeros((slots, META), jnp.float32)
    for group in range(sizes_ref.shape[0]):
        size = sizes_ref[group]
        inside = (row >= start) & (row < start + size)
        gain = jnp.where(inside, scales_ref[group], gain)
        live = jnp.where(inside, 1.0, live)
        start = start + size
    bins = jnp.zeros((slots, META), jnp.float32)
    for slot in range(slots):
        bins = jnp.where(row == slot, bins_ref[slot].astype(jnp.float32), bins)
    high = gain.astype(jnp.bfloat16).astype(jnp.float32)
    rest = gain - high
    middle = rest.astype(jnp.bfloat16).astype(jnp.float32)
    parity = lax.axis_index("cls") % 2
    fields = (high, middle, rest - middle, live, bins, jnp.full((slots, META), parity, jnp.float32))
    meta = jnp.zeros((slots, META), jnp.float32)
    for index, field in enumerate(fields):
        meta = jnp.where(column == index, field, meta)
    out_ref[:, :width] = images_ref[...]
    out_ref[:, width:] = meta.astype(out_ref.dtype)
    cut = half_ref.shape[1]

    @pl.when(parity == 0)
    def _():
        half_ref[...] = images_ref[:, :cut]

    @pl.when(parity == 1)
    def _():
        half_ref[:, : width - cut] = images_ref[:, cut:]
        half_ref[:, width - cut : width - cut + META] = meta.astype(half_ref.dtype)
        half_ref[:, width - cut + META :] = jnp.zeros(
            (slots, 2 * cut - width - META), half_ref.dtype
        )


def pack_rows(particles, group_counts, group_scale, defocus_bin):
    slots, width = particles.shape
    scalar = pl.BlockSpec(memory_space=pltpu.SMEM)
    whole = pl.BlockSpec(memory_space=pltpu.VMEM)
    cut = 128 * -(-(width + META) // 256)
    return pl.pallas_call(
        pack_kernel,
        out_shape=(
            jax.ShapeDtypeStruct((slots, width + META), particles.dtype),
            jax.ShapeDtypeStruct((slots, cut), particles.dtype),
        ),
        in_specs=[scalar, scalar, scalar, whole],
        out_specs=(whole, whole),
    )(group_counts, group_scale, defocus_bin, particles)


def xor_gather(value, axis, size):
    pieces = [value] + [
        lax.ppermute(value, axis, [(i, i ^ k) for i in range(size)]) for k in range(1, size)
    ]
    return jnp.concatenate(pieces, axis=0)


def xor_reorder(value, step, axis):
    return jnp.concatenate(
        [lax.slice_in_dim(value, j ^ step, (j ^ step) + 1, axis=axis) for j in range(value.shape[axis])],
        axis=axis,
    )


def xor_butterfly(stats, axis, size):
    step = 1
    while step < size:
        other = lax.ppermute(stats, axis, [(i, i ^ step) for i in range(size)])
        stats = jnp.stack(combine_stats(stats, other))
        step *= 2
    return stats


def accumulate(pieces, scores, gain_rows, ctf_rows, live_mask, peak_score, totals):
    weights = (
        jnp.exp(scores - peak_score[:, None, None])
        / totals[:, None, None]
        * live_mask[:, None, None]
    )
    scaled = (weights * gain_rows[:, None, None]).astype(jnp.bfloat16)
    numerator = None
    start = 0
    for shifted in pieces:
        count = shifted.shape[0] // scaled.shape[1]
        part = lax.dot_general(
            scaled[start : start + count].reshape(shifted.shape[0], -1),
            shifted,
            (((0,), (0,)), ((), ())),
            preferred_element_type=jnp.float32,
        )
        numerator = part if numerator is None else numerator + part
        start += count
    summed = jnp.sum(weights, axis=1) * (gain_rows * gain_rows)[:, None]
    denominator = lax.dot_general(
        summed, ctf_rows * ctf_rows, (((0,), (0,)), ((), ())), precision=HIGHEST
    )
    return (numerator, denominator)


def block_rows(images, gains, bins, bin_table, ref_tile, cosine_table, sine_table):
    half_width = images.shape[1] // 2
    picked = jnp.dot(bin_matrix(bins), bin_table, precision=HIGHEST)
    ctf_rows = picked[:, :half_width]
    shifted = shifted_rows(images, ctf_rows, cosine_table, sine_table)
    scores = tile_scores(shifted, ref_tile, picked[:, half_width:], gains)
    return (shifted, scores, ctf_rows)


def per_device(
    particles, references, ctf_table, spectral_reg, defocus_bin, group_counts, group_scale,
    *, n_blk, n_cls,
):
    cosine_table, sine_table = phase_tables()
    ctf_square = ctf_table * ctf_table
    batch_size, width = particles.shape
    ref_tile = references[0]
    own_norms = tile_norms(ref_tile, ctf_square)
    classes_here = ref_tile.shape[0]
    shifts_count = cosine_table.shape[0]

    small = n_blk <= 4 and n_blk & (n_blk - 1) == 0 and n_cls >= 2 and n_cls & (n_cls - 1) == 0
    tables = (jnp.concatenate([ctf_table, own_norms], axis=1), ref_tile, cosine_table, sine_table)
    if small:
        packed, half = pack_rows(particles, group_counts, group_scale, defocus_bin)
        mine = xor_gather(half, "blk", n_blk)[batch_size:]
        theirs = lax.ppermute(mine, "cls", [(i, i ^ 1) for i in range(n_cls)])
        own_rows = lax.optimization_barrier(packed.astype(jnp.float32))
        first = own_rows[0, width + 5] < 0.5
        cut = half.shape[1]
        others = jnp.concatenate(
            [jnp.where(first, mine, theirs), jnp.where(first, theirs, mine)[:, : width + META - cut]],
            axis=1,
        )
        groups = []
        for rows in (own_rows, others):
            meta = rows[:, width : width + 5].astype(jnp.float32)
            gains = (meta[:, 0] + meta[:, 1]) + meta[:, 2]
            groups.append((rows[:, :width], gains, meta[:, 3], meta[:, 4]))
        live_mask = groups[0][2]
    else:
        gain_rows, live_mask = slot_weights(
            group_counts.reshape(1, -1), group_scale.reshape(1, -1), batch_size
        )
        groups = [(
            lax.all_gather(particles, "blk", axis=0, tiled=True),
            lax.all_gather(gain_rows, "blk", axis=0, tiled=True),
            lax.all_gather(live_mask, "blk", axis=0, tiled=True),
            lax.all_gather(defocus_bin.astype(jnp.float32), "blk", axis=0, tiled=True),
        )]
    results = [block_rows(images, gains, bins, *tables) for images, gains, _, bins in groups]
    pieces = [shifted for shifted, _, _ in results]
    all_scores = jnp.concatenate([scores for _, scores, _ in results], axis=0)
    ctf_rows = jnp.concatenate([rows for _, _, rows in results], axis=0)
    gain_all = jnp.concatenate([group[1] for group in groups])
    live_all = jnp.concatenate([group[2] for group in groups])
    whole_count = all_scores.shape[0]
    flattened = all_scores.reshape(whole_count, -1)
    peak_all, totals_all = local_stats(flattened)

    if small:
        stats = jnp.stack([peak_all, totals_all]).reshape(2, n_blk, batch_size)
        stats = xor_butterfly(stats, "cls", n_cls)
        parts = [stats] + [
            xor_reorder(lax.ppermute(stats, "blk", [(i, i ^ k) for i in range(n_blk)]), k, 1)
            for k in range(1, n_blk)
        ]
        parts = jnp.stack(parts)
        peak_all, totals_all = combine_many(parts[:, 0], parts[:, 1])
        peak_all = peak_all.reshape(-1)
        totals_all = totals_all.reshape(-1)
        peak_score = peak_all[:batch_size]
        totals = totals_all[:batch_size]
    else:
        gathered = lax.all_gather(jnp.stack([peak_all, totals_all]), ("blk", "cls"))
        peak_all, totals_all = combine_many(gathered[:, 0], gathered[:, 1])
        own_offset = lax.axis_index("blk") * batch_size
        peak_score = lax.dynamic_slice_in_dim(peak_all, own_offset, batch_size)
        totals = lax.dynamic_slice_in_dim(totals_all, own_offset, batch_size)

    numerator, denominator = accumulate(
        pieces, all_scores, gain_all, ctf_rows, live_all, peak_all, totals_all
    )
    log_evidence = jnp.where(live_mask > 0.5, peak_score + jnp.log(totals), 0.0)
    denominator = (
        jnp.concatenate([denominator, denominator], axis=1)
        + jnp.concatenate([spectral_reg, spectral_reg])[None, :]
    )
    class_average = (numerator / denominator)[None]
    return (class_average, log_evidence)


def solution(mesh):
    placed = (
        P(("groups", "blk"), None),
        P("blk", ("groups", "cls"), None),
        P("groups", None),
        P("groups"),
        P(("groups", "blk")),
        P(("groups", "blk")),
        P(("groups", "blk")),
    )
    body = lambda *args: per_device(*args, n_blk=mesh.shape["blk"], n_cls=mesh.shape["cls"])
    return jax.shard_map(
        body,
        mesh=mesh,
        in_specs=placed,
        out_specs=(P("blk", ("groups", "cls"), None), P(("groups", "blk"))),
        check_vma=False,
    )
```

```python
import math

import jax
import numpy as np
import jax.numpy as jnp
from jax import lax
from jax.experimental import pallas as pl
from jax.experimental.pallas import tpu as pltpu
from jax.sharding import PartitionSpec as P

KX = 32
KY = 64
IMG = 128
SIDE = 4
BINS = 16
META = 128


HIGHEST = lax.Precision.HIGHEST


def phase_tables():
    column = np.arange(KX * KY, dtype=np.int32)
    freq_x = (column % KX).astype(np.float32)
    freq_y = (column // KX - KY // 2).astype(np.float32)
    offsets = np.arange(SIDE, dtype=np.float32) - np.float32((SIDE - 1) / 2.0)
    shift_x = np.tile(offsets, SIDE)
    shift_y = np.repeat(offsets, SIDE)
    phases = np.float32(2.0 * math.pi / IMG) * (
        shift_x[:, None] * freq_x[None, :] + shift_y[:, None] * freq_y[None, :]
    )
    return (jnp.asarray(np.cos(phases)), jnp.asarray(np.sin(phases)))


def bin_matrix(bin_values):
    return (bin_values[:, None] == jnp.arange(BINS, dtype=jnp.float32)[None, :]).astype(jnp.float32)


def slot_weights(group_sizes, scale_rows, slots):
    group_ends = jnp.cumsum(group_sizes, axis=1)
    group_starts = group_ends - group_sizes
    slot_index = jnp.arange(slots, dtype=jnp.int32)
    membership = (
        (slot_index[None, :, None] >= group_starts[:, None, :])
        & (slot_index[None, :, None] < group_ends[:, None, :])
    ).astype(jnp.float32)
    gain_rows = jnp.sum(membership * scale_rows[:, None, :], axis=2)
    live_mask = jnp.sum(membership, axis=2)
    return (gain_rows.reshape(-1), live_mask.reshape(-1))


def shifted_rows(images, ctf_rows, cosine_table, sine_table):
    half_width = ctf_rows.shape[1]
    real_part = images[:, :half_width].astype(jnp.float32)[:, None, :]
    imag_part = images[:, half_width:].astype(jnp.float32)[:, None, :]
    ctf_wide = ctf_rows[:, None, :]
    new_real = (real_part * cosine_table + imag_part * sine_table) * ctf_wide
    new_imag = (imag_part * cosine_table - real_part * sine_table) * ctf_wide
    joined = jnp.concatenate([new_real, new_imag], axis=2).astype(jnp.bfloat16)
    return joined.reshape(images.shape[0] * cosine_table.shape[0], 2 * half_width)


def tile_norms(ref_rows, ctf_square):
    half_width = ctf_square.shape[1]
    values = ref_rows.astype(jnp.float32)
    power_sum = (
        values[:, :half_width] * values[:, :half_width]
        + values[:, half_width:] * values[:, half_width:]
    )
    return lax.dot_general(ctf_square, power_sum, (((1,), (1,)), ((), ())), precision=HIGHEST)


def tile_scores(shifted, ref_rows, norm_term, gain_rows):
    count_here = gain_rows.shape[0]
    products = lax.dot_general(
        shifted, ref_rows, (((1,), (1,)), ((), ())), preferred_element_type=jnp.float32
    )
    products = products.reshape(count_here, shifted.shape[0] // count_here, ref_rows.shape[0])
    return (
        gain_rows[:, None, None] * products
        - 0.5 * (gain_rows * gain_rows)[:, None, None] * norm_term[:, None, :]
    )


def combine_stats(former, latter):
    new_peak = jnp.maximum(former[0], latter[0])
    return (
        new_peak,
        former[1] * jnp.exp(former[0] - new_peak) + latter[1] * jnp.exp(latter[0] - new_peak),
    )


def combine_many(peaks, totals):
    new_peak = jnp.max(peaks, axis=0)
    return (new_peak, jnp.sum(totals * jnp.exp(peaks - new_peak[None]), axis=0))


def merge_pair(former, latter):
    new_peak = jnp.maximum(former[0], latter[0])
    scale_former = jnp.where(former[0] == new_peak, 1.0, jnp.exp(former[0] - new_peak))
    scale_latter = jnp.where(latter[0] == new_peak, 1.0, jnp.exp(latter[0] - new_peak))
    return (new_peak, former[1] * scale_former + latter[1] * scale_latter)


def local_stats(flattened):
    return lax.reduce(
        (flattened, jnp.ones_like(flattened)),
        (jnp.float32(-jnp.inf), jnp.float32(0.0)),
        merge_pair,
        (1,),
    )


def split_exact(value):
    high = lax.reduce_precision(value, exponent_bits=8, mantissa_bits=7)
    rest = value - high
    middle = lax.reduce_precision(rest, exponent_bits=8, mantissa_bits=7)
    return (high, middle, rest - middle)


def pack_kernel(sizes_ref, scales_ref, bins_ref, images_ref, out_ref):
    slots, width = images_ref.shape
    row = lax.broadcasted_iota(jnp.int32, (slots, META), 0)
    column = lax.broadcasted_iota(jnp.int32, (slots, META), 1)
    start = jnp.int32(0)
    gain = jnp.zeros((slots, META), jnp.float32)
    live = jnp.zeros((slots, META), jnp.float32)
    for group in range(sizes_ref.shape[0]):
        size = sizes_ref[group]
        inside = (row >= start) & (row < start + size)
        gain = jnp.where(inside, scales_ref[group], gain)
        live = jnp.where(inside, 1.0, live)
        start = start + size
    bins = jnp.zeros((slots, META), jnp.float32)
    for slot in range(slots):
        bins = jnp.where(row == slot, bins_ref[slot].astype(jnp.float32), bins)
    high = gain.astype(jnp.bfloat16).astype(jnp.float32)
    rest = gain - high
    middle = rest.astype(jnp.bfloat16).astype(jnp.float32)
    fields = (high, middle, rest - middle, live, bins)
    meta = jnp.zeros((slots, META), jnp.float32)
    for index, field in enumerate(fields):
        meta = jnp.where(column == index, field, meta)
    out_ref[:, :width] = images_ref[...]
    out_ref[:, width:] = meta.astype(out_ref.dtype)


def pack_rows(particles, group_counts, group_scale, defocus_bin):
    slots, width = particles.shape
    scalar = pl.BlockSpec(memory_space=pltpu.SMEM)
    whole = pl.BlockSpec(memory_space=pltpu.VMEM)
    return pl.pallas_call(
        pack_kernel,
        out_shape=jax.ShapeDtypeStruct((slots, width + META), particles.dtype),
        in_specs=[scalar, scalar, scalar, whole],
        out_specs=whole,
    )(group_counts, group_scale, defocus_bin, particles)


def xor_gather(value, axis, size):
    pieces = [value] + [
        lax.ppermute(value, axis, [(i, i ^ k) for i in range(size)]) for k in range(1, size)
    ]
    return jnp.concatenate(pieces, axis=0)


def xor_reorder(value, step, axis):
    return jnp.concatenate(
        [lax.slice_in_dim(value, j ^ step, (j ^ step) + 1, axis=axis) for j in range(value.shape[axis])],
        axis=axis,
    )


def xor_butterfly(stats, axis, size):
    step = 1
    while step < size:
        other = lax.ppermute(stats, axis, [(i, i ^ step) for i in range(size)])
        stats = jnp.stack(combine_stats(stats, other))
        step *= 2
    return stats


def accumulate(pieces, scores, gain_rows, ctf_rows, live_mask, peak_score, totals):
    weights = (
        jnp.exp(scores - peak_score[:, None, None])
        / totals[:, None, None]
        * live_mask[:, None, None]
    )
    scaled = (weights * gain_rows[:, None, None]).astype(jnp.bfloat16)
    numerator = None
    start = 0
    for shifted in pieces:
        count = shifted.shape[0] // scaled.shape[1]
        part = lax.dot_general(
            scaled[start : start + count].reshape(shifted.shape[0], -1),
            shifted,
            (((0,), (0,)), ((), ())),
            preferred_element_type=jnp.float32,
        )
        numerator = part if numerator is None else numerator + part
        start += count
    summed = jnp.sum(weights, axis=1) * (gain_rows * gain_rows)[:, None]
    denominator = lax.dot_general(
        summed, ctf_rows * ctf_rows, (((0,), (0,)), ((), ())), precision=HIGHEST
    )
    return (numerator, denominator)


def block_rows(images, gains, bins, bin_table, ref_tile, cosine_table, sine_table):
    half_width = images.shape[1] // 2
    picked = jnp.dot(bin_matrix(bins), bin_table, precision=HIGHEST)
    ctf_rows = picked[:, :half_width]
    shifted = shifted_rows(images, ctf_rows, cosine_table, sine_table)
    scores = tile_scores(shifted, ref_tile, picked[:, half_width:], gains)
    return (shifted, scores, ctf_rows)


def per_device(
    particles, references, ctf_table, spectral_reg, defocus_bin, group_counts, group_scale,
    *, n_blk, n_cls,
):
    cosine_table, sine_table = phase_tables()
    ctf_square = ctf_table * ctf_table
    batch_size, width = particles.shape
    ref_tile = references[0]
    own_norms = tile_norms(ref_tile, ctf_square)
    classes_here = ref_tile.shape[0]
    shifts_count = cosine_table.shape[0]

    small = n_blk <= 4 and n_blk & (n_blk - 1) == 0 and n_cls & (n_cls - 1) == 0
    tables = (jnp.concatenate([ctf_table, own_norms], axis=1), ref_tile, cosine_table, sine_table)
    if small:
        packed = pack_rows(particles, group_counts, group_scale, defocus_bin)
        others = xor_gather(packed, "blk", n_blk)[batch_size:]
        own_rows = lax.optimization_barrier(packed.astype(jnp.float32))
        groups = []
        for rows in (own_rows, others):
            meta = rows[:, width : width + 5].astype(jnp.float32)
            gains = (meta[:, 0] + meta[:, 1]) + meta[:, 2]
            groups.append((rows[:, :width], gains, meta[:, 3], meta[:, 4]))
        live_mask = groups[0][2]
    else:
        gain_rows, live_mask = slot_weights(
            group_counts.reshape(1, -1), group_scale.reshape(1, -1), batch_size
        )
        groups = [(
            lax.all_gather(particles, "blk", axis=0, tiled=True),
            lax.all_gather(gain_rows, "blk", axis=0, tiled=True),
            lax.all_gather(live_mask, "blk", axis=0, tiled=True),
            lax.all_gather(defocus_bin.astype(jnp.float32), "blk", axis=0, tiled=True),
        )]
    results = [block_rows(images, gains, bins, *tables) for images, gains, _, bins in groups]
    pieces = [shifted for shifted, _, _ in results]
    all_scores = jnp.concatenate([scores for _, scores, _ in results], axis=0)
    ctf_rows = jnp.concatenate([rows for _, _, rows in results], axis=0)
    gain_all = jnp.concatenate([group[1] for group in groups])
    live_all = jnp.concatenate([group[2] for group in groups])
    whole_count = all_scores.shape[0]
    flattened = all_scores.reshape(whole_count, -1)
    peak_all, totals_all = local_stats(flattened)

    if small:
        stats = jnp.stack([peak_all, totals_all]).reshape(2, n_blk, batch_size)
        stats = xor_butterfly(stats, "cls", n_cls)
        parts = [stats] + [
            xor_reorder(lax.ppermute(stats, "blk", [(i, i ^ k) for i in range(n_blk)]), k, 1)
            for k in range(1, n_blk)
        ]
        parts = jnp.stack(parts)
        peak_all, totals_all = combine_many(parts[:, 0], parts[:, 1])
        peak_all = peak_all.reshape(-1)
        totals_all = totals_all.reshape(-1)
        peak_score = peak_all[:batch_size]
        totals = totals_all[:batch_size]
    else:
        gathered = lax.all_gather(jnp.stack([peak_all, totals_all]), ("blk", "cls"))
        peak_all, totals_all = combine_many(gathered[:, 0], gathered[:, 1])
        own_offset = lax.axis_index("blk") * batch_size
        peak_score = lax.dynamic_slice_in_dim(peak_all, own_offset, batch_size)
        totals = lax.dynamic_slice_in_dim(totals_all, own_offset, batch_size)

    numerator, denominator = accumulate(
        pieces, all_scores, gain_all, ctf_rows, live_all, peak_all, totals_all
    )
    log_evidence = jnp.where(live_all > 0.5, peak_all + jnp.log(totals_all), 0.0)[:batch_size]
    denominator = (
        jnp.concatenate([denominator, denominator], axis=1)
        + jnp.concatenate([spectral_reg, spectral_reg])[None, :]
    )
    class_average = (numerator / denominator)[None]
    return (class_average, log_evidence)


def solution(mesh):
    placed = (
        P(("groups", "blk"), None),
        P("blk", ("groups", "cls"), None),
        P("groups", None),
        P("groups"),
        P(("groups", "blk")),
        P(("groups", "blk")),
        P(("groups", "blk")),
    )
    body = lambda *args: per_device(*args, n_blk=mesh.shape["blk"], n_cls=mesh.shape["cls"])
    return jax.shard_map(
        body,
        mesh=mesh,
        in_specs=placed,
        out_specs=(P("blk", ("groups", "cls"), None), P(("groups", "blk"))),
        check_vma=False,
    )
```

```python
import math

import jax
import numpy as np
import jax.numpy as jnp
from jax import lax
from jax.experimental import pallas as pl
from jax.experimental.pallas import tpu as pltpu
from jax.sharding import PartitionSpec as P

KX = 32
KY = 64
IMG = 128
SIDE = 4
BINS = 16
META = 128


HIGHEST = lax.Precision.HIGHEST


def phase_tables():
    column = np.arange(KX * KY, dtype=np.int32)
    freq_x = (column % KX).astype(np.float32)
    freq_y = (column // KX - KY // 2).astype(np.float32)
    offsets = np.arange(SIDE, dtype=np.float32) - np.float32((SIDE - 1) / 2.0)
    shift_x = np.tile(offsets, SIDE)
    shift_y = np.repeat(offsets, SIDE)
    phases = np.float32(2.0 * math.pi / IMG) * (
        shift_x[:, None] * freq_x[None, :] + shift_y[:, None] * freq_y[None, :]
    )
    return (jnp.asarray(np.cos(phases)), jnp.asarray(np.sin(phases)))


def bin_matrix(bin_values):
    return (bin_values[:, None] == jnp.arange(BINS, dtype=jnp.float32)[None, :]).astype(jnp.float32)


def slot_weights(group_sizes, scale_rows, slots):
    group_ends = jnp.cumsum(group_sizes, axis=1)
    group_starts = group_ends - group_sizes
    slot_index = jnp.arange(slots, dtype=jnp.int32)
    membership = (
        (slot_index[None, :, None] >= group_starts[:, None, :])
        & (slot_index[None, :, None] < group_ends[:, None, :])
    ).astype(jnp.float32)
    gain_rows = jnp.sum(membership * scale_rows[:, None, :], axis=2)
    live_mask = jnp.sum(membership, axis=2)
    return (gain_rows.reshape(-1), live_mask.reshape(-1))


def shifted_rows(images, ctf_rows, cosine_table, sine_table):
    half_width = ctf_rows.shape[1]
    real_part = (images[:, :half_width].astype(jnp.float32) * ctf_rows)[:, None, :]
    imag_part = (images[:, half_width:].astype(jnp.float32) * ctf_rows)[:, None, :]
    new_real = real_part * cosine_table + imag_part * sine_table
    new_imag = imag_part * cosine_table - real_part * sine_table
    joined = jnp.concatenate([new_real, new_imag], axis=2).astype(jnp.bfloat16)
    return joined.reshape(images.shape[0] * cosine_table.shape[0], 2 * half_width)


def tile_norms(ref_rows, ctf_square):
    half_width = ctf_square.shape[1]
    values = ref_rows.astype(jnp.float32)
    power_sum = (
        values[:, :half_width] * values[:, :half_width]
        + values[:, half_width:] * values[:, half_width:]
    )
    return lax.dot_general(ctf_square, power_sum, (((1,), (1,)), ((), ())), precision=HIGHEST)


def tile_scores(shifted, ref_rows, norm_term, gain_rows):
    count_here = gain_rows.shape[0]
    products = lax.dot_general(
        shifted, ref_rows, (((1,), (1,)), ((), ())), preferred_element_type=jnp.float32
    )
    products = products.reshape(count_here, shifted.shape[0] // count_here, ref_rows.shape[0])
    return (
        gain_rows[:, None, None] * products
        - 0.5 * (gain_rows * gain_rows)[:, None, None] * norm_term[:, None, :]
    )


def combine_stats(former, latter):
    new_peak = jnp.maximum(former[0], latter[0])
    return (
        new_peak,
        former[1] * jnp.exp(former[0] - new_peak) + latter[1] * jnp.exp(latter[0] - new_peak),
    )


def combine_many(peaks, totals):
    new_peak = jnp.max(peaks, axis=0)
    return (new_peak, jnp.sum(totals * jnp.exp(peaks - new_peak[None]), axis=0))


def merge_pair(former, latter):
    new_peak = jnp.maximum(former[0], latter[0])
    scale_former = jnp.where(former[0] == new_peak, 1.0, jnp.exp(former[0] - new_peak))
    scale_latter = jnp.where(latter[0] == new_peak, 1.0, jnp.exp(latter[0] - new_peak))
    return (new_peak, former[1] * scale_former + latter[1] * scale_latter)


def local_stats(flattened):
    return lax.reduce(
        (flattened, jnp.ones_like(flattened)),
        (jnp.float32(-jnp.inf), jnp.float32(0.0)),
        merge_pair,
        (1,),
    )


def split_exact(value):
    high = lax.reduce_precision(value, exponent_bits=8, mantissa_bits=7)
    rest = value - high
    middle = lax.reduce_precision(rest, exponent_bits=8, mantissa_bits=7)
    return (high, middle, rest - middle)


def pack_kernel(sizes_ref, scales_ref, bins_ref, images_ref, out_ref):
    slots, width = images_ref.shape
    row = lax.broadcasted_iota(jnp.int32, (slots, META), 0)
    column = lax.broadcasted_iota(jnp.int32, (slots, META), 1)
    start = jnp.int32(0)
    gain = jnp.zeros((slots, META), jnp.float32)
    live = jnp.zeros((slots, META), jnp.float32)
    for group in range(sizes_ref.shape[0]):
        size = sizes_ref[group]
        inside = (row >= start) & (row < start + size)
        gain = jnp.where(inside, scales_ref[group], gain)
        live = jnp.where(inside, 1.0, live)
        start = start + size
    bins = jnp.zeros((slots, META), jnp.float32)
    for slot in range(slots):
        bins = jnp.where(row == slot, bins_ref[slot].astype(jnp.float32), bins)
    high = gain.astype(jnp.bfloat16).astype(jnp.float32)
    rest = gain - high
    middle = rest.astype(jnp.bfloat16).astype(jnp.float32)
    fields = (high, middle, rest - middle, live, bins)
    meta = jnp.zeros((slots, META), jnp.float32)
    for index, field in enumerate(fields):
        meta = jnp.where(column == index, field, meta)
    out_ref[:, :width] = images_ref[...]
    out_ref[:, width:] = meta.astype(out_ref.dtype)


def pack_rows(particles, group_counts, group_scale, defocus_bin):
    slots, width = particles.shape
    scalar = pl.BlockSpec(memory_space=pltpu.SMEM)
    whole = pl.BlockSpec(memory_space=pltpu.VMEM)
    return pl.pallas_call(
        pack_kernel,
        out_shape=jax.ShapeDtypeStruct((slots, width + META), particles.dtype),
        in_specs=[scalar, scalar, scalar, whole],
        out_specs=whole,
    )(group_counts, group_scale, defocus_bin, particles)


def xor_gather(value, axis, size):
    pieces = [value] + [
        lax.ppermute(value, axis, [(i, i ^ k) for i in range(size)]) for k in range(1, size)
    ]
    return jnp.concatenate(pieces, axis=0)


def xor_reorder(value, step, axis):
    return jnp.concatenate(
        [lax.slice_in_dim(value, j ^ step, (j ^ step) + 1, axis=axis) for j in range(value.shape[axis])],
        axis=axis,
    )


def xor_butterfly(stats, axis, size):
    step = 1
    while step < size:
        other = lax.ppermute(stats, axis, [(i, i ^ step) for i in range(size)])
        stats = jnp.stack(combine_stats(stats, other))
        step *= 2
    return stats


def accumulate(pieces, scores, gain_rows, ctf_rows, live_mask, peak_score, totals):
    weights = (
        jnp.exp(scores - peak_score[:, None, None])
        / totals[:, None, None]
        * live_mask[:, None, None]
    )
    scaled = (weights * gain_rows[:, None, None]).astype(jnp.bfloat16)
    numerator = None
    start = 0
    for shifted in pieces:
        count = shifted.shape[0] // scaled.shape[1]
        part = lax.dot_general(
            scaled[start : start + count].reshape(shifted.shape[0], -1),
            shifted,
            (((0,), (0,)), ((), ())),
            preferred_element_type=jnp.float32,
        )
        numerator = part if numerator is None else numerator + part
        start += count
    summed = jnp.sum(weights, axis=1) * (gain_rows * gain_rows)[:, None]
    denominator = lax.dot_general(
        summed, ctf_rows * ctf_rows, (((0,), (0,)), ((), ())), precision=HIGHEST
    )
    return (numerator, denominator)


def block_rows(images, gains, bins, bin_table, ref_tile, cosine_table, sine_table):
    half_width = images.shape[1] // 2
    picked = jnp.dot(bin_matrix(bins), bin_table, precision=HIGHEST)
    ctf_rows = picked[:, :half_width]
    shifted = shifted_rows(images, ctf_rows, cosine_table, sine_table)
    scores = tile_scores(shifted, ref_tile, picked[:, half_width:], gains)
    return (shifted, scores, ctf_rows)


def per_device(
    particles, references, ctf_table, spectral_reg, defocus_bin, group_counts, group_scale,
    *, n_blk, n_cls,
):
    cosine_table, sine_table = phase_tables()
    ctf_square = ctf_table * ctf_table
    batch_size, width = particles.shape
    ref_tile = references[0]
    own_norms = tile_norms(ref_tile, ctf_square)
    classes_here = ref_tile.shape[0]
    shifts_count = cosine_table.shape[0]

    small = n_blk <= 4 and n_blk & (n_blk - 1) == 0 and n_cls & (n_cls - 1) == 0
    tables = (jnp.concatenate([ctf_table, own_norms], axis=1), ref_tile, cosine_table, sine_table)
    if small:
        packed = pack_rows(particles, group_counts, group_scale, defocus_bin)
        others = xor_gather(packed, "blk", n_blk)[batch_size:]
        own_rows = lax.optimization_barrier(packed.astype(jnp.float32))
        groups = []
        for rows in (own_rows, others):
            meta = rows[:, width : width + 5].astype(jnp.float32)
            gains = (meta[:, 0] + meta[:, 1]) + meta[:, 2]
            groups.append((rows[:, :width], gains, meta[:, 3], meta[:, 4]))
        live_mask = groups[0][2]
    else:
        gain_rows, live_mask = slot_weights(
            group_counts.reshape(1, -1), group_scale.reshape(1, -1), batch_size
        )
        groups = [(
            lax.all_gather(particles, "blk", axis=0, tiled=True),
            lax.all_gather(gain_rows, "blk", axis=0, tiled=True),
            lax.all_gather(live_mask, "blk", axis=0, tiled=True),
            lax.all_gather(defocus_bin.astype(jnp.float32), "blk", axis=0, tiled=True),
        )]
    results = [block_rows(images, gains, bins, *tables) for images, gains, _, bins in groups]
    pieces = [shifted for shifted, _, _ in results]
    all_scores = jnp.concatenate([scores for _, scores, _ in results], axis=0)
    ctf_rows = jnp.concatenate([rows for _, _, rows in results], axis=0)
    gain_all = jnp.concatenate([group[1] for group in groups])
    live_all = jnp.concatenate([group[2] for group in groups])
    whole_count = all_scores.shape[0]
    flattened = all_scores.reshape(whole_count, -1)
    peak_all, totals_all = local_stats(flattened)

    if small:
        stats = jnp.stack([peak_all, totals_all]).reshape(2, n_blk, batch_size)
        stats = xor_butterfly(stats, "cls", n_cls)
        parts = [stats] + [
            xor_reorder(lax.ppermute(stats, "blk", [(i, i ^ k) for i in range(n_blk)]), k, 1)
            for k in range(1, n_blk)
        ]
        parts = jnp.stack(parts)
        peak_all, totals_all = combine_many(parts[:, 0], parts[:, 1])
        peak_all = peak_all.reshape(-1)
        totals_all = totals_all.reshape(-1)
        peak_score = peak_all[:batch_size]
        totals = totals_all[:batch_size]
    else:
        gathered = lax.all_gather(jnp.stack([peak_all, totals_all]), ("blk", "cls"))
        peak_all, totals_all = combine_many(gathered[:, 0], gathered[:, 1])
        own_offset = lax.axis_index("blk") * batch_size
        peak_score = lax.dynamic_slice_in_dim(peak_all, own_offset, batch_size)
        totals = lax.dynamic_slice_in_dim(totals_all, own_offset, batch_size)

    numerator, denominator = accumulate(
        pieces, all_scores, gain_all, ctf_rows, live_all, peak_all, totals_all
    )
    log_evidence = jnp.where(live_mask > 0.5, peak_score + jnp.log(totals), 0.0)
    denominator = (
        jnp.concatenate([denominator, denominator], axis=1)
        + jnp.concatenate([spectral_reg, spectral_reg])[None, :]
    )
    class_average = (numerator / denominator)[None]
    return (class_average, log_evidence)


def solution(mesh):
    placed = (
        P(("groups", "blk"), None),
        P("blk", ("groups", "cls"), None),
        P("groups", None),
        P("groups"),
        P(("groups", "blk")),
        P(("groups", "blk")),
        P(("groups", "blk")),
    )
    body = lambda *args: per_device(*args, n_blk=mesh.shape["blk"], n_cls=mesh.shape["cls"])
    return jax.shard_map(
        body,
        mesh=mesh,
        in_specs=placed,
        out_specs=(P("blk", ("groups", "cls"), None), P(("groups", "blk"))),
        check_vma=False,
    )
```

```python
import math

import jax
import numpy as np
import jax.numpy as jnp
from jax import lax
from jax.experimental import pallas as pl
from jax.experimental.pallas import tpu as pltpu
from jax.sharding import PartitionSpec as P

KX = 32
KY = 64
IMG = 128
SIDE = 4
BINS = 16
META = 128


HIGHEST = lax.Precision.HIGHEST


def phase_tables():
    column = np.arange(KX * KY, dtype=np.int32)
    freq_x = (column % KX).astype(np.float32)
    freq_y = (column // KX - KY // 2).astype(np.float32)
    offsets = np.arange(SIDE, dtype=np.float32) - np.float32((SIDE - 1) / 2.0)
    shift_x = np.tile(offsets, SIDE)
    shift_y = np.repeat(offsets, SIDE)
    phases = np.float32(2.0 * math.pi / IMG) * (
        shift_x[:, None] * freq_x[None, :] + shift_y[:, None] * freq_y[None, :]
    )
    return (jnp.asarray(np.cos(phases)), jnp.asarray(np.sin(phases)))


def bin_matrix(bin_values):
    return (bin_values[:, None] == jnp.arange(BINS, dtype=jnp.float32)[None, :]).astype(jnp.float32)


def slot_weights(group_sizes, scale_rows, slots):
    group_ends = jnp.cumsum(group_sizes, axis=1)
    group_starts = group_ends - group_sizes
    slot_index = jnp.arange(slots, dtype=jnp.int32)
    membership = (
        (slot_index[None, :, None] >= group_starts[:, None, :])
        & (slot_index[None, :, None] < group_ends[:, None, :])
    ).astype(jnp.float32)
    gain_rows = jnp.sum(membership * scale_rows[:, None, :], axis=2)
    live_mask = jnp.sum(membership, axis=2)
    return (gain_rows.reshape(-1), live_mask.reshape(-1))


def shifted_rows(images, ctf_rows, cosine_table, sine_table):
    half_width = ctf_rows.shape[1]
    real_part = images[:, :half_width].astype(jnp.float32)[:, None, :]
    imag_part = images[:, half_width:].astype(jnp.float32)[:, None, :]
    ctf_wide = ctf_rows[:, None, :]
    new_real = (real_part * cosine_table + imag_part * sine_table) * ctf_wide
    new_imag = (imag_part * cosine_table - real_part * sine_table) * ctf_wide
    joined = jnp.concatenate([new_real, new_imag], axis=2).astype(jnp.bfloat16)
    return joined.reshape(images.shape[0] * cosine_table.shape[0], 2 * half_width)


def tile_norms(ref_rows, ctf_square):
    half_width = ctf_square.shape[1]
    values = ref_rows.astype(jnp.float32)
    power_sum = (
        values[:, :half_width] * values[:, :half_width]
        + values[:, half_width:] * values[:, half_width:]
    )
    return lax.dot_general(ctf_square, power_sum, (((1,), (1,)), ((), ())), precision=HIGHEST)


def tile_scores(shifted, ref_rows, norm_term, gain_rows):
    count_here = gain_rows.shape[0]
    products = lax.dot_general(
        shifted, ref_rows, (((1,), (1,)), ((), ())), preferred_element_type=jnp.float32
    )
    products = products.reshape(count_here, shifted.shape[0] // count_here, ref_rows.shape[0])
    return (
        gain_rows[:, None, None] * products
        - 0.5 * (gain_rows * gain_rows)[:, None, None] * norm_term[:, None, :]
    )


def combine_stats(former, latter):
    new_peak = jnp.maximum(former[0], latter[0])
    return (
        new_peak,
        former[1] * jnp.exp(former[0] - new_peak) + latter[1] * jnp.exp(latter[0] - new_peak),
    )


def combine_many(peaks, totals):
    new_peak = jnp.max(peaks, axis=0)
    return (new_peak, jnp.sum(totals * jnp.exp(peaks - new_peak[None]), axis=0))


def merge_pair(former, latter):
    new_peak = jnp.maximum(former[0], latter[0])
    scale_former = jnp.where(former[0] == new_peak, 1.0, jnp.exp(former[0] - new_peak))
    scale_latter = jnp.where(latter[0] == new_peak, 1.0, jnp.exp(latter[0] - new_peak))
    return (new_peak, former[1] * scale_former + latter[1] * scale_latter)


def local_stats(flattened):
    return lax.reduce(
        (flattened, jnp.ones_like(flattened)),
        (jnp.float32(-jnp.inf), jnp.float32(0.0)),
        merge_pair,
        (1,),
    )


def split_exact(value):
    high = lax.reduce_precision(value, exponent_bits=8, mantissa_bits=7)
    rest = value - high
    middle = lax.reduce_precision(rest, exponent_bits=8, mantissa_bits=7)
    return (high, middle, rest - middle)


def pack_kernel(sizes_ref, scales_ref, bins_ref, images_ref, out_ref):
    slots, width = images_ref.shape
    row = lax.broadcasted_iota(jnp.int32, (slots, META), 0)
    column = lax.broadcasted_iota(jnp.int32, (slots, META), 1)
    start = jnp.int32(0)
    gain = jnp.zeros((slots, META), jnp.float32)
    live = jnp.zeros((slots, META), jnp.float32)
    for group in range(sizes_ref.shape[0]):
        size = sizes_ref[group]
        inside = (row >= start) & (row < start + size)
        gain = jnp.where(inside, scales_ref[group], gain)
        live = jnp.where(inside, 1.0, live)
        start = start + size
    bins = jnp.zeros((slots, META), jnp.float32)
    for slot in range(slots):
        bins = jnp.where(row == slot, bins_ref[slot].astype(jnp.float32), bins)
    high = gain.astype(jnp.bfloat16).astype(jnp.float32)
    rest = gain - high
    middle = rest.astype(jnp.bfloat16).astype(jnp.float32)
    fields = (high, middle, rest - middle, live, bins)
    meta = jnp.zeros((slots, META), jnp.float32)
    for index, field in enumerate(fields):
        meta = jnp.where(column == index, field, meta)
    out_ref[:, :width] = images_ref[...]
    out_ref[:, width:] = meta.astype(out_ref.dtype)


def pack_rows(particles, group_counts, group_scale, defocus_bin):
    slots, width = particles.shape
    scalar = pl.BlockSpec(memory_space=pltpu.SMEM)
    whole = pl.BlockSpec(memory_space=pltpu.VMEM)
    return pl.pallas_call(
        pack_kernel,
        out_shape=jax.ShapeDtypeStruct((slots, width + META), particles.dtype),
        in_specs=[scalar, scalar, scalar, whole],
        out_specs=whole,
    )(group_counts, group_scale, defocus_bin, particles)


def xor_gather(value, axis, size):
    pieces = [value] + [
        lax.ppermute(value, axis, [(i, i ^ k) for i in range(size)]) for k in range(1, size)
    ]
    return jnp.concatenate(pieces, axis=0)


def xor_reorder(value, step, axis):
    return jnp.concatenate(
        [lax.slice_in_dim(value, j ^ step, (j ^ step) + 1, axis=axis) for j in range(value.shape[axis])],
        axis=axis,
    )


def xor_butterfly(stats, axis, size):
    step = 1
    while step < size:
        other = lax.ppermute(stats, axis, [(i, i ^ step) for i in range(size)])
        stats = jnp.stack(combine_stats(stats, other))
        step *= 2
    return stats


def accumulate(pieces, scores, gain_rows, ctf_rows, live_mask, peak_score, totals):
    weights = (
        jnp.exp(scores - peak_score[:, None, None])
        / totals[:, None, None]
        * live_mask[:, None, None]
    )
    scaled = (weights * gain_rows[:, None, None]).astype(jnp.bfloat16)
    numerator = None
    start = 0
    for shifted in pieces:
        count = shifted.shape[0] // scaled.shape[1]
        part = lax.dot_general(
            scaled[start : start + count].reshape(shifted.shape[0], -1),
            shifted,
            (((0,), (0,)), ((), ())),
            preferred_element_type=jnp.float32,
        )
        numerator = part if numerator is None else numerator + part
        start += count
    summed = jnp.sum(weights, axis=1) * (gain_rows * gain_rows)[:, None]
    denominator = lax.dot_general(
        summed, ctf_rows * ctf_rows, (((0,), (0,)), ((), ())), precision=lax.Precision.HIGH
    )
    return (numerator, denominator)


def block_rows(images, gains, bins, bin_table, ref_tile, cosine_table, sine_table):
    half_width = images.shape[1] // 2
    picked = jnp.dot(bin_matrix(bins), bin_table, precision=HIGHEST)
    ctf_rows = picked[:, :half_width]
    shifted = shifted_rows(images, ctf_rows, cosine_table, sine_table)
    scores = tile_scores(shifted, ref_tile, picked[:, half_width:], gains)
    return (shifted, scores, ctf_rows)


def per_device(
    particles, references, ctf_table, spectral_reg, defocus_bin, group_counts, group_scale,
    *, n_blk, n_cls,
):
    cosine_table, sine_table = phase_tables()
    ctf_square = ctf_table * ctf_table
    batch_size, width = particles.shape
    ref_tile = references[0]
    own_norms = tile_norms(ref_tile, ctf_square)
    classes_here = ref_tile.shape[0]
    shifts_count = cosine_table.shape[0]

    small = n_blk <= 4 and n_blk & (n_blk - 1) == 0 and n_cls & (n_cls - 1) == 0
    tables = (jnp.concatenate([ctf_table, own_norms], axis=1), ref_tile, cosine_table, sine_table)
    if small:
        packed = pack_rows(particles, group_counts, group_scale, defocus_bin)
        others = xor_gather(packed, "blk", n_blk)[batch_size:]
        own_rows = lax.optimization_barrier(packed.astype(jnp.float32))
        groups = []
        for rows in (own_rows, others):
            meta = rows[:, width : width + 5].astype(jnp.float32)
            gains = (meta[:, 0] + meta[:, 1]) + meta[:, 2]
            groups.append((rows[:, :width], gains, meta[:, 3], meta[:, 4]))
        live_mask = groups[0][2]
    else:
        gain_rows, live_mask = slot_weights(
            group_counts.reshape(1, -1), group_scale.reshape(1, -1), batch_size
        )
        groups = [(
            lax.all_gather(particles, "blk", axis=0, tiled=True),
            lax.all_gather(gain_rows, "blk", axis=0, tiled=True),
            lax.all_gather(live_mask, "blk", axis=0, tiled=True),
            lax.all_gather(defocus_bin.astype(jnp.float32), "blk", axis=0, tiled=True),
        )]
    results = [block_rows(images, gains, bins, *tables) for images, gains, _, bins in groups]
    pieces = [shifted for shifted, _, _ in results]
    all_scores = jnp.concatenate([scores for _, scores, _ in results], axis=0)
    ctf_rows = jnp.concatenate([rows for _, _, rows in results], axis=0)
    gain_all = jnp.concatenate([group[1] for group in groups])
    live_all = jnp.concatenate([group[2] for group in groups])
    whole_count = all_scores.shape[0]
    flattened = all_scores.reshape(whole_count, -1)
    peak_all, totals_all = local_stats(flattened)

    if small:
        stats = jnp.stack([peak_all, totals_all]).reshape(2, n_blk, batch_size)
        stats = xor_butterfly(stats, "cls", n_cls)
        parts = [stats] + [
            xor_reorder(lax.ppermute(stats, "blk", [(i, i ^ k) for i in range(n_blk)]), k, 1)
            for k in range(1, n_blk)
        ]
        parts = jnp.stack(parts)
        peak_all, totals_all = combine_many(parts[:, 0], parts[:, 1])
        peak_all = peak_all.reshape(-1)
        totals_all = totals_all.reshape(-1)
        peak_score = peak_all[:batch_size]
        totals = totals_all[:batch_size]
    else:
        gathered = lax.all_gather(jnp.stack([peak_all, totals_all]), ("blk", "cls"))
        peak_all, totals_all = combine_many(gathered[:, 0], gathered[:, 1])
        own_offset = lax.axis_index("blk") * batch_size
        peak_score = lax.dynamic_slice_in_dim(peak_all, own_offset, batch_size)
        totals = lax.dynamic_slice_in_dim(totals_all, own_offset, batch_size)

    numerator, denominator = accumulate(
        pieces, all_scores, gain_all, ctf_rows, live_all, peak_all, totals_all
    )
    log_evidence = jnp.where(live_mask > 0.5, peak_score + jnp.log(totals), 0.0)
    denominator = (
        jnp.concatenate([denominator, denominator], axis=1)
        + jnp.concatenate([spectral_reg, spectral_reg])[None, :]
    )
    class_average = (numerator / denominator)[None]
    return (class_average, log_evidence)


def solution(mesh):
    placed = (
        P(("groups", "blk"), None),
        P("blk", ("groups", "cls"), None),
        P("groups", None),
        P("groups"),
        P(("groups", "blk")),
        P(("groups", "blk")),
        P(("groups", "blk")),
    )
    body = lambda *args: per_device(*args, n_blk=mesh.shape["blk"], n_cls=mesh.shape["cls"])
    return jax.shard_map(
        body,
        mesh=mesh,
        in_specs=placed,
        out_specs=(P("blk", ("groups", "cls"), None), P(("groups", "blk"))),
        check_vma=False,
    )
```

```python
import math

import jax
import numpy as np
import jax.numpy as jnp
from jax import lax
from jax.experimental import pallas as pl
from jax.experimental.pallas import tpu as pltpu
from jax.sharding import PartitionSpec as P

KX = 32
KY = 64
IMG = 128
SIDE = 4
BINS = 16
META = 128


HIGHEST = lax.Precision.HIGHEST


def phase_tables():
    column = np.arange(KX * KY, dtype=np.int32)
    freq_x = (column % KX).astype(np.float32)
    freq_y = (column // KX - KY // 2).astype(np.float32)
    offsets = np.arange(SIDE, dtype=np.float32) - np.float32((SIDE - 1) / 2.0)
    shift_x = np.tile(offsets, SIDE)
    shift_y = np.repeat(offsets, SIDE)
    phases = np.float32(2.0 * math.pi / IMG) * (
        shift_x[:, None] * freq_x[None, :] + shift_y[:, None] * freq_y[None, :]
    )
    return (jnp.asarray(np.cos(phases)), jnp.asarray(np.sin(phases)))


def bin_matrix(bin_values):
    return (bin_values[:, None] == jnp.arange(BINS, dtype=jnp.float32)[None, :]).astype(jnp.float32)


def slot_weights(group_sizes, scale_rows, slots):
    group_ends = jnp.cumsum(group_sizes, axis=1)
    group_starts = group_ends - group_sizes
    slot_index = jnp.arange(slots, dtype=jnp.int32)
    membership = (
        (slot_index[None, :, None] >= group_starts[:, None, :])
        & (slot_index[None, :, None] < group_ends[:, None, :])
    ).astype(jnp.float32)
    gain_rows = jnp.sum(membership * scale_rows[:, None, :], axis=2)
    live_mask = jnp.sum(membership, axis=2)
    return (gain_rows.reshape(-1), live_mask.reshape(-1))


def shifted_rows(images, ctf_rows, cosine_table, sine_table):
    half_width = ctf_rows.shape[1]
    real_part = images[:, :half_width].astype(jnp.float32)[:, None, :]
    imag_part = images[:, half_width:].astype(jnp.float32)[:, None, :]
    ctf_wide = ctf_rows[:, None, :]
    new_real = (real_part * cosine_table + imag_part * sine_table) * ctf_wide
    new_imag = (imag_part * cosine_table - real_part * sine_table) * ctf_wide
    joined = jnp.concatenate([new_real, new_imag], axis=2).astype(jnp.bfloat16)
    return joined.reshape(images.shape[0] * cosine_table.shape[0], 2 * half_width)


def tile_norms(ref_rows, ctf_square):
    half_width = ctf_square.shape[1]
    values = ref_rows.astype(jnp.float32)
    power_sum = (
        values[:, :half_width] * values[:, :half_width]
        + values[:, half_width:] * values[:, half_width:]
    )
    return lax.dot_general(ctf_square, power_sum, (((1,), (1,)), ((), ())), precision=HIGHEST)


def tile_scores(shifted, ref_rows, norm_term, gain_rows):
    count_here = gain_rows.shape[0]
    products = lax.dot_general(
        shifted, ref_rows, (((1,), (1,)), ((), ())), preferred_element_type=jnp.float32
    )
    products = products.reshape(count_here, shifted.shape[0] // count_here, ref_rows.shape[0])
    return (
        gain_rows[:, None, None] * products
        - 0.5 * (gain_rows * gain_rows)[:, None, None] * norm_term[:, None, :]
    )


def combine_stats(former, latter):
    new_peak = jnp.maximum(former[0], latter[0])
    return (
        new_peak,
        former[1] * jnp.exp(former[0] - new_peak) + latter[1] * jnp.exp(latter[0] - new_peak),
    )


def combine_many(peaks, totals):
    new_peak = jnp.max(peaks, axis=0)
    return (new_peak, jnp.sum(totals * jnp.exp(peaks - new_peak[None]), axis=0))


def merge_pair(former, latter):
    new_peak = jnp.maximum(former[0], latter[0])
    scale_former = jnp.where(former[0] == new_peak, 1.0, jnp.exp(former[0] - new_peak))
    scale_latter = jnp.where(latter[0] == new_peak, 1.0, jnp.exp(latter[0] - new_peak))
    return (new_peak, former[1] * scale_former + latter[1] * scale_latter)


def local_stats(flattened):
    return lax.reduce(
        (flattened, jnp.ones_like(flattened)),
        (jnp.float32(-jnp.inf), jnp.float32(0.0)),
        merge_pair,
        (1,),
    )


def split_exact(value):
    high = lax.reduce_precision(value, exponent_bits=8, mantissa_bits=7)
    rest = value - high
    middle = lax.reduce_precision(rest, exponent_bits=8, mantissa_bits=7)
    return (high, middle, rest - middle)


def pack_kernel(sizes_ref, scales_ref, bins_ref, images_ref, out_ref):
    slots, width = images_ref.shape
    row = lax.broadcasted_iota(jnp.int32, (slots, META), 0)
    column = lax.broadcasted_iota(jnp.int32, (slots, META), 1)
    start = jnp.int32(0)
    gain = jnp.zeros((slots, META), jnp.float32)
    live = jnp.zeros((slots, META), jnp.float32)
    for group in range(sizes_ref.shape[0]):
        size = sizes_ref[group]
        inside = (row >= start) & (row < start + size)
        gain = jnp.where(inside, scales_ref[group], gain)
        live = jnp.where(inside, 1.0, live)
        start = start + size
    bins = jnp.zeros((slots, META), jnp.float32)
    for slot in range(slots):
        bins = jnp.where(row == slot, bins_ref[slot].astype(jnp.float32), bins)
    high = gain.astype(jnp.bfloat16).astype(jnp.float32)
    rest = gain - high
    middle = rest.astype(jnp.bfloat16).astype(jnp.float32)
    fields = (high, middle, rest - middle, live, bins)
    meta = jnp.zeros((slots, META), jnp.float32)
    for index, field in enumerate(fields):
        meta = jnp.where(column == index, field, meta)
    out_ref[:, :width] = images_ref[...]
    out_ref[:, width:] = meta.astype(out_ref.dtype)


def pack_rows(particles, group_counts, group_scale, defocus_bin):
    slots, width = particles.shape
    scalar = pl.BlockSpec(memory_space=pltpu.SMEM)
    whole = pl.BlockSpec(memory_space=pltpu.VMEM)
    return pl.pallas_call(
        pack_kernel,
        out_shape=jax.ShapeDtypeStruct((slots, width + META), particles.dtype),
        in_specs=[scalar, scalar, scalar, whole],
        out_specs=whole,
    )(group_counts, group_scale, defocus_bin, particles)


def xor_gather(value, axis, size):
    pieces = [value] + [
        lax.ppermute(value, axis, [(i, i ^ k) for i in range(size)]) for k in range(1, size)
    ]
    return jnp.concatenate(pieces, axis=0)


def xor_reorder(value, step, axis):
    return jnp.concatenate(
        [lax.slice_in_dim(value, j ^ step, (j ^ step) + 1, axis=axis) for j in range(value.shape[axis])],
        axis=axis,
    )


def xor_butterfly(stats, axis, size):
    step = size // 2
    while step >= 1:
        other = lax.ppermute(stats, axis, [(i, i ^ step) for i in range(size)])
        stats = jnp.stack(combine_stats(stats, other))
        step //= 2
    return stats


def accumulate(pieces, scores, gain_rows, ctf_rows, live_mask, peak_score, totals):
    weights = (
        jnp.exp(scores - peak_score[:, None, None])
        / totals[:, None, None]
        * live_mask[:, None, None]
    )
    scaled = (weights * gain_rows[:, None, None]).astype(jnp.bfloat16)
    numerator = None
    start = 0
    for shifted in pieces:
        count = shifted.shape[0] // scaled.shape[1]
        part = lax.dot_general(
            scaled[start : start + count].reshape(shifted.shape[0], -1),
            shifted,
            (((0,), (0,)), ((), ())),
            preferred_element_type=jnp.float32,
        )
        numerator = part if numerator is None else numerator + part
        start += count
    summed = jnp.sum(weights, axis=1) * (gain_rows * gain_rows)[:, None]
    denominator = lax.dot_general(
        summed, ctf_rows * ctf_rows, (((0,), (0,)), ((), ())), precision=HIGHEST
    )
    return (numerator, denominator)


def block_rows(images, gains, bins, bin_table, ref_tile, cosine_table, sine_table):
    half_width = images.shape[1] // 2
    picked = jnp.dot(bin_matrix(bins), bin_table, precision=HIGHEST)
    ctf_rows = picked[:, :half_width]
    shifted = shifted_rows(images, ctf_rows, cosine_table, sine_table)
    scores = tile_scores(shifted, ref_tile, picked[:, half_width:], gains)
    return (shifted, scores, ctf_rows)


def per_device(
    particles, references, ctf_table, spectral_reg, defocus_bin, group_counts, group_scale,
    *, n_blk, n_cls,
):
    cosine_table, sine_table = phase_tables()
    ctf_square = ctf_table * ctf_table
    batch_size, width = particles.shape
    ref_tile = references[0]
    own_norms = tile_norms(ref_tile, ctf_square)
    classes_here = ref_tile.shape[0]
    shifts_count = cosine_table.shape[0]

    small = n_blk <= 4 and n_blk & (n_blk - 1) == 0 and n_cls & (n_cls - 1) == 0
    tables = (jnp.concatenate([ctf_table, own_norms], axis=1), ref_tile, cosine_table, sine_table)
    if small:
        packed = pack_rows(particles, group_counts, group_scale, defocus_bin)
        others = xor_gather(packed, "blk", n_blk)[batch_size:]
        own_rows = lax.optimization_barrier(packed.astype(jnp.float32))
        groups = []
        for rows in (own_rows, others):
            meta = rows[:, width : width + 5].astype(jnp.float32)
            gains = (meta[:, 0] + meta[:, 1]) + meta[:, 2]
            groups.append((rows[:, :width], gains, meta[:, 3], meta[:, 4]))
        live_mask = groups[0][2]
    else:
        gain_rows, live_mask = slot_weights(
            group_counts.reshape(1, -1), group_scale.reshape(1, -1), batch_size
        )
        groups = [(
            lax.all_gather(particles, "blk", axis=0, tiled=True),
            lax.all_gather(gain_rows, "blk", axis=0, tiled=True),
            lax.all_gather(live_mask, "blk", axis=0, tiled=True),
            lax.all_gather(defocus_bin.astype(jnp.float32), "blk", axis=0, tiled=True),
        )]
    results = [block_rows(images, gains, bins, *tables) for images, gains, _, bins in groups]
    pieces = [shifted for shifted, _, _ in results]
    all_scores = jnp.concatenate([scores for _, scores, _ in results], axis=0)
    ctf_rows = jnp.concatenate([rows for _, _, rows in results], axis=0)
    gain_all = jnp.concatenate([group[1] for group in groups])
    live_all = jnp.concatenate([group[2] for group in groups])
    whole_count = all_scores.shape[0]
    flattened = all_scores.reshape(whole_count, -1)
    peak_all, totals_all = local_stats(flattened)

    if small:
        stats = jnp.stack([peak_all, totals_all]).reshape(2, n_blk, batch_size)
        stats = xor_butterfly(stats, "cls", n_cls)
        parts = [stats] + [
            xor_reorder(lax.ppermute(stats, "blk", [(i, i ^ k) for i in range(n_blk)]), k, 1)
            for k in range(1, n_blk)
        ]
        parts = jnp.stack(parts)
        peak_all, totals_all = combine_many(parts[:, 0], parts[:, 1])
        peak_all = peak_all.reshape(-1)
        totals_all = totals_all.reshape(-1)
        peak_score = peak_all[:batch_size]
        totals = totals_all[:batch_size]
    else:
        gathered = lax.all_gather(jnp.stack([peak_all, totals_all]), ("blk", "cls"))
        peak_all, totals_all = combine_many(gathered[:, 0], gathered[:, 1])
        own_offset = lax.axis_index("blk") * batch_size
        peak_score = lax.dynamic_slice_in_dim(peak_all, own_offset, batch_size)
        totals = lax.dynamic_slice_in_dim(totals_all, own_offset, batch_size)

    numerator, denominator = accumulate(
        pieces, all_scores, gain_all, ctf_rows, live_all, peak_all, totals_all
    )
    log_evidence = jnp.where(live_mask > 0.5, peak_score + jnp.log(totals), 0.0)
    denominator = (
        jnp.concatenate([denominator, denominator], axis=1)
        + jnp.concatenate([spectral_reg, spectral_reg])[None, :]
    )
    class_average = (numerator / denominator)[None]
    return (class_average, log_evidence)


def solution(mesh):
    placed = (
        P(("groups", "blk"), None),
        P("blk", ("groups", "cls"), None),
        P("groups", None),
        P("groups"),
        P(("groups", "blk")),
        P(("groups", "blk")),
        P(("groups", "blk")),
    )
    body = lambda *args: per_device(*args, n_blk=mesh.shape["blk"], n_cls=mesh.shape["cls"])
    return jax.shard_map(
        body,
        mesh=mesh,
        in_specs=placed,
        out_specs=(P("blk", ("groups", "cls"), None), P(("groups", "blk"))),
        check_vma=False,
    )
```

```python
import math

import jax
import numpy as np
import jax.numpy as jnp
from jax import lax
from jax.experimental import pallas as pl
from jax.experimental.pallas import tpu as pltpu
from jax.experimental.layout import Layout, with_layout_constraint
from jax.sharding import PartitionSpec as P

KX = 32
KY = 64
IMG = 128
SIDE = 4
BINS = 16
META = 128


HIGHEST = lax.Precision.HIGHEST


def phase_tables():
    column = np.arange(KX * KY, dtype=np.int32)
    freq_x = (column % KX).astype(np.float32)
    freq_y = (column // KX - KY // 2).astype(np.float32)
    offsets = np.arange(SIDE, dtype=np.float32) - np.float32((SIDE - 1) / 2.0)
    shift_x = np.tile(offsets, SIDE)
    shift_y = np.repeat(offsets, SIDE)
    phases = np.float32(2.0 * math.pi / IMG) * (
        shift_x[:, None] * freq_x[None, :] + shift_y[:, None] * freq_y[None, :]
    )
    return (jnp.asarray(np.cos(phases)), jnp.asarray(np.sin(phases)))


def bin_matrix(bin_values):
    return (bin_values[:, None] == jnp.arange(BINS, dtype=jnp.float32)[None, :]).astype(jnp.float32)


def slot_weights(group_sizes, scale_rows, slots):
    group_ends = jnp.cumsum(group_sizes, axis=1)
    group_starts = group_ends - group_sizes
    slot_index = jnp.arange(slots, dtype=jnp.int32)
    membership = (
        (slot_index[None, :, None] >= group_starts[:, None, :])
        & (slot_index[None, :, None] < group_ends[:, None, :])
    ).astype(jnp.float32)
    gain_rows = jnp.sum(membership * scale_rows[:, None, :], axis=2)
    live_mask = jnp.sum(membership, axis=2)
    return (gain_rows.reshape(-1), live_mask.reshape(-1))


def shifted_rows(images, ctf_rows, cosine_table, sine_table):
    half_width = ctf_rows.shape[1]
    real_part = images[:, :half_width].astype(jnp.float32)[:, None, :]
    imag_part = images[:, half_width:].astype(jnp.float32)[:, None, :]
    ctf_wide = ctf_rows[:, None, :]
    new_real = (real_part * cosine_table + imag_part * sine_table) * ctf_wide
    new_imag = (imag_part * cosine_table - real_part * sine_table) * ctf_wide
    joined = jnp.concatenate([new_real, new_imag], axis=2).astype(jnp.bfloat16)
    return joined.reshape(images.shape[0] * cosine_table.shape[0], 2 * half_width)


def tile_norms(ref_rows, ctf_square):
    half_width = ctf_square.shape[1]
    values = ref_rows.astype(jnp.float32)
    power_sum = (
        values[:, :half_width] * values[:, :half_width]
        + values[:, half_width:] * values[:, half_width:]
    )
    return lax.dot_general(ctf_square, power_sum, (((1,), (1,)), ((), ())), precision=HIGHEST)


def tile_scores(shifted, ref_rows, norm_term, gain_rows):
    count_here = gain_rows.shape[0]
    products = lax.dot_general(
        shifted, ref_rows, (((1,), (1,)), ((), ())), preferred_element_type=jnp.float32
    )
    products = products.reshape(count_here, shifted.shape[0] // count_here, ref_rows.shape[0])
    return (
        gain_rows[:, None, None] * products
        - 0.5 * (gain_rows * gain_rows)[:, None, None] * norm_term[:, None, :]
    )


def combine_stats(former, latter):
    new_peak = jnp.maximum(former[0], latter[0])
    return (
        new_peak,
        former[1] * jnp.exp(former[0] - new_peak) + latter[1] * jnp.exp(latter[0] - new_peak),
    )


def combine_many(peaks, totals):
    new_peak = jnp.max(peaks, axis=0)
    return (new_peak, jnp.sum(totals * jnp.exp(peaks - new_peak[None]), axis=0))


def merge_pair(former, latter):
    new_peak = jnp.maximum(former[0], latter[0])
    scale_former = jnp.where(former[0] == new_peak, 1.0, jnp.exp(former[0] - new_peak))
    scale_latter = jnp.where(latter[0] == new_peak, 1.0, jnp.exp(latter[0] - new_peak))
    return (new_peak, former[1] * scale_former + latter[1] * scale_latter)


def local_stats(flattened):
    return lax.reduce(
        (flattened, jnp.ones_like(flattened)),
        (jnp.float32(-jnp.inf), jnp.float32(0.0)),
        merge_pair,
        (1,),
    )


def split_exact(value):
    high = lax.reduce_precision(value, exponent_bits=8, mantissa_bits=7)
    rest = value - high
    middle = lax.reduce_precision(rest, exponent_bits=8, mantissa_bits=7)
    return (high, middle, rest - middle)


def pack_kernel(sizes_ref, scales_ref, bins_ref, images_ref, out_ref):
    slots, width = images_ref.shape
    row = lax.broadcasted_iota(jnp.int32, (slots, META), 0)
    column = lax.broadcasted_iota(jnp.int32, (slots, META), 1)
    start = jnp.int32(0)
    gain = jnp.zeros((slots, META), jnp.float32)
    live = jnp.zeros((slots, META), jnp.float32)
    for group in range(sizes_ref.shape[0]):
        size = sizes_ref[group]
        inside = (row >= start) & (row < start + size)
        gain = jnp.where(inside, scales_ref[group], gain)
        live = jnp.where(inside, 1.0, live)
        start = start + size
    bins = jnp.zeros((slots, META), jnp.float32)
    for slot in range(slots):
        bins = jnp.where(row == slot, bins_ref[slot].astype(jnp.float32), bins)
    high = gain.astype(jnp.bfloat16).astype(jnp.float32)
    rest = gain - high
    middle = rest.astype(jnp.bfloat16).astype(jnp.float32)
    fields = (high, middle, rest - middle, live, bins)
    meta = jnp.zeros((slots, META), jnp.float32)
    for index, field in enumerate(fields):
        meta = jnp.where(column == index, field, meta)
    out_ref[:, :width] = images_ref[...]
    out_ref[:, width:] = meta.astype(out_ref.dtype)


def pack_rows(particles, group_counts, group_scale, defocus_bin):
    slots, width = particles.shape
    scalar = pl.BlockSpec(memory_space=pltpu.SMEM)
    whole = pl.BlockSpec(memory_space=pltpu.VMEM)
    return pl.pallas_call(
        pack_kernel,
        out_shape=jax.ShapeDtypeStruct((slots, width + META), particles.dtype),
        in_specs=[scalar, scalar, scalar, whole],
        out_specs=whole,
    )(group_counts, group_scale, defocus_bin, particles)


def xor_gather(value, axis, size):
    pieces = [value] + [
        lax.ppermute(value, axis, [(i, i ^ k) for i in range(size)]) for k in range(1, size)
    ]
    return jnp.concatenate(pieces, axis=0)


def xor_reorder(value, step, axis):
    return jnp.concatenate(
        [lax.slice_in_dim(value, j ^ step, (j ^ step) + 1, axis=axis) for j in range(value.shape[axis])],
        axis=axis,
    )


def xor_butterfly(stats, axis, size):
    step = 1
    while step < size:
        other = lax.ppermute(stats, axis, [(i, i ^ step) for i in range(size)])
        stats = jnp.stack(combine_stats(stats, other))
        step *= 2
    return stats


def accumulate(pieces, scores, gain_rows, ctf_rows, live_mask, peak_score, totals):
    weights = (
        jnp.exp(scores - peak_score[:, None, None])
        / totals[:, None, None]
        * live_mask[:, None, None]
    )
    scaled = (weights * gain_rows[:, None, None]).astype(jnp.bfloat16)
    numerator = None
    start = 0
    for shifted in pieces:
        count = shifted.shape[0] // scaled.shape[1]
        part = lax.dot_general(
            scaled[start : start + count].reshape(shifted.shape[0], -1),
            shifted,
            (((0,), (0,)), ((), ())),
            preferred_element_type=jnp.float32,
        )
        numerator = part if numerator is None else numerator + part
        start += count
    summed = jnp.sum(weights, axis=1) * (gain_rows * gain_rows)[:, None]
    denominator = lax.dot_general(
        summed, ctf_rows * ctf_rows, (((0,), (0,)), ((), ())), precision=HIGHEST
    )
    return (numerator, denominator)


def block_rows(images, gains, bins, bin_table, ref_tile, cosine_table, sine_table):
    half_width = images.shape[1] // 2
    picked = jnp.dot(bin_matrix(bins), bin_table, precision=HIGHEST)
    ctf_rows = picked[:, :half_width]
    shifted = shifted_rows(images, ctf_rows, cosine_table, sine_table)
    scores = tile_scores(shifted, ref_tile, picked[:, half_width:], gains)
    return (shifted, scores, ctf_rows)


def per_device(
    particles, references, ctf_table, spectral_reg, defocus_bin, group_counts, group_scale,
    *, n_blk, n_cls,
):
    cosine_table, sine_table = phase_tables()
    ctf_square = ctf_table * ctf_table
    batch_size, width = particles.shape
    ref_tile = references[0]
    own_norms = tile_norms(ref_tile, ctf_square)
    classes_here = ref_tile.shape[0]
    shifts_count = cosine_table.shape[0]

    small = n_blk <= 4 and n_blk & (n_blk - 1) == 0 and n_cls & (n_cls - 1) == 0
    tables = (jnp.concatenate([ctf_table, own_norms], axis=1), ref_tile, cosine_table, sine_table)
    if small:
        packed = pack_rows(particles, group_counts, group_scale, defocus_bin)
        others = xor_gather(packed, "blk", n_blk)[batch_size:]
        own_rows = lax.optimization_barrier(packed.astype(jnp.float32))
        groups = []
        for rows in (own_rows, others):
            meta = rows[:, width : width + 5].astype(jnp.float32)
            gains = (meta[:, 0] + meta[:, 1]) + meta[:, 2]
            groups.append((rows[:, :width], gains, meta[:, 3], meta[:, 4]))
        live_mask = groups[0][2]
    else:
        gain_rows, live_mask = slot_weights(
            group_counts.reshape(1, -1), group_scale.reshape(1, -1), batch_size
        )
        groups = [(
            lax.all_gather(particles, "blk", axis=0, tiled=True),
            lax.all_gather(gain_rows, "blk", axis=0, tiled=True),
            lax.all_gather(live_mask, "blk", axis=0, tiled=True),
            lax.all_gather(defocus_bin.astype(jnp.float32), "blk", axis=0, tiled=True),
        )]
    results = [block_rows(images, gains, bins, *tables) for images, gains, _, bins in groups]
    pieces = [shifted for shifted, _, _ in results]
    all_scores = jnp.concatenate([scores for _, scores, _ in results], axis=0)
    ctf_rows = jnp.concatenate([rows for _, _, rows in results], axis=0)
    gain_all = jnp.concatenate([group[1] for group in groups])
    live_all = jnp.concatenate([group[2] for group in groups])
    whole_count = all_scores.shape[0]
    flattened = all_scores.reshape(whole_count, -1)
    peak_all, totals_all = local_stats(flattened)

    if small:
        stats = jnp.stack([peak_all, totals_all]).reshape(2, n_blk, batch_size)
        stats = xor_butterfly(stats, "cls", n_cls)
        parts = [stats] + [
            xor_reorder(lax.ppermute(stats, "blk", [(i, i ^ k) for i in range(n_blk)]), k, 1)
            for k in range(1, n_blk)
        ]
        parts = jnp.stack(parts)
        peak_all, totals_all = combine_many(parts[:, 0], parts[:, 1])
        peak_all = peak_all.reshape(-1)
        totals_all = totals_all.reshape(-1)
        peak_score = peak_all[:batch_size]
        totals = totals_all[:batch_size]
    else:
        gathered = lax.all_gather(jnp.stack([peak_all, totals_all]), ("blk", "cls"))
        peak_all, totals_all = combine_many(gathered[:, 0], gathered[:, 1])
        own_offset = lax.axis_index("blk") * batch_size
        peak_score = lax.dynamic_slice_in_dim(peak_all, own_offset, batch_size)
        totals = lax.dynamic_slice_in_dim(totals_all, own_offset, batch_size)

    numerator, denominator = accumulate(
        pieces, all_scores, gain_all, ctf_rows, live_all, peak_all, totals_all
    )
    log_evidence = jnp.where(live_mask > 0.5, peak_score + jnp.log(totals), 0.0)
    denominator = (
        jnp.concatenate([denominator, denominator], axis=1)
        + jnp.concatenate([spectral_reg, spectral_reg])[None, :]
    )
    class_average = with_layout_constraint(
        (numerator / denominator)[None], Layout(major_to_minor=(1, 0, 2))
    )
    return (class_average, log_evidence)


def solution(mesh):
    placed = (
        P(("groups", "blk"), None),
        P("blk", ("groups", "cls"), None),
        P("groups", None),
        P("groups"),
        P(("groups", "blk")),
        P(("groups", "blk")),
        P(("groups", "blk")),
    )
    body = lambda *args: per_device(*args, n_blk=mesh.shape["blk"], n_cls=mesh.shape["cls"])
    return jax.shard_map(
        body,
        mesh=mesh,
        in_specs=placed,
        out_specs=(P("blk", ("groups", "cls"), None), P(("groups", "blk"))),
        check_vma=False,
    )
```
